32 devices in a mesh: real: 4 (over x, core), space: 8 (over z, y).
Axes of the slice: x: 2, y: 2, z: 4, core: 2. Of those that a mesh axis runs over, the one named last changes fastest.
Arguments:
- perm_class: int32 [8, 16, 16, 128], P('space'), may hold values from 0 to 7
- class_values: float32 [8], replicated, may hold values from 0.3 to 10
- well_cells: int32 [64], P('real'), parts along dimension 0, may hold values from 0 to 262143
- well_rates: float32 [64], P('real'), parts along dimension 0, may hold values from 0.5 to 3
- guess: float32 [32, 16, 16, 128], P(('real', 'space')), parts along dimension 0, may hold values from -4 to 4
Outputs:
- pressure: float32 [32, 16, 16, 128], P(('real', 'space')), parts along dimension 0
- residual: float32 [32, 16, 16, 128], P(('real', 'space')), parts along dimension 0
The draws below stay inside these ranges and needn't reach their ends.
There are 4 independent parts, one for each index of `real`. The reference program is written for one: setup_inputs(seed, part) draws one part's arguments, and reference() takes and returns one part's arrays. A program takes and returns all parts, laid end to end along the dimension named above; an argument that names none is the same for every part. Nothing has to cross between parts.
All inputs are finite; a program needn't handle non-finite values.
Results may differ from the reference program's by a relative error of at most 0.00015.
Values sent between devices are 32-bit elements; how exact they have to be, the bound alone decides.
No kernel may reach another device: no remote copies, remote signals or barrier semaphores. Data moves between devices by JAX's collectives and lax.ppermute only.
A program may use at most 128 MiB of HBM per device.

```python
import math
import jax
import jax.numpy as jnp

CX = 16
CY = 16
CZ = 128
NCLASS = 8
NWELLS = 16
LEVELS = 3
SWEEPS = 2
CSWEEPS = 6
BLOCKS = 8
SIDE = 2
ROTATE = 7
NX = 32
NY = 32
NZ = 256


def place_ends(entries, stream_key, low, high):
    extent = entries.shape
    spot = [jax.random.randint(jax.random.fold_in(stream_key, axis), (), 0, extent[axis]) for axis in range(len(extent))]
    entries = entries.at[tuple(spot)].set(low)
    longest = extent.index(max(extent))
    spot[longest] = (spot[longest] + 1) % extent[longest]
    return entries.at[tuple(spot)].set(high)


def steps_of(rng, shape, shards, least, largest):
    gain, own = 1.0, jax.random.fold_in(rng, 6)
    for position, blocks in shards:
        draws = jnp.exp(jax.random.uniform(jax.random.fold_in(own, position), (blocks,), jnp.float32, least / len(shards), largest / len(shards)))
        gain = gain * jnp.repeat(draws, shape[position] // blocks).reshape([-1 if axis == position else 1 for axis in range(len(shape))])
    return gain


def bell_draw(rng, extent, width, most, split=(), held_as=jnp.bfloat16):
    factor_of = steps_of(rng, extent, split, -0.22, 0.18) if split else 1.0
    drawn = jax.random.normal(rng, extent, jnp.float32) * width * factor_of
    return jnp.minimum(jnp.maximum(drawn, -most), most).astype(held_as)


def setup_inputs(seed: int = 0, part: int = 0) -> dict:
    keys = jax.random.split(jax.random.key(seed), 6)
    part_keys = jax.random.split(jax.random.fold_in(keys[5], part), 6)
    return {
        "perm_class": place_ends(jax.random.randint(keys[0], (BLOCKS, CX, CY, CZ), 0, NCLASS), jax.random.fold_in(keys[0], 1), 0, NCLASS - 1).astype(jnp.int32),
        "class_values": jnp.clip(jnp.exp(jax.random.uniform(keys[1], (NCLASS,), jnp.float32, math.log(0.3), math.log(10.0))), 0.3, 10.0),
        "well_cells": place_ends(jax.random.randint(part_keys[2], (NWELLS,), 0, NX * NY * NZ), jax.random.fold_in(part_keys[2], 1), 0, (NX * NY * NZ) - 1).astype(jnp.int32),
        "well_rates": jnp.clip(jax.random.uniform(part_keys[3], (NWELLS,), jnp.float32, 0.5, 3.0), 0.5, 3.0),
        "guess": bell_draw(part_keys[4], (BLOCKS, CX, CY, CZ), 0.3, 4.0, ((0, 8),), jnp.float32),
    }


OMEGA = 0.8


def to_blocks(grid_vals):
    arranged = grid_vals.reshape(SIDE, CX, SIDE, CY, SIDE, CZ).transpose(0, 2, 4, 1, 3, 5)
    return jnp.roll(arranged.reshape(BLOCKS, CX, CY, CZ), -ROTATE, axis=0)


def rolled_faces(values, per_side):
    plane_step = per_side * per_side
    return [jnp.concatenate([jnp.roll(values[:, -1:], plane_step, axis=0), values[:, :-1]], axis=1),
            jnp.concatenate([values[:, 1:], jnp.roll(values[:, :1], -plane_step, axis=0)], axis=1),
            jnp.concatenate([jnp.roll(values[:, :, -1:], per_side, axis=0), values[:, :, :-1]], axis=2),
            jnp.concatenate([values[:, :, 1:], jnp.roll(values[:, :, :1], -per_side, axis=0)], axis=2),
            jnp.concatenate([jnp.roll(values[:, :, :, -1:], 1, axis=0), values[:, :, :, :-1]], axis=3),
            jnp.concatenate([values[:, :, :, 1:], jnp.roll(values[:, :, :, :1], -1, axis=0)], axis=3)]


def coefficients(permeab, neighbors, scaling):
    face_coefs = [0.5 * (permeab + beside) for beside in neighbors]
    total_sum = face_coefs[0]
    for number in range(1, 6):
        total_sum = total_sum + face_coefs[number]
    return face_coefs, scaling * total_sum


def operate(values, neighbors, face_coefs, scaling):
    total_sum = face_coefs[0] * (values - neighbors[0])
    for number in range(1, 6):
        total_sum = total_sum + face_coefs[number] * (values - neighbors[number])
    return scaling * total_sum


def smooth(values, right_side, face_coefs, diagonal, scaling):
    return values + OMEGA * (right_side - operate(values, rolled_faces(values, SIDE), face_coefs, scaling)) / diagonal


def coarsen(values):
    count_b, size_x, size_y, size_z = values.shape
    return values.reshape(count_b, size_x // 2, 2, size_y // 2, 2, size_z // 2, 2).mean(axis=(2, 4, 6))


def refine(values):
    return jnp.repeat(jnp.repeat(jnp.repeat(values, 2, axis=1), 2, axis=2), 2, axis=3)


def reference(perm_class, class_values, well_cells, well_rates, guess):
    permeab = jnp.zeros(perm_class.shape, jnp.float32)
    for number in range(NCLASS):
        permeab = permeab + jnp.where(perm_class == number, class_values[number], 0.0)
    source = to_blocks(jnp.zeros((NX * NY * NZ,), jnp.float32).at[well_cells].add(well_rates).reshape(NX, NY, NZ))
    perms = [permeab]
    for level_no in range(LEVELS):
        perms.append(coarsen(perms[-1]))
    coefs = [coefficients(perms[level_no], rolled_faces(perms[level_no], SIDE), 0.25 ** level_no) for level_no in range(LEVELS + 1)]
    values = guess
    right_side = source
    stored = []
    rights = []
    for level_no in range(LEVELS):
        face_coefs, diagonal = coefs[level_no]
        scaling = 0.25 ** level_no
        if level_no == 0:
            count_sw = SWEEPS
        else:
            values = OMEGA * right_side / diagonal
            count_sw = SWEEPS - 1
        for sweep_no in range(count_sw):
            values = smooth(values, right_side, face_coefs, diagonal, scaling)
        leftover = right_side - operate(values, rolled_faces(values, SIDE), face_coefs, scaling)
        stored.append(values)
        rights.append(right_side)
        right_side = coarsen(leftover)
    face_coefs, diagonal = coefs[LEVELS]
    scaling = 0.25 ** LEVELS
    correction = OMEGA * right_side / diagonal
    for sweep_no in range(CSWEEPS - 1):
        correction = smooth(correction, right_side, face_coefs, diagonal, scaling)
    for level_no in reversed(range(LEVELS)):
        face_coefs, diagonal = coefs[level_no]
        scaling = 0.25 ** level_no
        values = stored[level_no] + refine(correction)
        for sweep_no in range(SWEEPS):
            values = smooth(values, rights[level_no], face_coefs, diagonal, scaling)
        correction = values
    residual = source - operate(correction, rolled_faces(correction, SIDE), coefs[0][0], 1.0)
    return correction, residual
```

```python
from functools import partial

import jax
import jax.numpy as jnp
from jax import lax
from jax.sharding import PartitionSpec as P

LEVELS = 3
SWEEPS = 2
CSWEEPS = 6


OMEGA = 0.8


def shifted(shard, axis, by):
    peers = lax.axis_size(axis)
    return lax.ppermute(shard, axis, [(i, (i + by) % peers) for i in range(peers)])


def exchange_faces(values, per_side):
    lower_x = shifted(values[-1:], "space", per_side * per_side)
    upper_x = shifted(values[:1], "space", -per_side * per_side)
    lower_y = shifted(values[:, -1:], "space", per_side)
    upper_y = shifted(values[:, :1], "space", -per_side)
    lower_z = shifted(values[:, :, -1:], "space", 1)
    upper_z = shifted(values[:, :, :1], "space", -1)
    return [
        jnp.concatenate([lower_x, values[:-1]], axis=0),
        jnp.concatenate([values[1:], upper_x], axis=0),
        jnp.concatenate([lower_y, values[:, :-1]], axis=1),
        jnp.concatenate([values[:, 1:], upper_y], axis=1),
        jnp.concatenate([lower_z, values[:, :, :-1]], axis=2),
        jnp.concatenate([values[:, :, 1:], upper_z], axis=2),
    ]


def rolled_faces(values, per_side):
    plane_step = per_side * per_side
    return [
        jnp.concatenate([jnp.roll(values[:, -1:], plane_step, axis=0), values[:, :-1]], axis=1),
        jnp.concatenate([values[:, 1:], jnp.roll(values[:, :1], -plane_step, axis=0)], axis=1),
        jnp.concatenate([jnp.roll(values[:, :, -1:], per_side, axis=0), values[:, :, :-1]], axis=2),
        jnp.concatenate([values[:, :, 1:], jnp.roll(values[:, :, :1], -per_side, axis=0)], axis=2),
        jnp.concatenate([jnp.roll(values[:, :, :, -1:], 1, axis=0), values[:, :, :, :-1]], axis=3),
        jnp.concatenate([values[:, :, :, 1:], jnp.roll(values[:, :, :, :1], -1, axis=0)], axis=3),
    ]


def coefficients(permeab, neighbors, scaling):
    face_coefs = [0.5 * (permeab + beside) for beside in neighbors]
    total_sum = face_coefs[0]
    for number in range(1, 6):
        total_sum = total_sum + face_coefs[number]
    return (face_coefs, scaling * total_sum)


def operate(values, neighbors, face_coefs, scaling):
    total_sum = face_coefs[0] * (values - neighbors[0])
    for number in range(1, 6):
        total_sum = total_sum + face_coefs[number] * (values - neighbors[number])
    return scaling * total_sum


def smooth(values, right_side, face_coefs, diagonal, scaling, per_side):
    neighbors = rolled_faces(values, per_side)
    return values + OMEGA * (right_side - operate(values, neighbors, face_coefs, scaling)) / diagonal


def coarsen_all(values):
    count_b, size_x, size_y, size_z = values.shape
    return values.reshape(count_b, size_x // 2, 2, size_y // 2, 2, size_z // 2, 2).mean(
        axis=(2, 4, 6)
    )


def refine_all(values):
    return jnp.repeat(jnp.repeat(jnp.repeat(values, 2, axis=1), 2, axis=2), 2, axis=3)


def whole_source(well_cells, well_rates, count_b, per_side, width_x, width_y, width_z):
    row_len = per_side * width_z
    plane = per_side * width_y * row_len
    glob_x = well_cells // plane
    glob_y = well_cells // row_len % (per_side * width_y)
    glob_z = well_cells % row_len
    block = ((glob_x // width_x) * per_side + glob_y // width_y) * per_side + glob_z // width_z
    row = (block - (per_side * per_side + per_side + 1)) % count_b
    onehot_r = jnp.where(row[:, None] == jnp.arange(count_b)[None, :], well_rates[:, None], 0.0)
    onehot_x = jnp.where((glob_x % width_x)[:, None] == jnp.arange(width_x)[None, :], 1.0, 0.0)
    onehot_y = jnp.where((glob_y % width_y)[:, None] == jnp.arange(width_y)[None, :], 1.0, 0.0)
    onehot_z = jnp.where((glob_z % width_z)[:, None] == jnp.arange(width_z)[None, :], 1.0, 0.0)
    count_w = well_cells.shape[0]
    left = (onehot_r[:, :, None] * onehot_x[:, None, :]).reshape(count_w, count_b * width_x)
    right = (onehot_y[:, :, None] * onehot_z[:, None, :]).reshape(count_w, width_y * width_z)
    source = jnp.einsum(
        "wa,wb->ab",
        left.astype(jnp.float32),
        right.astype(jnp.float32),
        precision=lax.Precision.HIGHEST,
    )
    return source.reshape(count_b, width_x, width_y, width_z)


def v_cycle(permeab, source, guess, per_side):
    perms = [permeab]
    for level_no in range(LEVELS):
        perms.append(coarsen_all(perms[-1]))
    coefs = [
        coefficients(perms[level_no], rolled_faces(perms[level_no], per_side), 0.25**level_no)
        for level_no in range(LEVELS + 1)
    ]
    values = guess
    right_side = source
    stored = []
    rights = []
    for level_no in range(LEVELS):
        face_coefs, diagonal = coefs[level_no]
        scaling = 0.25**level_no
        if level_no == 0:
            count_sw = SWEEPS
        else:
            values = OMEGA * right_side / diagonal
            count_sw = SWEEPS - 1
        for sweep_no in range(count_sw):
            values = smooth(values, right_side, face_coefs, diagonal, scaling, per_side)
        leftover = right_side - operate(
            values, rolled_faces(values, per_side), face_coefs, scaling
        )
        stored.append(values)
        rights.append(right_side)
        right_side = coarsen_all(leftover)
    face_coefs, diagonal = coefs[LEVELS]
    scaling = 0.25**LEVELS
    correction = OMEGA * right_side / diagonal
    for sweep_no in range(CSWEEPS - 1):
        correction = smooth(correction, right_side, face_coefs, diagonal, scaling, per_side)
    for level_no in reversed(range(LEVELS)):
        face_coefs, diagonal = coefs[level_no]
        scaling = 0.25**level_no
        values = stored[level_no] + refine_all(correction)
        for sweep_no in range(SWEEPS):
            values = smooth(values, rights[level_no], face_coefs, diagonal, scaling, per_side)
        correction = values
    residual = source - operate(
        correction, rolled_faces(correction, per_side), coefs[0][0], 1.0
    )
    return correction, residual


def smooth_with(values, right_side, face_coefs, diagonal, scaling, neighbour):
    return (
        values
        + OMEGA * (right_side - operate(values, neighbour(values), face_coefs, scaling)) / diagonal
    )


def coarsen(values):
    size_x, size_y, size_z = values.shape
    return values.reshape(size_x // 2, 2, size_y // 2, 2, size_z // 2, 2).mean(axis=(1, 3, 5))


def refine(values):
    return jnp.repeat(jnp.repeat(jnp.repeat(values, 2, axis=0), 2, axis=1), 2, axis=2)


def global_cycle(all_rhs, all_perm, first_level, per_side):
    whole_faces = partial(rolled_faces, per_side=per_side)
    perms = [all_perm]
    perms.append(coarsen_all(perms[-1]))
    coefs = [
        coefficients(perms[number], whole_faces(perms[number]), 0.25 ** (first_level + number))
        for number in range(LEVELS - first_level + 1)
    ]
    right_side = all_rhs
    number = 0
    face_coefs, diagonal = coefs[number]
    scaling = 0.25 ** (first_level + number)
    values = OMEGA * right_side / diagonal
    values = smooth_with(values, right_side, face_coefs, diagonal, scaling, whole_faces)
    leftover = right_side - operate(values, whole_faces(values), face_coefs, scaling)
    stored = [values]
    rights = [right_side]
    right_side = coarsen_all(leftover)
    face_coefs, diagonal = coefs[LEVELS - first_level]
    scaling = 0.25**LEVELS
    correction = OMEGA * right_side / diagonal
    for sweep_no in range(CSWEEPS - 1):
        correction = smooth_with(correction, right_side, face_coefs, diagonal, scaling, whole_faces)
    for number in reversed(range(LEVELS - first_level)):
        face_coefs, diagonal = coefs[number]
        scaling = 0.25 ** (first_level + number)
        values = stored[number] + refine_all(correction)
        for sweep_no in range(SWEEPS):
            values = smooth_with(values, rights[number], face_coefs, diagonal, scaling, whole_faces)
        correction = values
    return correction


def distributed_shards(perm_class, class_values, well_cells, well_rates, guess):
    count_dev = lax.axis_size("space")
    per_side = 2 + 2 * (count_dev // 64)
    my_row = lax.axis_index("space")
    block_no = (my_row + per_side * per_side + per_side + 1) % count_dev
    block_x = block_no // (per_side * per_side)
    block_y = block_no // per_side % per_side
    block_z = block_no % per_side
    classes = perm_class[0]
    width_x, width_y, width_z = classes.shape
    neighbour = partial(exchange_faces, per_side=per_side)
    permeab = jnp.zeros(classes.shape, jnp.float32)
    for number in range(class_values.shape[0]):
        permeab = permeab + jnp.where(classes == number, class_values[number], 0.0)
    row_len = per_side * width_z
    plane = per_side * width_y * row_len
    glob_x = well_cells // plane
    glob_y = well_cells // row_len % (per_side * width_y)
    glob_z = well_cells % row_len
    onehot_x = jnp.where(
        (glob_x - block_x * width_x)[:, None] == jnp.arange(width_x)[None, :],
        well_rates[:, None],
        0.0,
    )
    onehot_y = jnp.where(
        (glob_y - block_y * width_y)[:, None] == jnp.arange(width_y)[None, :], 1.0, 0.0
    ).astype(jnp.float32)
    onehot_z = jnp.where(
        (glob_z - block_z * width_z)[:, None] == jnp.arange(width_z)[None, :], 1.0, 0.0
    ).astype(jnp.float32)
    source = jnp.einsum(
        "wi,wj,wk->ijk", onehot_x, onehot_y, onehot_z, precision=lax.Precision.HIGHEST
    )
    perms = [permeab]
    for level_no in range(LEVELS):
        perms.append(coarsen(perms[-1]))
    top_level = LEVELS - 1
    coefs = [
        coefficients(perms[level_no], neighbour(perms[level_no]), 0.25**level_no)
        for level_no in range(top_level)
    ]
    values = guess[0]
    right_side = source
    stored = []
    rights = []
    for level_no in range(top_level):
        face_coefs, diagonal = coefs[level_no]
        scaling = 0.25**level_no
        if level_no == 0:
            count_sw = SWEEPS
        else:
            values = OMEGA * right_side / diagonal
            count_sw = SWEEPS - 1
        for sweep_no in range(count_sw):
            values = smooth_with(values, right_side, face_coefs, diagonal, scaling, neighbour)
        leftover = right_side - operate(values, neighbour(values), face_coefs, scaling)
        stored.append(values)
        rights.append(right_side)
        right_side = coarsen(leftover)
    scaling = 0.25**LEVELS
    all_rhs, all_perm = (
        lax.all_gather(right_side[None], "space", axis=0, tiled=True),
        lax.all_gather(perms[top_level][None], "space", axis=0, tiled=True),
    )
    coarse = global_cycle(all_rhs, all_perm, top_level, per_side)
    correction = lax.dynamic_index_in_dim(coarse, my_row, 0, keepdims=False)
    for level_no in reversed(range(top_level)):
        face_coefs, diagonal = coefs[level_no]
        scaling = 0.25**level_no
        values = stored[level_no] + refine(correction)
        for sweep_no in range(SWEEPS):
            values = smooth_with(values, rights[level_no], face_coefs, diagonal, scaling, neighbour)
        correction = values
    residual = source - operate(correction, neighbour(correction), coefs[0][0], 1.0)
    return (correction[None], residual[None])


def replicated_shards(perm_class, class_values, well_cells, well_rates, guess):
    count_dev = lax.axis_size("space")
    per_side = 2 + 2 * (count_dev // 64)
    my_row = lax.axis_index("space")
    classes = perm_class[0]
    width_x, width_y, width_z = classes.shape
    permeab = jnp.zeros(classes.shape, jnp.float32)
    for number in range(class_values.shape[0]):
        permeab = permeab + jnp.where(classes == number, class_values[number], 0.0)
    local = jnp.stack([permeab, guess[0]])[None]
    gathered = lax.all_gather(local, "space", axis=0, tiled=True)
    all_perm = gathered[:, 0]
    all_guess = gathered[:, 1]
    source = whole_source(
        well_cells, well_rates, count_dev, per_side, width_x, width_y, width_z
    )
    pressure, residual = v_cycle(all_perm, source, all_guess, per_side)
    mine_p = lax.dynamic_index_in_dim(pressure, my_row, 0, keepdims=True)
    mine_r = lax.dynamic_index_in_dim(residual, my_row, 0, keepdims=True)
    return (mine_p, mine_r)


def shards(perm_class, class_values, well_cells, well_rates, guess):
    count_dev = lax.axis_size("space")
    if count_dev * perm_class[0].size <= 2**18:
        return replicated_shards(perm_class, class_values, well_cells, well_rates, guess)
    return distributed_shards(perm_class, class_values, well_cells, well_rates, guess)


def solution(mesh):
    return jax.shard_map(
        shards,
        mesh=mesh,
        in_specs=(
            P("space", None, None, None),
            P(),
            P("real"),
            P("real"),
            P(("real", "space"), None, None, None),
        ),
        out_specs=(P(("real", "space"), None, None, None), P(("real", "space"), None, None, None)),
        check_vma=False,
    )
```

```python
import jax
import jax.numpy as jnp
from jax import lax
from jax.sharding import PartitionSpec as P

LEVELS = 3
SWEEPS = 2
CSWEEPS = 6


OMEGA = 0.8


def shifted(shard, axis, by):
    peers = lax.axis_size(axis)
    return lax.ppermute(shard, axis, [(i, (i + by) % peers) for i in range(peers)])


def exchange(fields, per_side):
    count_dev = lax.axis_size("space")
    plane_step = per_side * per_side
    if (2 * plane_step) % count_dev == 0:
        both_x = shifted(jnp.concatenate([fields[:, -1:], fields[:, :1]], axis=1), "space", plane_step)
        lower_x, upper_x = both_x[:, :1], both_x[:, 1:]
    else:
        lower_x = shifted(fields[:, -1:], "space", plane_step)
        upper_x = shifted(fields[:, :1], "space", -plane_step)
    lower_y = shifted(fields[:, :, -1:], "space", per_side)
    upper_y = shifted(fields[:, :, :1], "space", -per_side)
    lower_z = shifted(fields[:, :, :, -1:], "space", 1)
    upper_z = shifted(fields[:, :, :, :1], "space", -1)
    return [lower_x, upper_x, lower_y, upper_y, lower_z, upper_z]


def pick(faces, number):
    return [face[number] for face in faces]


def with_faces(values, faces):
    lower_x, upper_x, lower_y, upper_y, lower_z, upper_z = faces
    return [
        jnp.concatenate([lower_x, values[:-1]], axis=0),
        jnp.concatenate([values[1:], upper_x], axis=0),
        jnp.concatenate([lower_y, values[:, :-1]], axis=1),
        jnp.concatenate([values[:, 1:], upper_y], axis=1),
        jnp.concatenate([lower_z, values[:, :, :-1]], axis=2),
        jnp.concatenate([values[:, :, 1:], upper_z], axis=2),
    ]


def rolled_faces(values, per_side):
    plane_step = per_side * per_side
    return [
        jnp.concatenate([jnp.roll(values[:, -1:], plane_step, axis=0), values[:, :-1]], axis=1),
        jnp.concatenate([values[:, 1:], jnp.roll(values[:, :1], -plane_step, axis=0)], axis=1),
        jnp.concatenate([jnp.roll(values[:, :, -1:], per_side, axis=0), values[:, :, :-1]], axis=2),
        jnp.concatenate([values[:, :, 1:], jnp.roll(values[:, :, :1], -per_side, axis=0)], axis=2),
        jnp.concatenate([jnp.roll(values[:, :, :, -1:], 1, axis=0), values[:, :, :, :-1]], axis=3),
        jnp.concatenate([values[:, :, :, 1:], jnp.roll(values[:, :, :, :1], -1, axis=0)], axis=3),
    ]


def coefficients(permeab, neighbors, scaling):
    face_coefs = [0.5 * (permeab + beside) for beside in neighbors]
    total_sum = face_coefs[0]
    for number in range(1, 6):
        total_sum = total_sum + face_coefs[number]
    return (face_coefs, scaling * total_sum)


def operate(values, neighbors, face_coefs, scaling):
    total_sum = face_coefs[0] * (values - neighbors[0])
    for number in range(1, 6):
        total_sum = total_sum + face_coefs[number] * (values - neighbors[number])
    return scaling * total_sum


def smooth(values, right_side, face_coefs, diagonal, scaling, neighbors):
    return values + OMEGA * (right_side - operate(values, neighbors, face_coefs, scaling)) / diagonal


def coarsen(values):
    size_x, size_y, size_z = values.shape
    return values.reshape(size_x // 2, 2, size_y // 2, 2, size_z // 2, 2).mean(axis=(1, 3, 5))


def refine(values):
    return jnp.repeat(jnp.repeat(jnp.repeat(values, 2, axis=0), 2, axis=1), 2, axis=2)


def coarsen_all(values):
    count_b, size_x, size_y, size_z = values.shape
    return values.reshape(count_b, size_x // 2, 2, size_y // 2, 2, size_z // 2, 2).mean(
        axis=(2, 4, 6)
    )


def refine_all(values):
    return jnp.repeat(jnp.repeat(jnp.repeat(values, 2, axis=1), 2, axis=2), 2, axis=3)


def refine_face(face):
    return jnp.repeat(jnp.repeat(face, 2, axis=0), 2, axis=1)


def refined_faces(coarse_all, my_row, per_side):
    count_b = coarse_all.shape[0]

    def row(offset):
        return lax.dynamic_index_in_dim(coarse_all, (my_row + offset) % count_b, 0, keepdims=False)

    plane_step = per_side * per_side
    return [
        refine_face(row(-plane_step)[-1])[None],
        refine_face(row(plane_step)[0])[None],
        refine_face(row(-per_side)[:, -1])[:, None],
        refine_face(row(per_side)[:, 0])[:, None],
        refine_face(row(-1)[:, :, -1])[:, :, None],
        refine_face(row(1)[:, :, 0])[:, :, None],
    ]


def global_cycle(all_rhs, all_perm, first_level, per_side):
    perms = [all_perm]
    for number in range(LEVELS - first_level):
        perms.append(coarsen_all(perms[-1]))
    coefs = [
        coefficients(
            perms[number], rolled_faces(perms[number], per_side), 0.25 ** (first_level + number)
        )
        for number in range(LEVELS - first_level + 1)
    ]
    right_side = all_rhs
    stored = []
    rights = []
    for number in range(LEVELS - first_level):
        face_coefs, diagonal = coefs[number]
        scaling = 0.25 ** (first_level + number)
        values = OMEGA * right_side / diagonal
        for sweep_no in range(SWEEPS - 1):
            values = smooth(
                values, right_side, face_coefs, diagonal, scaling, rolled_faces(values, per_side)
            )
        leftover = right_side - operate(
            values, rolled_faces(values, per_side), face_coefs, scaling
        )
        stored.append(values)
        rights.append(right_side)
        right_side = coarsen_all(leftover)
    face_coefs, diagonal = coefs[LEVELS - first_level]
    scaling = 0.25**LEVELS
    correction = OMEGA * right_side / diagonal
    for sweep_no in range(CSWEEPS - 1):
        correction = smooth(
            correction, right_side, face_coefs, diagonal, scaling, rolled_faces(correction, per_side)
        )
    for number in reversed(range(LEVELS - first_level)):
        face_coefs, diagonal = coefs[number]
        scaling = 0.25 ** (first_level + number)
        values = stored[number] + refine_all(correction)
        for sweep_no in range(SWEEPS):
            values = smooth(
                values, rights[number], face_coefs, diagonal, scaling, rolled_faces(values, per_side)
            )
        correction = values
    return correction


def shards(perm_class, class_values, well_cells, well_rates, guess):
    count_dev = lax.axis_size("space")
    per_side = 2 + 2 * (count_dev // 64)
    my_row = lax.axis_index("space")
    block_no = (my_row + per_side * per_side + per_side + 1) % count_dev
    block_x = block_no // (per_side * per_side)
    block_y = block_no // per_side % per_side
    block_z = block_no % per_side
    classes = perm_class[0]
    width_x, width_y, width_z = classes.shape
    permeab = jnp.zeros(classes.shape, jnp.float32)
    for number in range(class_values.shape[0]):
        permeab = permeab + jnp.where(classes == number, class_values[number], 0.0)
    row_len = per_side * width_z
    plane = per_side * width_y * row_len
    glob_x = well_cells // plane
    glob_y = well_cells // row_len % (per_side * width_y)
    glob_z = well_cells % row_len
    onehot_x = jnp.where(
        (glob_x - block_x * width_x)[:, None] == jnp.arange(width_x)[None, :],
        well_rates[:, None],
        0.0,
    )
    onehot_y = jnp.where(
        (glob_y - block_y * width_y)[:, None] == jnp.arange(width_y)[None, :], 1.0, 0.0
    ).astype(jnp.float32)
    onehot_z = jnp.where(
        (glob_z - block_z * width_z)[:, None] == jnp.arange(width_z)[None, :], 1.0, 0.0
    ).astype(jnp.float32)
    source = jnp.einsum(
        "wi,wj,wk->ijk", onehot_x, onehot_y, onehot_z, precision=lax.Precision.HIGHEST
    )

    values = guess[0]
    first = exchange(jnp.stack([permeab, values]), per_side)
    face_coefs, diagonal = coefficients(permeab, with_faces(permeab, pick(first, 0)), 1.0)
    values = smooth(values, source, face_coefs, diagonal, 1.0, with_faces(values, pick(first, 1)))
    for sweep_no in range(SWEEPS - 1):
        faces = pick(exchange(values[None], per_side), 0)
        values = smooth(values, source, face_coefs, diagonal, 1.0, with_faces(values, faces))
    stored_faces = pick(exchange(values[None], per_side), 0)
    leftover = source - operate(values, with_faces(values, stored_faces), face_coefs, 1.0)
    stored = values

    coarse = jnp.stack([coarsen(permeab), coarsen(leftover)])[None]
    gathered = lax.all_gather(coarse, "space", axis=0, tiled=True)
    correction_all = global_cycle(gathered[:, 1], gathered[:, 0], 1, per_side)

    correction = lax.dynamic_index_in_dim(correction_all, my_row, 0, keepdims=False)
    values = stored + refine(correction)
    faces = [
        mine + theirs
        for mine, theirs in zip(stored_faces, refined_faces(correction_all, my_row, per_side))
    ]
    values = smooth(values, source, face_coefs, diagonal, 1.0, with_faces(values, faces))
    for sweep_no in range(SWEEPS - 1):
        faces = pick(exchange(values[None], per_side), 0)
        values = smooth(values, source, face_coefs, diagonal, 1.0, with_faces(values, faces))
    faces = pick(exchange(values[None], per_side), 0)
    residual = source - operate(values, with_faces(values, faces), face_coefs, 1.0)
    return (values[None], residual[None])


def solution(mesh):
    return jax.shard_map(
        shards,
        mesh=mesh,
        in_specs=(
            P("space", None, None, None),
            P(),
            P("real"),
            P("real"),
            P(("real", "space"), None, None, None),
        ),
        out_specs=(P(("real", "space"), None, None, None), P(("real", "space"), None, None, None)),
        check_vma=False,
    )
```

```python
import jax
import jax.numpy as jnp
from jax import lax
from jax.sharding import PartitionSpec as P

LEVELS = 3
SWEEPS = 2
CSWEEPS = 6


OMEGA = 0.8


def shifted(shard, axis, by):
    peers = lax.axis_size(axis)
    return lax.ppermute(shard, axis, [(i, (i + by) % peers) for i in range(peers)])


def exchange(fields, per_side):
    count_dev = lax.axis_size("space")
    plane_step = per_side * per_side
    if (2 * plane_step) % count_dev == 0:
        both_x = shifted(jnp.concatenate([fields[:, -1:], fields[:, :1]], axis=1), "space", plane_step)
        lower_x, upper_x = both_x[:, :1], both_x[:, 1:]
    else:
        lower_x = shifted(fields[:, -1:], "space", plane_step)
        upper_x = shifted(fields[:, :1], "space", -plane_step)
    lower_y = shifted(fields[:, :, -1:], "space", per_side)
    upper_y = shifted(fields[:, :, :1], "space", -per_side)
    lower_z = shifted(fields[:, :, :, -1:], "space", 1)
    upper_z = shifted(fields[:, :, :, :1], "space", -1)
    return [lower_x, upper_x, lower_y, upper_y, lower_z, upper_z]


def own_faces(values):
    return [values[-1:], values[:1], values[:, -1:], values[:, :1], values[:, :, -1:], values[:, :, :1]]


def exchange_mixed(fields, per_side):
    count_dev = lax.axis_size("space")
    plane_step = per_side * per_side
    outgoing = [own_faces(values) for values in fields]
    shifts = [plane_step, -plane_step, per_side, -per_side, 1, -1]
    flat = [jnp.concatenate([faces[d].reshape(-1) for faces in outgoing]) for d in range(6)]
    received = [None] * 6
    if (2 * plane_step) % count_dev == 0:
        both = shifted(jnp.concatenate([flat[0], flat[1]]), "space", plane_step)
        received[0], received[1] = both[: flat[0].shape[0]], both[flat[0].shape[0] :]
        rest = range(2, 6)
    else:
        rest = range(6)
    for d in rest:
        received[d] = shifted(flat[d], "space", shifts[d])
    result = [[None] * 6 for _ in fields]
    for d in range(6):
        offset = 0
        for number, faces in enumerate(outgoing):
            size = faces[d].size
            result[number][d] = received[d][offset : offset + size].reshape(faces[d].shape)
            offset += size
    return result


def gather_rows(block, per_side):
    count_dev = lax.axis_size("space")
    if count_dev > 16:
        return lax.all_gather(block[None], "space", axis=0, tiled=True)
    my_row = lax.axis_index("space")
    by_offset = jnp.stack([block] + [shifted(block, "space", k) for k in range(1, count_dev)])
    return jnp.take(by_offset, (my_row - jnp.arange(count_dev)) % count_dev, axis=0)


def pick(faces, number):
    return [face[number] for face in faces]


def with_faces(values, faces):
    lower_x, upper_x, lower_y, upper_y, lower_z, upper_z = faces
    return [
        jnp.concatenate([lower_x, values[:-1]], axis=0),
        jnp.concatenate([values[1:], upper_x], axis=0),
        jnp.concatenate([lower_y, values[:, :-1]], axis=1),
        jnp.concatenate([values[:, 1:], upper_y], axis=1),
        jnp.concatenate([lower_z, values[:, :, :-1]], axis=2),
        jnp.concatenate([values[:, :, 1:], upper_z], axis=2),
    ]


def rolled_faces(values, per_side):
    plane_step = per_side * per_side
    return [
        jnp.concatenate([jnp.roll(values[:, -1:], plane_step, axis=0), values[:, :-1]], axis=1),
        jnp.concatenate([values[:, 1:], jnp.roll(values[:, :1], -plane_step, axis=0)], axis=1),
        jnp.concatenate([jnp.roll(values[:, :, -1:], per_side, axis=0), values[:, :, :-1]], axis=2),
        jnp.concatenate([values[:, :, 1:], jnp.roll(values[:, :, :1], -per_side, axis=0)], axis=2),
        jnp.concatenate([jnp.roll(values[:, :, :, -1:], 1, axis=0), values[:, :, :, :-1]], axis=3),
        jnp.concatenate([values[:, :, :, 1:], jnp.roll(values[:, :, :, :1], -1, axis=0)], axis=3),
    ]


def coefficients(permeab, neighbors, scaling):
    face_coefs = [0.5 * (permeab + beside) for beside in neighbors]
    total_sum = face_coefs[0]
    for number in range(1, 6):
        total_sum = total_sum + face_coefs[number]
    return (face_coefs, scaling * total_sum)


def operate(values, neighbors, face_coefs, scaling):
    total_sum = face_coefs[0] * (values - neighbors[0])
    for number in range(1, 6):
        total_sum = total_sum + face_coefs[number] * (values - neighbors[number])
    return scaling * total_sum


def smooth(values, right_side, face_coefs, diagonal, scaling, neighbors):
    return values + OMEGA * (right_side - operate(values, neighbors, face_coefs, scaling)) / diagonal


def coarsen(values):
    size_x, size_y, size_z = values.shape
    return values.reshape(size_x // 2, 2, size_y // 2, 2, size_z // 2, 2).mean(axis=(1, 3, 5))


def refine(values):
    return jnp.repeat(jnp.repeat(jnp.repeat(values, 2, axis=0), 2, axis=1), 2, axis=2)


def coarsen_all(values):
    count_b, size_x, size_y, size_z = values.shape
    return values.reshape(count_b, size_x // 2, 2, size_y // 2, 2, size_z // 2, 2).mean(
        axis=(2, 4, 6)
    )


def refine_all(values):
    return jnp.repeat(jnp.repeat(jnp.repeat(values, 2, axis=1), 2, axis=2), 2, axis=3)


def refine_face(face):
    return jnp.repeat(jnp.repeat(face, 2, axis=0), 2, axis=1)


def refine_face_of(face):
    for axis in range(3):
        if face.shape[axis] != 1:
            face = jnp.repeat(face, 2, axis=axis)
    return face


def refined_faces(coarse_all, my_row, per_side):
    count_b = coarse_all.shape[0]

    def row(offset):
        return lax.dynamic_index_in_dim(coarse_all, (my_row + offset) % count_b, 0, keepdims=False)

    plane_step = per_side * per_side
    return [
        refine_face(row(-plane_step)[-1])[None],
        refine_face(row(plane_step)[0])[None],
        refine_face(row(-per_side)[:, -1])[:, None],
        refine_face(row(per_side)[:, 0])[:, None],
        refine_face(row(-1)[:, :, -1])[:, :, None],
        refine_face(row(1)[:, :, 0])[:, :, None],
    ]


def global_cycle(all_rhs, all_perm, first_level, per_side):
    perms = [all_perm]
    for number in range(LEVELS - first_level):
        perms.append(coarsen_all(perms[-1]))
    coefs = [
        coefficients(
            perms[number], rolled_faces(perms[number], per_side), 0.25 ** (first_level + number)
        )
        for number in range(LEVELS - first_level + 1)
    ]
    right_side = all_rhs
    stored = []
    rights = []
    for number in range(LEVELS - first_level):
        face_coefs, diagonal = coefs[number]
        scaling = 0.25 ** (first_level + number)
        values = OMEGA * right_side / diagonal
        for sweep_no in range(SWEEPS - 1):
            values = smooth(
                values, right_side, face_coefs, diagonal, scaling, rolled_faces(values, per_side)
            )
        leftover = right_side - operate(
            values, rolled_faces(values, per_side), face_coefs, scaling
        )
        stored.append(values)
        rights.append(right_side)
        right_side = coarsen_all(leftover)
    face_coefs, diagonal = coefs[LEVELS - first_level]
    scaling = 0.25**LEVELS
    correction = OMEGA * right_side / diagonal
    for sweep_no in range(CSWEEPS - 1):
        correction = smooth(
            correction, right_side, face_coefs, diagonal, scaling, rolled_faces(correction, per_side)
        )
    for number in reversed(range(LEVELS - first_level)):
        face_coefs, diagonal = coefs[number]
        scaling = 0.25 ** (first_level + number)
        values = stored[number] + refine_all(correction)
        for sweep_no in range(SWEEPS):
            values = smooth(
                values, rights[number], face_coefs, diagonal, scaling, rolled_faces(values, per_side)
            )
        correction = values
    return correction


def shards(perm_class, class_values, well_cells, well_rates, guess):
    count_dev = lax.axis_size("space")
    per_side = 2 + 2 * (count_dev // 64)
    my_row = lax.axis_index("space")
    block_no = (my_row + per_side * per_side + per_side + 1) % count_dev
    block_x = block_no // (per_side * per_side)
    block_y = block_no // per_side % per_side
    block_z = block_no % per_side
    classes = perm_class[0]
    width_x, width_y, width_z = classes.shape
    permeab = jnp.zeros(classes.shape, jnp.float32)
    for number in range(class_values.shape[0]):
        permeab = permeab + jnp.where(classes == number, class_values[number], 0.0)
    row_len = per_side * width_z
    plane = per_side * width_y * row_len
    glob_x = well_cells // plane
    glob_y = well_cells // row_len % (per_side * width_y)
    glob_z = well_cells % row_len
    onehot_x = jnp.where(
        (glob_x - block_x * width_x)[:, None] == jnp.arange(width_x)[None, :],
        well_rates[:, None],
        0.0,
    )
    onehot_y = jnp.where(
        (glob_y - block_y * width_y)[:, None] == jnp.arange(width_y)[None, :], 1.0, 0.0
    ).astype(jnp.float32)
    onehot_z = jnp.where(
        (glob_z - block_z * width_z)[:, None] == jnp.arange(width_z)[None, :], 1.0, 0.0
    ).astype(jnp.float32)
    source = jnp.einsum(
        "wi,wj,wk->ijk", onehot_x, onehot_y, onehot_z, precision=lax.Precision.HIGHEST
    )

    values = guess[0]
    coarse_perm = coarsen(permeab)
    first = exchange_mixed([permeab, values, coarse_perm], per_side)
    face_coefs, diagonal = coefficients(permeab, with_faces(permeab, first[0]), 1.0)
    values = smooth(values, source, face_coefs, diagonal, 1.0, with_faces(values, first[1]))
    for sweep_no in range(SWEEPS - 1):
        faces = pick(exchange(values[None], per_side), 0)
        values = smooth(values, source, face_coefs, diagonal, 1.0, with_faces(values, faces))
    stored_faces = pick(exchange(values[None], per_side), 0)
    leftover = source - operate(values, with_faces(values, stored_faces), face_coefs, 1.0)
    stored = values

    scaling = 0.25
    right_1 = coarsen(leftover)
    coefs_1, diagonal_1 = coefficients(coarse_perm, with_faces(coarse_perm, first[2]), scaling)
    values_1 = OMEGA * right_1 / diagonal_1
    for sweep_no in range(SWEEPS - 1):
        faces = pick(exchange(values_1[None], per_side), 0)
        values_1 = smooth(values_1, right_1, coefs_1, diagonal_1, scaling, with_faces(values_1, faces))
    stored_faces_1 = pick(exchange(values_1[None], per_side), 0)
    leftover_1 = right_1 - operate(values_1, with_faces(values_1, stored_faces_1), coefs_1, scaling)
    stored_1 = values_1

    gathered = gather_rows(jnp.stack([coarsen(coarse_perm), coarsen(leftover_1)]), per_side)
    correction_all = global_cycle(gathered[:, 1], gathered[:, 0], 2, per_side)

    correction = lax.dynamic_index_in_dim(correction_all, my_row, 0, keepdims=False)
    values_1 = stored_1 + refine(correction)
    faces = [
        mine + theirs
        for mine, theirs in zip(stored_faces_1, refined_faces(correction_all, my_row, per_side))
    ]
    values_1 = smooth(values_1, right_1, coefs_1, diagonal_1, scaling, with_faces(values_1, faces))
    for sweep_no in range(SWEEPS - 1):
        faces = pick(exchange(values_1[None], per_side), 0)
        values_1 = smooth(values_1, right_1, coefs_1, diagonal_1, scaling, with_faces(values_1, faces))
    coarse_faces = pick(exchange(values_1[None], per_side), 0)

    values = stored + refine(values_1)
    faces = [mine + refine_face_of(theirs) for mine, theirs in zip(stored_faces, coarse_faces)]
    values = smooth(values, source, face_coefs, diagonal, 1.0, with_faces(values, faces))
    for sweep_no in range(SWEEPS - 1):
        faces = pick(exchange(values[None], per_side), 0)
        values = smooth(values, source, face_coefs, diagonal, 1.0, with_faces(values, faces))
    faces = pick(exchange(values[None], per_side), 0)
    residual = source - operate(values, with_faces(values, faces), face_coefs, 1.0)
    return (values[None], residual[None])


def solution(mesh):
    return jax.shard_map(
        shards,
        mesh=mesh,
        in_specs=(
            P("space", None, None, None),
            P(),
            P("real"),
            P("real"),
            P(("real", "space"), None, None, None),
        ),
        out_specs=(P(("real", "space"), None, None, None), P(("real", "space"), None, None, None)),
        check_vma=False,
    )
```

```python
import jax
import jax.numpy as jnp
from jax import lax
from jax.sharding import PartitionSpec as P

LEVELS = 3
SWEEPS = 2
CSWEEPS = 6


OMEGA = 0.8


def shifted(shard, axis, by):
    peers = lax.axis_size(axis)
    return lax.ppermute(shard, axis, [(i, (i + by) % peers) for i in range(peers)])


def exchange(fields, per_side):
    count_dev = lax.axis_size("space")
    plane_step = per_side * per_side
    if (2 * plane_step) % count_dev == 0:
        both_x = shifted(jnp.concatenate([fields[:, -1:], fields[:, :1]], axis=1), "space", plane_step)
        lower_x, upper_x = both_x[:, :1], both_x[:, 1:]
    else:
        lower_x = shifted(fields[:, -1:], "space", plane_step)
        upper_x = shifted(fields[:, :1], "space", -plane_step)
    lower_y = shifted(fields[:, :, -1:], "space", per_side)
    upper_y = shifted(fields[:, :, :1], "space", -per_side)
    lower_z = shifted(fields[:, :, :, -1:], "space", 1)
    upper_z = shifted(fields[:, :, :, :1], "space", -1)
    return [lower_x, upper_x, lower_y, upper_y, lower_z, upper_z]


def own_faces(values):
    return [values[-1:], values[:1], values[:, -1:], values[:, :1], values[:, :, -1:], values[:, :, :1]]


def exchange_mixed(fields, per_side):
    count_dev = lax.axis_size("space")
    plane_step = per_side * per_side
    outgoing = [own_faces(values) for values in fields]
    shifts = [plane_step, -plane_step, per_side, -per_side, 1, -1]
    flat = [jnp.concatenate([faces[d].reshape(-1) for faces in outgoing]) for d in range(6)]
    received = [None] * 6
    if (2 * plane_step) % count_dev == 0:
        both = shifted(jnp.concatenate([flat[0], flat[1]]), "space", plane_step)
        received[0], received[1] = both[: flat[0].shape[0]], both[flat[0].shape[0] :]
        rest = range(2, 6)
    else:
        rest = range(6)
    for d in rest:
        received[d] = shifted(flat[d], "space", shifts[d])
    result = [[None] * 6 for _ in fields]
    for d in range(6):
        offset = 0
        for number, faces in enumerate(outgoing):
            size = faces[d].size
            result[number][d] = received[d][offset : offset + size].reshape(faces[d].shape)
            offset += size
    return result


def gather_rows(block, per_side):
    count_dev = lax.axis_size("space")
    if count_dev > 16:
        return lax.all_gather(block[None], "space", axis=0, tiled=True)
    my_row = lax.axis_index("space")
    by_offset = jnp.stack([block] + [shifted(block, "space", k) for k in range(1, count_dev)])
    return jnp.take(by_offset, (my_row - jnp.arange(count_dev)) % count_dev, axis=0)


def pick(faces, number):
    return [face[number] for face in faces]


def with_faces(values, faces):
    lower_x, upper_x, lower_y, upper_y, lower_z, upper_z = faces
    return [
        jnp.concatenate([lower_x, values[:-1]], axis=0),
        jnp.concatenate([values[1:], upper_x], axis=0),
        jnp.concatenate([lower_y, values[:, :-1]], axis=1),
        jnp.concatenate([values[:, 1:], upper_y], axis=1),
        jnp.concatenate([lower_z, values[:, :, :-1]], axis=2),
        jnp.concatenate([values[:, :, 1:], upper_z], axis=2),
    ]


def rolled_faces(values, per_side):
    plane_step = per_side * per_side
    return [
        jnp.concatenate([jnp.roll(values[:, -1:], plane_step, axis=0), values[:, :-1]], axis=1),
        jnp.concatenate([values[:, 1:], jnp.roll(values[:, :1], -plane_step, axis=0)], axis=1),
        jnp.concatenate([jnp.roll(values[:, :, -1:], per_side, axis=0), values[:, :, :-1]], axis=2),
        jnp.concatenate([values[:, :, 1:], jnp.roll(values[:, :, :1], -per_side, axis=0)], axis=2),
        jnp.concatenate([jnp.roll(values[:, :, :, -1:], 1, axis=0), values[:, :, :, :-1]], axis=3),
        jnp.concatenate([values[:, :, :, 1:], jnp.roll(values[:, :, :, :1], -1, axis=0)], axis=3),
    ]


def coefficients(permeab, neighbors, scaling):
    face_coefs = [0.5 * (permeab + beside) for beside in neighbors]
    total_sum = face_coefs[0]
    for number in range(1, 6):
        total_sum = total_sum + face_coefs[number]
    return (face_coefs, scaling * total_sum)


def operate(values, neighbors, face_coefs, scaling):
    total_sum = face_coefs[0] * (values - neighbors[0])
    for number in range(1, 6):
        total_sum = total_sum + face_coefs[number] * (values - neighbors[number])
    return scaling * total_sum


def smooth(values, right_side, face_coefs, diagonal, scaling, neighbors):
    return values + OMEGA * (right_side - operate(values, neighbors, face_coefs, scaling)) / diagonal


def pair_mean(size, scale):
    rows = jnp.arange(size)[:, None] // 2
    cols = jnp.arange(size // 2)[None, :]
    return jnp.where(rows == cols, scale, 0.0).astype(jnp.float32)


def plane_mean(size_x, size_y):
    fine = jnp.arange(size_x * size_y)
    coarse_of = (fine // size_y // 2) * (size_y // 2) + (fine % size_y) // 2
    return jnp.where(
        jnp.arange(size_x * size_y // 4)[:, None] == coarse_of[None, :], 0.25, 0.0
    ).astype(jnp.float32)


def coarsen(values):
    size_x, size_y, size_z = values.shape
    along_z = jnp.dot(
        values.reshape(size_x * size_y, size_z),
        pair_mean(size_z, 0.5),
        precision=lax.Precision.HIGHEST,
    )
    both = jnp.dot(plane_mean(size_x, size_y), along_z, precision=lax.Precision.HIGHEST)
    return both.reshape(size_x // 2, size_y // 2, size_z // 2)


def refine(values):
    return jnp.repeat(jnp.repeat(jnp.repeat(values, 2, axis=0), 2, axis=1), 2, axis=2)


def coarsen_all(values):
    count_b, size_x, size_y, size_z = values.shape
    along_z = jnp.dot(
        values.reshape(count_b * size_x * size_y, size_z),
        pair_mean(size_z, 0.5),
        precision=lax.Precision.HIGHEST,
    ).reshape(count_b, size_x * size_y, size_z // 2)
    both = jnp.einsum(
        "pq,bqz->bpz", plane_mean(size_x, size_y), along_z, precision=lax.Precision.HIGHEST
    )
    return both.reshape(count_b, size_x // 2, size_y // 2, size_z // 2)


def refine_all(values):
    return jnp.repeat(jnp.repeat(jnp.repeat(values, 2, axis=1), 2, axis=2), 2, axis=3)


def refine_face(face):
    return jnp.repeat(jnp.repeat(face, 2, axis=0), 2, axis=1)


def refine_face_of(face):
    for axis in range(3):
        if face.shape[axis] != 1:
            face = jnp.repeat(face, 2, axis=axis)
    return face


def refined_faces(coarse_all, my_row, per_side):
    count_b = coarse_all.shape[0]

    def row(offset):
        return lax.dynamic_index_in_dim(coarse_all, (my_row + offset) % count_b, 0, keepdims=False)

    plane_step = per_side * per_side
    return [
        refine_face(row(-plane_step)[-1])[None],
        refine_face(row(plane_step)[0])[None],
        refine_face(row(-per_side)[:, -1])[:, None],
        refine_face(row(per_side)[:, 0])[:, None],
        refine_face(row(-1)[:, :, -1])[:, :, None],
        refine_face(row(1)[:, :, 0])[:, :, None],
    ]


def global_cycle(all_rhs, all_perm, first_level, per_side):
    perms = [all_perm]
    for number in range(LEVELS - first_level):
        perms.append(coarsen_all(perms[-1]))
    coefs = [
        coefficients(
            perms[number], rolled_faces(perms[number], per_side), 0.25 ** (first_level + number)
        )
        for number in range(LEVELS - first_level + 1)
    ]
    right_side = all_rhs
    stored = []
    rights = []
    for number in range(LEVELS - first_level):
        face_coefs, diagonal = coefs[number]
        scaling = 0.25 ** (first_level + number)
        values = OMEGA * right_side / diagonal
        for sweep_no in range(SWEEPS - 1):
            values = smooth(
                values, right_side, face_coefs, diagonal, scaling, rolled_faces(values, per_side)
            )
        leftover = right_side - operate(
            values, rolled_faces(values, per_side), face_coefs, scaling
        )
        stored.append(values)
        rights.append(right_side)
        right_side = coarsen_all(leftover)
    face_coefs, diagonal = coefs[LEVELS - first_level]
    scaling = 0.25**LEVELS
    correction = OMEGA * right_side / diagonal
    for sweep_no in range(CSWEEPS - 1):
        correction = smooth(
            correction, right_side, face_coefs, diagonal, scaling, rolled_faces(correction, per_side)
        )
    for number in reversed(range(LEVELS - first_level)):
        face_coefs, diagonal = coefs[number]
        scaling = 0.25 ** (first_level + number)
        values = stored[number] + refine_all(correction)
        for sweep_no in range(SWEEPS):
            values = smooth(
                values, rights[number], face_coefs, diagonal, scaling, rolled_faces(values, per_side)
            )
        correction = values
    return correction


def shards(perm_class, class_values, well_cells, well_rates, guess):
    count_dev = lax.axis_size("space")
    per_side = 2 + 2 * (count_dev // 64)
    my_row = lax.axis_index("space")
    block_no = (my_row + per_side * per_side + per_side + 1) % count_dev
    block_x = block_no // (per_side * per_side)
    block_y = block_no // per_side % per_side
    block_z = block_no % per_side
    classes = perm_class[0]
    width_x, width_y, width_z = classes.shape
    permeab = jnp.zeros(classes.shape, jnp.float32)
    for number in range(class_values.shape[0]):
        permeab = permeab + jnp.where(classes == number, class_values[number], 0.0)
    row_len = per_side * width_z
    plane = per_side * width_y * row_len
    glob_x = well_cells // plane
    glob_y = well_cells // row_len % (per_side * width_y)
    glob_z = well_cells % row_len
    onehot_x = jnp.where(
        (glob_x - block_x * width_x)[:, None] == jnp.arange(width_x)[None, :],
        well_rates[:, None],
        0.0,
    )
    onehot_y = jnp.where(
        (glob_y - block_y * width_y)[:, None] == jnp.arange(width_y)[None, :], 1.0, 0.0
    ).astype(jnp.float32)
    onehot_z = jnp.where(
        (glob_z - block_z * width_z)[:, None] == jnp.arange(width_z)[None, :], 1.0, 0.0
    ).astype(jnp.float32)
    source = jnp.einsum(
        "wi,wj,wk->ijk", onehot_x, onehot_y, onehot_z, precision=lax.Precision.HIGHEST
    )

    values = guess[0]
    coarse_perm = coarsen(permeab)
    first = exchange_mixed([permeab, values, coarse_perm], per_side)
    face_coefs, diagonal = coefficients(permeab, with_faces(permeab, first[0]), 1.0)
    values = smooth(values, source, face_coefs, diagonal, 1.0, with_faces(values, first[1]))
    for sweep_no in range(SWEEPS - 1):
        faces = pick(exchange(values[None], per_side), 0)
        values = smooth(values, source, face_coefs, diagonal, 1.0, with_faces(values, faces))
    stored_faces = pick(exchange(values[None], per_side), 0)
    leftover = source - operate(values, with_faces(values, stored_faces), face_coefs, 1.0)
    stored = values

    scaling = 0.25
    right_1 = coarsen(leftover)
    coefs_1, diagonal_1 = coefficients(coarse_perm, with_faces(coarse_perm, first[2]), scaling)
    values_1 = OMEGA * right_1 / diagonal_1
    for sweep_no in range(SWEEPS - 1):
        faces = pick(exchange(values_1[None], per_side), 0)
        values_1 = smooth(values_1, right_1, coefs_1, diagonal_1, scaling, with_faces(values_1, faces))
    stored_faces_1 = pick(exchange(values_1[None], per_side), 0)
    leftover_1 = right_1 - operate(values_1, with_faces(values_1, stored_faces_1), coefs_1, scaling)
    stored_1 = values_1

    gathered = gather_rows(jnp.stack([coarsen(coarse_perm), coarsen(leftover_1)]), per_side)
    correction_all = global_cycle(gathered[:, 1], gathered[:, 0], 2, per_side)

    correction = lax.dynamic_index_in_dim(correction_all, my_row, 0, keepdims=False)
    values_1 = stored_1 + refine(correction)
    faces = [
        mine + theirs
        for mine, theirs in zip(stored_faces_1, refined_faces(correction_all, my_row, per_side))
    ]
    values_1 = smooth(values_1, right_1, coefs_1, diagonal_1, scaling, with_faces(values_1, faces))
    for sweep_no in range(SWEEPS - 1):
        faces = pick(exchange(values_1[None], per_side), 0)
        values_1 = smooth(values_1, right_1, coefs_1, diagonal_1, scaling, with_faces(values_1, faces))
    coarse_faces = pick(exchange(values_1[None], per_side), 0)

    values = stored + refine(values_1)
    faces = [mine + refine_face_of(theirs) for mine, theirs in zip(stored_faces, coarse_faces)]
    values = smooth(values, source, face_coefs, diagonal, 1.0, with_faces(values, faces))
    for sweep_no in range(SWEEPS - 1):
        faces = pick(exchange(values[None], per_side), 0)
        values = smooth(values, source, face_coefs, diagonal, 1.0, with_faces(values, faces))
    faces = pick(exchange(values[None], per_side), 0)
    residual = source - operate(values, with_faces(values, faces), face_coefs, 1.0)
    return (values[None], residual[None])


def solution(mesh):
    return jax.shard_map(
        shards,
        mesh=mesh,
        in_specs=(
            P("space", None, None, None),
            P(),
            P("real"),
            P("real"),
            P(("real", "space"), None, None, None),
        ),
        out_specs=(P(("real", "space"), None, None, None), P(("real", "space"), None, None, None)),
        check_vma=False,
    )
```

```python
import jax
import jax.numpy as jnp
from jax import lax
from jax.sharding import PartitionSpec as P

LEVELS = 3
SWEEPS = 2
CSWEEPS = 6


OMEGA = 0.8


def shifted(shard, axis, by):
    peers = lax.axis_size(axis)
    return lax.ppermute(shard, axis, [(i, (i + by) % peers) for i in range(peers)])


def exchange(fields, per_side):
    count_dev = lax.axis_size("space")
    plane_step = per_side * per_side
    if (2 * plane_step) % count_dev == 0:
        both_x = shifted(jnp.concatenate([fields[:, -1:], fields[:, :1]], axis=1), "space", plane_step)
        lower_x, upper_x = both_x[:, :1], both_x[:, 1:]
    else:
        lower_x = shifted(fields[:, -1:], "space", plane_step)
        upper_x = shifted(fields[:, :1], "space", -plane_step)
    lower_y = shifted(fields[:, :, -1:], "space", per_side)
    upper_y = shifted(fields[:, :, :1], "space", -per_side)
    lower_z = shifted(fields[:, :, :, -1:], "space", 1)
    upper_z = shifted(fields[:, :, :, :1], "space", -1)
    return [lower_x, upper_x, lower_y, upper_y, lower_z, upper_z]


def own_faces(values):
    return [values[-1:], values[:1], values[:, -1:], values[:, :1], values[:, :, -1:], values[:, :, :1]]


def exchange_mixed(fields, per_side):
    count_dev = lax.axis_size("space")
    plane_step = per_side * per_side
    outgoing = [own_faces(values) for values in fields]
    shifts = [plane_step, -plane_step, per_side, -per_side, 1, -1]
    flat = [jnp.concatenate([faces[d].reshape(-1) for faces in outgoing]) for d in range(6)]
    received = [None] * 6
    if (2 * plane_step) % count_dev == 0:
        both = shifted(jnp.concatenate([flat[0], flat[1]]), "space", plane_step)
        received[0], received[1] = both[: flat[0].shape[0]], both[flat[0].shape[0] :]
        rest = range(2, 6)
    else:
        rest = range(6)
    for d in rest:
        received[d] = shifted(flat[d], "space", shifts[d])
    result = [[None] * 6 for _ in fields]
    for d in range(6):
        offset = 0
        for number, faces in enumerate(outgoing):
            size = faces[d].size
            result[number][d] = received[d][offset : offset + size].reshape(faces[d].shape)
            offset += size
    return result


def gather_rows(block, per_side):
    count_dev = lax.axis_size("space")
    if count_dev > 16:
        return lax.all_gather(block[None], "space", axis=0, tiled=True)
    my_row = lax.axis_index("space")
    by_offset = jnp.stack([block] + [shifted(block, "space", k) for k in range(1, count_dev)])
    return jnp.take(by_offset, (my_row - jnp.arange(count_dev)) % count_dev, axis=0)


def pick(faces, number):
    return [face[number] for face in faces]


def with_faces(values, faces):
    lower_x, upper_x, lower_y, upper_y, lower_z, upper_z = faces
    return [
        jnp.concatenate([lower_x, values[:-1]], axis=0),
        jnp.concatenate([values[1:], upper_x], axis=0),
        jnp.concatenate([lower_y, values[:, :-1]], axis=1),
        jnp.concatenate([values[:, 1:], upper_y], axis=1),
        jnp.concatenate([lower_z, values[:, :, :-1]], axis=2),
        jnp.concatenate([values[:, :, 1:], upper_z], axis=2),
    ]


def rolled_faces(values, per_side):
    plane_step = per_side * per_side
    return [
        jnp.concatenate([jnp.roll(values[:, -1:], plane_step, axis=0), values[:, :-1]], axis=1),
        jnp.concatenate([values[:, 1:], jnp.roll(values[:, :1], -plane_step, axis=0)], axis=1),
        jnp.concatenate([jnp.roll(values[:, :, -1:], per_side, axis=0), values[:, :, :-1]], axis=2),
        jnp.concatenate([values[:, :, 1:], jnp.roll(values[:, :, :1], -per_side, axis=0)], axis=2),
        jnp.concatenate([jnp.roll(values[:, :, :, -1:], 1, axis=0), values[:, :, :, :-1]], axis=3),
        jnp.concatenate([values[:, :, :, 1:], jnp.roll(values[:, :, :, :1], -1, axis=0)], axis=3),
    ]


def coefficients(permeab, neighbors, scaling):
    face_coefs = [0.5 * (permeab + beside) for beside in neighbors]
    total_sum = face_coefs[0]
    for number in range(1, 6):
        total_sum = total_sum + face_coefs[number]
    return (face_coefs, scaling * total_sum)


def operate(values, neighbors, face_coefs, scaling):
    total_sum = face_coefs[0] * (values - neighbors[0])
    for number in range(1, 6):
        total_sum = total_sum + face_coefs[number] * (values - neighbors[number])
    return scaling * total_sum


def smooth(values, right_side, face_coefs, diagonal, scaling, neighbors):
    return values + OMEGA * (right_side - operate(values, neighbors, face_coefs, scaling)) / diagonal


def pair_mean(size, scale):
    rows = jnp.arange(size)[:, None] // 2
    cols = jnp.arange(size // 2)[None, :]
    return jnp.where(rows == cols, scale, 0.0).astype(jnp.float32)


def plane_mean(size_x, size_y):
    fine = jnp.arange(size_x * size_y)
    coarse_of = (fine // size_y // 2) * (size_y // 2) + (fine % size_y) // 2
    return jnp.where(
        jnp.arange(size_x * size_y // 4)[:, None] == coarse_of[None, :], 0.25, 0.0
    ).astype(jnp.float32)


def coarsen(values):
    size_x, size_y, size_z = values.shape
    along_z = jnp.dot(
        values.reshape(size_x * size_y, size_z),
        pair_mean(size_z, 0.5),
        precision=lax.Precision.HIGHEST,
    )
    both = jnp.dot(plane_mean(size_x, size_y), along_z, precision=lax.Precision.HIGHEST)
    return both.reshape(size_x // 2, size_y // 2, size_z // 2)


def refine(values):
    return jnp.repeat(jnp.repeat(jnp.repeat(values, 2, axis=0), 2, axis=1), 2, axis=2)


def coarsen_all(values):
    count_b, size_x, size_y, size_z = values.shape
    along_z = jnp.dot(
        values.reshape(count_b * size_x * size_y, size_z),
        pair_mean(size_z, 0.5),
        precision=lax.Precision.HIGHEST,
    ).reshape(count_b, size_x * size_y, size_z // 2)
    both = jnp.einsum(
        "pq,bqz->bpz", plane_mean(size_x, size_y), along_z, precision=lax.Precision.HIGHEST
    )
    return both.reshape(count_b, size_x // 2, size_y // 2, size_z // 2)


def refine_all(values):
    return jnp.repeat(jnp.repeat(jnp.repeat(values, 2, axis=1), 2, axis=2), 2, axis=3)


def refine_face(face):
    return jnp.repeat(jnp.repeat(face, 2, axis=0), 2, axis=1)


def refine_face_of(face):
    for axis in range(3):
        if face.shape[axis] != 1:
            face = jnp.repeat(face, 2, axis=axis)
    return face


def refined_faces(coarse_all, my_row, per_side):
    count_b = coarse_all.shape[0]

    def row(offset):
        return lax.dynamic_index_in_dim(coarse_all, (my_row + offset) % count_b, 0, keepdims=False)

    plane_step = per_side * per_side
    return [
        refine_face(row(-plane_step)[-1])[None],
        refine_face(row(plane_step)[0])[None],
        refine_face(row(-per_side)[:, -1])[:, None],
        refine_face(row(per_side)[:, 0])[:, None],
        refine_face(row(-1)[:, :, -1])[:, :, None],
        refine_face(row(1)[:, :, 0])[:, :, None],
    ]


def global_cycle(all_rhs, all_perm, first_level, per_side):
    perms = [all_perm]
    for number in range(LEVELS - first_level):
        perms.append(coarsen_all(perms[-1]))
    coefs = [
        coefficients(
            perms[number], rolled_faces(perms[number], per_side), 0.25 ** (first_level + number)
        )
        for number in range(LEVELS - first_level + 1)
    ]
    right_side = all_rhs
    stored = []
    rights = []
    for number in range(LEVELS - first_level):
        face_coefs, diagonal = coefs[number]
        scaling = 0.25 ** (first_level + number)
        values = OMEGA * right_side / diagonal
        for sweep_no in range(SWEEPS - 1):
            values = smooth(
                values, right_side, face_coefs, diagonal, scaling, rolled_faces(values, per_side)
            )
        leftover = right_side - operate(
            values, rolled_faces(values, per_side), face_coefs, scaling
        )
        stored.append(values)
        rights.append(right_side)
        right_side = coarsen_all(leftover)
    face_coefs, diagonal = coefs[LEVELS - first_level]
    scaling = 0.25**LEVELS
    correction = OMEGA * right_side / diagonal
    for sweep_no in range(CSWEEPS - 1):
        correction = smooth(
            correction, right_side, face_coefs, diagonal, scaling, rolled_faces(correction, per_side)
        )
    for number in reversed(range(LEVELS - first_level)):
        face_coefs, diagonal = coefs[number]
        scaling = 0.25 ** (first_level + number)
        values = stored[number] + refine_all(correction)
        for sweep_no in range(SWEEPS):
            values = smooth(
                values, rights[number], face_coefs, diagonal, scaling, rolled_faces(values, per_side)
            )
        correction = values
    return correction


def shards(perm_class, class_values, well_cells, well_rates, guess):
    count_dev = lax.axis_size("space")
    per_side = 2 + 2 * (count_dev // 64)
    my_row = lax.axis_index("space")
    block_no = (my_row + per_side * per_side + per_side + 1) % count_dev
    block_x = block_no // (per_side * per_side)
    block_y = block_no // per_side % per_side
    block_z = block_no % per_side
    classes = perm_class[0]
    width_x, width_y, width_z = classes.shape
    permeab = jnp.zeros(classes.shape, jnp.float32)
    for number in range(class_values.shape[0]):
        permeab = permeab + jnp.where(classes == number, class_values[number], 0.0)
    row_len = per_side * width_z
    plane = per_side * width_y * row_len
    glob_x = well_cells // plane
    glob_y = well_cells // row_len % (per_side * width_y)
    glob_z = well_cells % row_len
    onehot_x = jnp.where(
        (glob_x - block_x * width_x)[:, None] == jnp.arange(width_x)[None, :],
        well_rates[:, None],
        0.0,
    )
    onehot_y = jnp.where(
        (glob_y - block_y * width_y)[:, None] == jnp.arange(width_y)[None, :], 1.0, 0.0
    ).astype(jnp.float32)
    onehot_z = jnp.where(
        (glob_z - block_z * width_z)[:, None] == jnp.arange(width_z)[None, :], 1.0, 0.0
    ).astype(jnp.float32)
    source = jnp.einsum(
        "wi,wj,wk->ijk", onehot_x, onehot_y, onehot_z, precision=lax.Precision.HIGHEST
    )

    values = guess[0]
    first = exchange(jnp.stack([permeab, values]), per_side)
    face_coefs, diagonal = coefficients(permeab, with_faces(permeab, pick(first, 0)), 1.0)
    values = smooth(values, source, face_coefs, diagonal, 1.0, with_faces(values, pick(first, 1)))
    for sweep_no in range(SWEEPS - 1):
        faces = pick(exchange(values[None], per_side), 0)
        values = smooth(values, source, face_coefs, diagonal, 1.0, with_faces(values, faces))
    stored_faces = pick(exchange(values[None], per_side), 0)
    leftover = source - operate(values, with_faces(values, stored_faces), face_coefs, 1.0)
    stored = values

    gathered = gather_rows(jnp.stack([coarsen(permeab), coarsen(leftover)]), per_side)
    correction_all = global_cycle(gathered[:, 1], gathered[:, 0], 1, per_side)

    correction = lax.dynamic_index_in_dim(correction_all, my_row, 0, keepdims=False)
    values = stored + refine(correction)
    faces = [
        mine + theirs
        for mine, theirs in zip(stored_faces, refined_faces(correction_all, my_row, per_side))
    ]
    values = smooth(values, source, face_coefs, diagonal, 1.0, with_faces(values, faces))
    for sweep_no in range(SWEEPS - 1):
        faces = pick(exchange(values[None], per_side), 0)
        values = smooth(values, source, face_coefs, diagonal, 1.0, with_faces(values, faces))
    faces = pick(exchange(values[None], per_side), 0)
    residual = source - operate(values, with_faces(values, faces), face_coefs, 1.0)
    return (values[None], residual[None])


def solution(mesh):
    return jax.shard_map(
        shards,
        mesh=mesh,
        in_specs=(
            P("space", None, None, None),
            P(),
            P("real"),
            P("real"),
            P(("real", "space"), None, None, None),
        ),
        out_specs=(P(("real", "space"), None, None, None), P(("real", "space"), None, None, None)),
        check_vma=False,
    )
```

```python
import jax
import jax.numpy as jnp
from jax import lax
from jax.sharding import PartitionSpec as P

LEVELS = 3
SWEEPS = 2
CSWEEPS = 6


OMEGA = 0.8


def shifted(shard, axis, by):
    peers = lax.axis_size(axis)
    return lax.ppermute(shard, axis, [(i, (i + by) % peers) for i in range(peers)])


def own_faces(values):
    return [values[-1:], values[:1], values[:, -1:], values[:, :1], values[:, :, -1:], values[:, :, :1]]


def send_faces(flat, shifts):
    count_dev = lax.axis_size("space")
    if count_dev > 16:
        return [shifted(piece, "space", by) for piece, by in zip(flat, shifts)]
    groups = {}
    for number, by in enumerate(shifts):
        groups.setdefault(by % count_dev, []).append(number)
    width = max(sum(flat[n].shape[0] for n in members) for members in groups.values())
    rows = []
    for offset in range(count_dev):
        members = groups.get(offset, [])
        if members:
            piece = jnp.concatenate([flat[n] for n in members])
            rows.append(jnp.pad(piece, (0, width - piece.shape[0])))
        else:
            rows.append(jnp.zeros((width,), jnp.float32))
    by_offset = jnp.stack(rows)
    my_row = lax.axis_index("space")
    lanes = jnp.arange(count_dev)
    chunks = jnp.take(by_offset, (lanes - my_row) % count_dev, axis=0)
    arrived = lax.all_to_all(chunks, "space", 0, 0, tiled=True)
    arrived_by_offset = jnp.take(arrived, (my_row - lanes) % count_dev, axis=0)
    result = [None] * len(flat)
    for offset, members in groups.items():
        start = 0
        for n in members:
            size = flat[n].shape[0]
            result[n] = arrived_by_offset[offset, start : start + size]
            start += size
    return result


def exchange_mixed(fields, per_side):
    plane_step = per_side * per_side
    shifts = [plane_step, -plane_step, per_side, -per_side, 1, -1]
    outgoing = [own_faces(values) for values in fields]
    flat = [jnp.concatenate([faces[d].reshape(-1) for faces in outgoing]) for d in range(6)]
    received = send_faces(flat, shifts)
    result = [[None] * 6 for _ in fields]
    for d in range(6):
        offset = 0
        for number, faces in enumerate(outgoing):
            size = faces[d].size
            result[number][d] = received[d][offset : offset + size].reshape(faces[d].shape)
            offset += size
    return result


def exchange(fields, per_side):
    per_field = exchange_mixed([fields[n] for n in range(fields.shape[0])], per_side)
    return [jnp.stack([faces[d] for faces in per_field]) for d in range(6)]


def gather_rows(block, per_side):
    count_dev = lax.axis_size("space")
    if count_dev > 16:
        return lax.all_gather(block[None], "space", axis=0, tiled=True)
    my_row = lax.axis_index("space")
    by_offset = jnp.stack([block] + [shifted(block, "space", k) for k in range(1, count_dev)])
    return jnp.take(by_offset, (my_row - jnp.arange(count_dev)) % count_dev, axis=0)


def pick(faces, number):
    return [face[number] for face in faces]


def with_faces(values, faces):
    lower_x, upper_x, lower_y, upper_y, lower_z, upper_z = faces
    return [
        jnp.concatenate([lower_x, values[:-1]], axis=0),
        jnp.concatenate([values[1:], upper_x], axis=0),
        jnp.concatenate([lower_y, values[:, :-1]], axis=1),
        jnp.concatenate([values[:, 1:], upper_y], axis=1),
        jnp.concatenate([lower_z, values[:, :, :-1]], axis=2),
        jnp.concatenate([values[:, :, 1:], upper_z], axis=2),
    ]


def rolled_faces(values, per_side):
    plane_step = per_side * per_side
    return [
        jnp.concatenate([jnp.roll(values[:, -1:], plane_step, axis=0), values[:, :-1]], axis=1),
        jnp.concatenate([values[:, 1:], jnp.roll(values[:, :1], -plane_step, axis=0)], axis=1),
        jnp.concatenate([jnp.roll(values[:, :, -1:], per_side, axis=0), values[:, :, :-1]], axis=2),
        jnp.concatenate([values[:, :, 1:], jnp.roll(values[:, :, :1], -per_side, axis=0)], axis=2),
        jnp.concatenate([jnp.roll(values[:, :, :, -1:], 1, axis=0), values[:, :, :, :-1]], axis=3),
        jnp.concatenate([values[:, :, :, 1:], jnp.roll(values[:, :, :, :1], -1, axis=0)], axis=3),
    ]


def coefficients(permeab, neighbors, scaling):
    face_coefs = [0.5 * (permeab + beside) for beside in neighbors]
    total_sum = face_coefs[0]
    for number in range(1, 6):
        total_sum = total_sum + face_coefs[number]
    return (face_coefs, scaling * total_sum)


def operate(values, neighbors, face_coefs, scaling):
    total_sum = face_coefs[0] * (values - neighbors[0])
    for number in range(1, 6):
        total_sum = total_sum + face_coefs[number] * (values - neighbors[number])
    return scaling * total_sum


def smooth(values, right_side, face_coefs, diagonal, scaling, neighbors):
    return values + OMEGA * (right_side - operate(values, neighbors, face_coefs, scaling)) / diagonal


def pair_mean(size, scale):
    rows = jnp.arange(size)[:, None] // 2
    cols = jnp.arange(size // 2)[None, :]
    return jnp.where(rows == cols, scale, 0.0).astype(jnp.float32)


def plane_mean(size_x, size_y):
    fine = jnp.arange(size_x * size_y)
    coarse_of = (fine // size_y // 2) * (size_y // 2) + (fine % size_y) // 2
    return jnp.where(
        jnp.arange(size_x * size_y // 4)[:, None] == coarse_of[None, :], 0.25, 0.0
    ).astype(jnp.float32)


def coarsen(values):
    size_x, size_y, size_z = values.shape
    along_z = jnp.dot(
        values.reshape(size_x * size_y, size_z),
        pair_mean(size_z, 0.5),
        precision=lax.Precision.HIGHEST,
    )
    both = jnp.dot(plane_mean(size_x, size_y), along_z, precision=lax.Precision.HIGHEST)
    return both.reshape(size_x // 2, size_y // 2, size_z // 2)


def refine(values):
    return jnp.repeat(jnp.repeat(jnp.repeat(values, 2, axis=0), 2, axis=1), 2, axis=2)


def coarsen_all(values):
    count_b, size_x, size_y, size_z = values.shape
    along_z = jnp.dot(
        values.reshape(count_b * size_x * size_y, size_z),
        pair_mean(size_z, 0.5),
        precision=lax.Precision.HIGHEST,
    ).reshape(count_b, size_x * size_y, size_z // 2)
    both = jnp.einsum(
        "pq,bqz->bpz", plane_mean(size_x, size_y), along_z, precision=lax.Precision.HIGHEST
    )
    return both.reshape(count_b, size_x // 2, size_y // 2, size_z // 2)


def refine_all(values):
    return jnp.repeat(jnp.repeat(jnp.repeat(values, 2, axis=1), 2, axis=2), 2, axis=3)


def refine_face(face):
    return jnp.repeat(jnp.repeat(face, 2, axis=0), 2, axis=1)


def refine_face_of(face):
    for axis in range(3):
        if face.shape[axis] != 1:
            face = jnp.repeat(face, 2, axis=axis)
    return face


def refined_faces(coarse_all, my_row, per_side):
    count_b = coarse_all.shape[0]

    def row(offset):
        return lax.dynamic_index_in_dim(coarse_all, (my_row + offset) % count_b, 0, keepdims=False)

    plane_step = per_side * per_side
    return [
        refine_face(row(-plane_step)[-1])[None],
        refine_face(row(plane_step)[0])[None],
        refine_face(row(-per_side)[:, -1])[:, None],
        refine_face(row(per_side)[:, 0])[:, None],
        refine_face(row(-1)[:, :, -1])[:, :, None],
        refine_face(row(1)[:, :, 0])[:, :, None],
    ]


def global_cycle(all_rhs, all_perm, first_level, per_side):
    perms = [all_perm]
    for number in range(LEVELS - first_level):
        perms.append(coarsen_all(perms[-1]))
    coefs = [
        coefficients(
            perms[number], rolled_faces(perms[number], per_side), 0.25 ** (first_level + number)
        )
        for number in range(LEVELS - first_level + 1)
    ]
    right_side = all_rhs
    stored = []
    rights = []
    for number in range(LEVELS - first_level):
        face_coefs, diagonal = coefs[number]
        scaling = 0.25 ** (first_level + number)
        values = OMEGA * right_side / diagonal
        for sweep_no in range(SWEEPS - 1):
            values = smooth(
                values, right_side, face_coefs, diagonal, scaling, rolled_faces(values, per_side)
            )
        leftover = right_side - operate(
            values, rolled_faces(values, per_side), face_coefs, scaling
        )
        stored.append(values)
        rights.append(right_side)
        right_side = coarsen_all(leftover)
    face_coefs, diagonal = coefs[LEVELS - first_level]
    scaling = 0.25**LEVELS
    correction = OMEGA * right_side / diagonal
    for sweep_no in range(CSWEEPS - 1):
        correction = smooth(
            correction, right_side, face_coefs, diagonal, scaling, rolled_faces(correction, per_side)
        )
    for number in reversed(range(LEVELS - first_level)):
        face_coefs, diagonal = coefs[number]
        scaling = 0.25 ** (first_level + number)
        values = stored[number] + refine_all(correction)
        for sweep_no in range(SWEEPS):
            values = smooth(
                values, rights[number], face_coefs, diagonal, scaling, rolled_faces(values, per_side)
            )
        correction = values
    return correction


def shards(perm_class, class_values, well_cells, well_rates, guess):
    count_dev = lax.axis_size("space")
    per_side = 2 + 2 * (count_dev // 64)
    my_row = lax.axis_index("space")
    block_no = (my_row + per_side * per_side + per_side + 1) % count_dev
    block_x = block_no // (per_side * per_side)
    block_y = block_no // per_side % per_side
    block_z = block_no % per_side
    classes = perm_class[0]
    width_x, width_y, width_z = classes.shape
    permeab = jnp.zeros(classes.shape, jnp.float32)
    for number in range(class_values.shape[0]):
        permeab = permeab + jnp.where(classes == number, class_values[number], 0.0)
    row_len = per_side * width_z
    plane = per_side * width_y * row_len
    glob_x = well_cells // plane
    glob_y = well_cells // row_len % (per_side * width_y)
    glob_z = well_cells % row_len
    onehot_x = jnp.where(
        (glob_x - block_x * width_x)[:, None] == jnp.arange(width_x)[None, :],
        well_rates[:, None],
        0.0,
    )
    onehot_y = jnp.where(
        (glob_y - block_y * width_y)[:, None] == jnp.arange(width_y)[None, :], 1.0, 0.0
    ).astype(jnp.float32)
    onehot_z = jnp.where(
        (glob_z - block_z * width_z)[:, None] == jnp.arange(width_z)[None, :], 1.0, 0.0
    ).astype(jnp.float32)
    source = jnp.einsum(
        "wi,wj,wk->ijk", onehot_x, onehot_y, onehot_z, precision=lax.Precision.HIGHEST
    )

    values = guess[0]
    coarse_perm = coarsen(permeab)
    first = exchange_mixed([permeab, values, coarse_perm], per_side)
    face_coefs, diagonal = coefficients(permeab, with_faces(permeab, first[0]), 1.0)
    values = smooth(values, source, face_coefs, diagonal, 1.0, with_faces(values, first[1]))
    for sweep_no in range(SWEEPS - 1):
        faces = pick(exchange(values[None], per_side), 0)
        values = smooth(values, source, face_coefs, diagonal, 1.0, with_faces(values, faces))
    stored_faces = pick(exchange(values[None], per_side), 0)
    leftover = source - operate(values, with_faces(values, stored_faces), face_coefs, 1.0)
    stored = values

    scaling = 0.25
    right_1 = coarsen(leftover)
    coefs_1, diagonal_1 = coefficients(coarse_perm, with_faces(coarse_perm, first[2]), scaling)
    values_1 = OMEGA * right_1 / diagonal_1
    for sweep_no in range(SWEEPS - 1):
        faces = pick(exchange(values_1[None], per_side), 0)
        values_1 = smooth(values_1, right_1, coefs_1, diagonal_1, scaling, with_faces(values_1, faces))
    stored_faces_1 = pick(exchange(values_1[None], per_side), 0)
    leftover_1 = right_1 - operate(values_1, with_faces(values_1, stored_faces_1), coefs_1, scaling)
    stored_1 = values_1

    gathered = gather_rows(jnp.stack([coarsen(coarse_perm), coarsen(leftover_1)]), per_side)
    correction_all = global_cycle(gathered[:, 1], gathered[:, 0], 2, per_side)

    correction = lax.dynamic_index_in_dim(correction_all, my_row, 0, keepdims=False)
    values_1 = stored_1 + refine(correction)
    faces = [
        mine + theirs
        for mine, theirs in zip(stored_faces_1, refined_faces(correction_all, my_row, per_side))
    ]
    values_1 = smooth(values_1, right_1, coefs_1, diagonal_1, scaling, with_faces(values_1, faces))
    for sweep_no in range(SWEEPS - 1):
        faces = pick(exchange(values_1[None], per_side), 0)
        values_1 = smooth(values_1, right_1, coefs_1, diagonal_1, scaling, with_faces(values_1, faces))
    coarse_faces = pick(exchange(values_1[None], per_side), 0)

    values = stored + refine(values_1)
    faces = [mine + refine_face_of(theirs) for mine, theirs in zip(stored_faces, coarse_faces)]
    values = smooth(values, source, face_coefs, diagonal, 1.0, with_faces(values, faces))
    for sweep_no in range(SWEEPS - 1):
        faces = pick(exchange(values[None], per_side), 0)
        values = smooth(values, source, face_coefs, diagonal, 1.0, with_faces(values, faces))
    faces = pick(exchange(values[None], per_side), 0)
    residual = source - operate(values, with_faces(values, faces), face_coefs, 1.0)
    return (values[None], residual[None])


def solution(mesh):
    return jax.shard_map(
        shards,
        mesh=mesh,
        in_specs=(
            P("space", None, None, None),
            P(),
            P("real"),
            P("real"),
            P(("real", "space"), None, None, None),
        ),
        out_specs=(P(("real", "space"), None, None, None), P(("real", "space"), None, None, None)),
        check_vma=False,
    )
```

```python
import jax
import jax.numpy as jnp
from jax import lax
from jax.sharding import PartitionSpec as P

LEVELS = 3
SWEEPS = 2
CSWEEPS = 6


OMEGA = 0.8


def shifted(shard, axis, by):
    peers = lax.axis_size(axis)
    return lax.ppermute(shard, axis, [(i, (i + by) % peers) for i in range(peers)])


def exchange(fields, per_side):
    count_dev = lax.axis_size("space")
    plane_step = per_side * per_side
    if (2 * plane_step) % count_dev == 0:
        both_x = shifted(jnp.concatenate([fields[:, -1:], fields[:, :1]], axis=1), "space", plane_step)
        lower_x, upper_x = both_x[:, :1], both_x[:, 1:]
    else:
        lower_x = shifted(fields[:, -1:], "space", plane_step)
        upper_x = shifted(fields[:, :1], "space", -plane_step)
    lower_y = shifted(fields[:, :, -1:], "space", per_side)
    upper_y = shifted(fields[:, :, :1], "space", -per_side)
    lower_z = shifted(fields[:, :, :, -1:], "space", 1)
    upper_z = shifted(fields[:, :, :, :1], "space", -1)
    return [lower_x, upper_x, lower_y, upper_y, lower_z, upper_z]


def own_faces(values):
    return [values[-1:], values[:1], values[:, -1:], values[:, :1], values[:, :, -1:], values[:, :, :1]]


def exchange_mixed(fields, per_side):
    count_dev = lax.axis_size("space")
    plane_step = per_side * per_side
    outgoing = [own_faces(values) for values in fields]
    shifts = [plane_step, -plane_step, per_side, -per_side, 1, -1]
    flat = [jnp.concatenate([faces[d].reshape(-1) for faces in outgoing]) for d in range(6)]
    received = [None] * 6
    if (2 * plane_step) % count_dev == 0:
        both = shifted(jnp.concatenate([flat[0], flat[1]]), "space", plane_step)
        received[0], received[1] = both[: flat[0].shape[0]], both[flat[0].shape[0] :]
        rest = range(2, 6)
    else:
        rest = range(6)
    for d in rest:
        received[d] = shifted(flat[d], "space", shifts[d])
    result = [[None] * 6 for _ in fields]
    for d in range(6):
        offset = 0
        for number, faces in enumerate(outgoing):
            size = faces[d].size
            result[number][d] = received[d][offset : offset + size].reshape(faces[d].shape)
            offset += size
    return result


def gather_rows(block, per_side):
    count_dev = lax.axis_size("space")
    if count_dev > 16:
        return lax.all_gather(block[None], "space", axis=0, tiled=True)
    my_row = lax.axis_index("space")
    by_offset = jnp.stack([block] + [shifted(block, "space", k) for k in range(1, count_dev)])
    return jnp.take(by_offset, (my_row - jnp.arange(count_dev)) % count_dev, axis=0)


def pick(faces, number):
    return [face[number] for face in faces]


def with_faces(values, faces):
    lower_x, upper_x, lower_y, upper_y, lower_z, upper_z = faces
    return [
        jnp.concatenate([lower_x, values[:-1]], axis=0),
        jnp.concatenate([values[1:], upper_x], axis=0),
        jnp.concatenate([lower_y, values[:, :-1]], axis=1),
        jnp.concatenate([values[:, 1:], upper_y], axis=1),
        jnp.concatenate([lower_z, values[:, :, :-1]], axis=2),
        jnp.concatenate([values[:, :, 1:], upper_z], axis=2),
    ]


def rolled_faces(values, per_side):
    plane_step = per_side * per_side
    return [
        jnp.concatenate([jnp.roll(values[:, -1:], plane_step, axis=0), values[:, :-1]], axis=1),
        jnp.concatenate([values[:, 1:], jnp.roll(values[:, :1], -plane_step, axis=0)], axis=1),
        jnp.concatenate([jnp.roll(values[:, :, -1:], per_side, axis=0), values[:, :, :-1]], axis=2),
        jnp.concatenate([values[:, :, 1:], jnp.roll(values[:, :, :1], -per_side, axis=0)], axis=2),
        jnp.concatenate([jnp.roll(values[:, :, :, -1:], 1, axis=0), values[:, :, :, :-1]], axis=3),
        jnp.concatenate([values[:, :, :, 1:], jnp.roll(values[:, :, :, :1], -1, axis=0)], axis=3),
    ]


def coefficients(permeab, neighbors, scaling):
    face_coefs = [0.5 * (permeab + beside) for beside in neighbors]
    total_sum = face_coefs[0]
    for number in range(1, 6):
        total_sum = total_sum + face_coefs[number]
    return (face_coefs, scaling * total_sum)


def operate(values, neighbors, face_coefs, scaling):
    total_sum = face_coefs[0] * (values - neighbors[0])
    for number in range(1, 6):
        total_sum = total_sum + face_coefs[number] * (values - neighbors[number])
    return scaling * total_sum


def smooth(values, right_side, face_coefs, diagonal, scaling, neighbors):
    return values + OMEGA * (right_side - operate(values, neighbors, face_coefs, scaling)) / diagonal


def pair_mean(size, scale):
    rows = jnp.arange(size)[:, None] // 2
    cols = jnp.arange(size // 2)[None, :]
    return jnp.where(rows == cols, scale, 0.0).astype(jnp.float32)


def plane_mean(size_x, size_y):
    fine = jnp.arange(size_x * size_y)
    coarse_of = (fine // size_y // 2) * (size_y // 2) + (fine % size_y) // 2
    return jnp.where(
        jnp.arange(size_x * size_y // 4)[:, None] == coarse_of[None, :], 0.25, 0.0
    ).astype(jnp.float32)


def coarsen(values):
    size_x, size_y, size_z = values.shape
    along_z = jnp.dot(
        values.reshape(size_x * size_y, size_z),
        pair_mean(size_z, 0.5),
        precision=lax.Precision.HIGHEST,
    )
    both = jnp.dot(plane_mean(size_x, size_y), along_z, precision=lax.Precision.HIGHEST)
    return both.reshape(size_x // 2, size_y // 2, size_z // 2)


def refine(values):
    return jnp.repeat(jnp.repeat(jnp.repeat(values, 2, axis=0), 2, axis=1), 2, axis=2)


def coarsen_all(values):
    count_b, size_x, size_y, size_z = values.shape
    along_z = jnp.dot(
        values.reshape(count_b * size_x * size_y, size_z),
        pair_mean(size_z, 0.5),
        precision=lax.Precision.HIGHEST,
    ).reshape(count_b, size_x * size_y, size_z // 2)
    both = jnp.einsum(
        "pq,bqz->bpz", plane_mean(size_x, size_y), along_z, precision=lax.Precision.HIGHEST
    )
    return both.reshape(count_b, size_x // 2, size_y // 2, size_z // 2)


def refine_all(values):
    return jnp.repeat(jnp.repeat(jnp.repeat(values, 2, axis=1), 2, axis=2), 2, axis=3)


def refine_face(face):
    return jnp.repeat(jnp.repeat(face, 2, axis=0), 2, axis=1)


def refine_face_of(face):
    for axis in range(3):
        if face.shape[axis] != 1:
            face = jnp.repeat(face, 2, axis=axis)
    return face


def refined_faces(coarse_all, my_row, per_side):
    count_b = coarse_all.shape[0]

    def row(offset):
        return lax.dynamic_index_in_dim(coarse_all, (my_row + offset) % count_b, 0, keepdims=False)

    plane_step = per_side * per_side
    return [
        refine_face(row(-plane_step)[-1])[None],
        refine_face(row(plane_step)[0])[None],
        refine_face(row(-per_side)[:, -1])[:, None],
        refine_face(row(per_side)[:, 0])[:, None],
        refine_face(row(-1)[:, :, -1])[:, :, None],
        refine_face(row(1)[:, :, 0])[:, :, None],
    ]


def neighbour_rows(count_b, size_x, size_y, per_side):
    count_r = count_b * size_x * size_y
    index = jnp.arange(count_r)
    row = index // (size_x * size_y)
    at_x = index // size_y % size_x
    at_y = index % size_y
    plane_step = per_side * per_side
    picks = []
    for axis_no, (size, step) in enumerate(((size_x, plane_step), (size_y, per_side))):
        coord = at_x if axis_no == 0 else at_y
        for sign in (-1, 1):
            edge = size - 1 if sign > 0 else 0
            moved = jnp.where(coord == edge, size - 1 - edge, coord + sign)
            new_row = jnp.where(coord == edge, (row + sign * step) % count_b, row)
            if axis_no == 0:
                picks.append((new_row * size_x + moved) * size_y + at_y)
            else:
                picks.append((new_row * size_x + at_x) * size_y + moved)
    for sign in (-1, 1):
        picks.append((((row + sign) % count_b) * size_x + at_x) * size_y + at_y)
    target = jnp.concatenate(picks)
    return jnp.where(target[:, None] == index[None, :], 1.0, 0.0).astype(jnp.float32)


def lane_shift(size_z, sign):
    lanes_in = jnp.arange(size_z)[:, None]
    lanes_out = jnp.arange(size_z)[None, :]
    inner = jnp.where(lanes_in == lanes_out + sign, 1.0, 0.0)
    edge_in, edge_out = (size_z - 1, 0) if sign < 0 else (0, size_z - 1)
    wrap = jnp.where((lanes_in == edge_in) & (lanes_out == edge_out), 1.0, 0.0)
    return jnp.concatenate([inner, wrap]).astype(jnp.float32)


def flat_faces(values, picker, lower_z, upper_z):
    count_r = values.shape[0]
    rows = jnp.dot(picker, values, precision=lax.Precision.HIGHEST)
    lower = jnp.dot(
        jnp.concatenate([values, rows[4 * count_r : 5 * count_r]], axis=1),
        lower_z,
        precision=lax.Precision.HIGHEST,
    )
    upper = jnp.dot(
        jnp.concatenate([values, rows[5 * count_r :]], axis=1),
        upper_z,
        precision=lax.Precision.HIGHEST,
    )
    return [rows[k * count_r : (k + 1) * count_r] for k in range(4)] + [lower, upper]


def row_mean(count_b, size_x, size_y):
    index = jnp.arange(count_b * size_x * size_y)
    row = index // (size_x * size_y)
    coarse_of = (row * (size_x // 2) + index // size_y % size_x // 2) * (size_y // 2) + index % size_y // 2
    return jnp.where(
        jnp.arange(count_b * size_x * size_y // 4)[:, None] == coarse_of[None, :], 0.25, 0.0
    ).astype(jnp.float32)


def global_cycle(all_rhs, all_perm, first_level, per_side):
    count_b, size_x, size_y, size_z = all_rhs.shape
    shapes = [(size_x >> n, size_y >> n, size_z >> n) for n in range(LEVELS - first_level + 1)]
    pickers = [neighbour_rows(count_b, sx, sy, per_side) for sx, sy, sz in shapes]
    shifts = [(lane_shift(sz, -1), lane_shift(sz, 1)) for sx, sy, sz in shapes]
    means = [(row_mean(count_b, sx, sy), pair_mean(sz, 0.5)) for sx, sy, sz in shapes[:-1]]

    def faces(values, number):
        return flat_faces(values, pickers[number], *shifts[number])

    def down(values, number):
        rows, lanes = means[number]
        return jnp.dot(
            rows,
            jnp.dot(values, lanes, precision=lax.Precision.HIGHEST),
            precision=lax.Precision.HIGHEST,
        )

    def up(values, number):
        rows, lanes = means[number]
        return jnp.dot(
            rows.T * 4.0,
            jnp.dot(values, lanes.T * 2.0, precision=lax.Precision.HIGHEST),
            precision=lax.Precision.HIGHEST,
        )

    perms = [all_perm.reshape(-1, size_z)]
    for number in range(LEVELS - first_level):
        perms.append(down(perms[-1], number))
    coefs = [
        coefficients(perms[number], faces(perms[number], number), 0.25 ** (first_level + number))
        for number in range(LEVELS - first_level + 1)
    ]
    right_side = all_rhs.reshape(-1, size_z)
    stored = []
    rights = []
    for number in range(LEVELS - first_level):
        face_coefs, diagonal = coefs[number]
        scaling = 0.25 ** (first_level + number)
        values = OMEGA * right_side / diagonal
        for sweep_no in range(SWEEPS - 1):
            values = smooth(values, right_side, face_coefs, diagonal, scaling, faces(values, number))
        leftover = right_side - operate(values, faces(values, number), face_coefs, scaling)
        stored.append(values)
        rights.append(right_side)
        right_side = down(leftover, number)
    last = LEVELS - first_level
    face_coefs, diagonal = coefs[last]
    scaling = 0.25**LEVELS
    correction = OMEGA * right_side / diagonal
    for sweep_no in range(CSWEEPS - 1):
        correction = smooth(
            correction, right_side, face_coefs, diagonal, scaling, faces(correction, last)
        )
    for number in reversed(range(LEVELS - first_level)):
        face_coefs, diagonal = coefs[number]
        scaling = 0.25 ** (first_level + number)
        values = stored[number] + up(correction, number)
        for sweep_no in range(SWEEPS):
            values = smooth(
                values, rights[number], face_coefs, diagonal, scaling, faces(values, number)
            )
        correction = values
    return correction.reshape(count_b, size_x, size_y, size_z)


def shards(perm_class, class_values, well_cells, well_rates, guess):
    count_dev = lax.axis_size("space")
    per_side = 2 + 2 * (count_dev // 64)
    my_row = lax.axis_index("space")
    block_no = (my_row + per_side * per_side + per_side + 1) % count_dev
    block_x = block_no // (per_side * per_side)
    block_y = block_no // per_side % per_side
    block_z = block_no % per_side
    classes = perm_class[0]
    width_x, width_y, width_z = classes.shape
    permeab = jnp.zeros(classes.shape, jnp.float32)
    for number in range(class_values.shape[0]):
        permeab = permeab + jnp.where(classes == number, class_values[number], 0.0)
    row_len = per_side * width_z
    plane = per_side * width_y * row_len
    glob_x = well_cells // plane
    glob_y = well_cells // row_len % (per_side * width_y)
    glob_z = well_cells % row_len
    onehot_x = jnp.where(
        (glob_x - block_x * width_x)[:, None] == jnp.arange(width_x)[None, :],
        well_rates[:, None],
        0.0,
    )
    onehot_y = jnp.where(
        (glob_y - block_y * width_y)[:, None] == jnp.arange(width_y)[None, :], 1.0, 0.0
    ).astype(jnp.float32)
    onehot_z = jnp.where(
        (glob_z - block_z * width_z)[:, None] == jnp.arange(width_z)[None, :], 1.0, 0.0
    ).astype(jnp.float32)
    source = jnp.einsum(
        "wi,wj,wk->ijk", onehot_x, onehot_y, onehot_z, precision=lax.Precision.HIGHEST
    )

    values = guess[0]
    coarse_perm = coarsen(permeab)
    first = exchange_mixed([permeab, values, coarse_perm], per_side)
    face_coefs, diagonal = coefficients(permeab, with_faces(permeab, first[0]), 1.0)
    values = smooth(values, source, face_coefs, diagonal, 1.0, with_faces(values, first[1]))
    for sweep_no in range(SWEEPS - 1):
        faces = pick(exchange(values[None], per_side), 0)
        values = smooth(values, source, face_coefs, diagonal, 1.0, with_faces(values, faces))
    stored_faces = pick(exchange(values[None], per_side), 0)
    leftover = source - operate(values, with_faces(values, stored_faces), face_coefs, 1.0)
    stored = values

    scaling = 0.25
    right_1 = coarsen(leftover)
    coefs_1, diagonal_1 = coefficients(coarse_perm, with_faces(coarse_perm, first[2]), scaling)
    values_1 = OMEGA * right_1 / diagonal_1
    for sweep_no in range(SWEEPS - 1):
        faces = pick(exchange(values_1[None], per_side), 0)
        values_1 = smooth(values_1, right_1, coefs_1, diagonal_1, scaling, with_faces(values_1, faces))
    stored_faces_1 = pick(exchange(values_1[None], per_side), 0)
    leftover_1 = right_1 - operate(values_1, with_faces(values_1, stored_faces_1), coefs_1, scaling)
    stored_1 = values_1

    gathered = gather_rows(jnp.stack([coarsen(coarse_perm), coarsen(leftover_1)]), per_side)
    correction_all = global_cycle(gathered[:, 1], gathered[:, 0], 2, per_side)

    correction = lax.dynamic_index_in_dim(correction_all, my_row, 0, keepdims=False)
    values_1 = stored_1 + refine(correction)
    faces = [
        mine + theirs
        for mine, theirs in zip(stored_faces_1, refined_faces(correction_all, my_row, per_side))
    ]
    values_1 = smooth(values_1, right_1, coefs_1, diagonal_1, scaling, with_faces(values_1, faces))
    for sweep_no in range(SWEEPS - 1):
        faces = pick(exchange(values_1[None], per_side), 0)
        values_1 = smooth(values_1, right_1, coefs_1, diagonal_1, scaling, with_faces(values_1, faces))
    coarse_faces = pick(exchange(values_1[None], per_side), 0)

    values = stored + refine(values_1)
    faces = [mine + refine_face_of(theirs) for mine, theirs in zip(stored_faces, coarse_faces)]
    values = smooth(values, source, face_coefs, diagonal, 1.0, with_faces(values, faces))
    for sweep_no in range(SWEEPS - 1):
        faces = pick(exchange(values[None], per_side), 0)
        values = smooth(values, source, face_coefs, diagonal, 1.0, with_faces(values, faces))
    faces = pick(exchange(values[None], per_side), 0)
    residual = source - operate(values, with_faces(values, faces), face_coefs, 1.0)
    return (values[None], residual[None])


def solution(mesh):
    return jax.shard_map(
        shards,
        mesh=mesh,
        in_specs=(
            P("space", None, None, None),
            P(),
            P("real"),
            P("real"),
            P(("real", "space"), None, None, None),
        ),
        out_specs=(P(("real", "space"), None, None, None), P(("real", "space"), None, None, None)),
        check_vma=False,
    )
```

```python
import jax
import jax.numpy as jnp
from jax import lax
from jax.sharding import PartitionSpec as P

LEVELS = 3
SWEEPS = 2
CSWEEPS = 6


OMEGA = 0.8


def shifted(shard, axis, by):
    peers = lax.axis_size(axis)
    return lax.ppermute(shard, axis, [(i, (i + by) % peers) for i in range(peers)])


def exchange(fields, per_side):
    count_dev = lax.axis_size("space")
    plane_step = per_side * per_side
    if (2 * plane_step) % count_dev == 0:
        both_x = shifted(jnp.concatenate([fields[:, -1:], fields[:, :1]], axis=1), "space", plane_step)
        lower_x, upper_x = both_x[:, :1], both_x[:, 1:]
    else:
        lower_x = shifted(fields[:, -1:], "space", plane_step)
        upper_x = shifted(fields[:, :1], "space", -plane_step)
    lower_y = shifted(fields[:, :, -1:], "space", per_side)
    upper_y = shifted(fields[:, :, :1], "space", -per_side)
    lower_z = shifted(fields[:, :, :, -1:], "space", 1)
    upper_z = shifted(fields[:, :, :, :1], "space", -1)
    return [lower_x, upper_x, lower_y, upper_y, lower_z, upper_z]


def own_faces(values):
    return [values[-1:], values[:1], values[:, -1:], values[:, :1], values[:, :, -1:], values[:, :, :1]]


def exchange_mixed(fields, per_side):
    count_dev = lax.axis_size("space")
    plane_step = per_side * per_side
    outgoing = [own_faces(values) for values in fields]
    shifts = [plane_step, -plane_step, per_side, -per_side, 1, -1]
    flat = [jnp.concatenate([faces[d].reshape(-1) for faces in outgoing]) for d in range(6)]
    received = [None] * 6
    if (2 * plane_step) % count_dev == 0:
        both = shifted(jnp.concatenate([flat[0], flat[1]]), "space", plane_step)
        received[0], received[1] = both[: flat[0].shape[0]], both[flat[0].shape[0] :]
        rest = range(2, 6)
    else:
        rest = range(6)
    for d in rest:
        received[d] = shifted(flat[d], "space", shifts[d])
    result = [[None] * 6 for _ in fields]
    for d in range(6):
        offset = 0
        for number, faces in enumerate(outgoing):
            size = faces[d].size
            result[number][d] = received[d][offset : offset + size].reshape(faces[d].shape)
            offset += size
    return result


def exchange_with_coarse(fields, coarse, per_side):
    count_dev = lax.axis_size("space")
    plane_step = per_side * per_side
    size_x, size_y, size_z = fields.shape[1:]
    half_x, half_y, half_z = coarse.shape

    def padded(face):
        pads = [(0, full - part) if part != 1 else (0, 0) for full, part in zip((size_x, size_y, size_z), face.shape)]
        return jnp.pad(face, pads)[None]

    def message(number):
        pieces = [fields[:, -1:], fields[:, :1], fields[:, :, -1:], fields[:, :, :1], fields[:, :, :, -1:], fields[:, :, :, :1]]
        return jnp.concatenate([pieces[number], padded(own_faces(coarse)[number])], axis=0)

    shifts = [plane_step, -plane_step, per_side, -per_side, 1, -1]
    received = [None] * 6
    if (2 * plane_step) % count_dev == 0:
        both = shifted(jnp.concatenate([message(0), message(1)], axis=1), "space", plane_step)
        received[0], received[1] = both[:, :1], both[:, 1:]
        rest = range(2, 6)
    else:
        rest = range(6)
    for number in rest:
        received[number] = shifted(message(number), "space", shifts[number])
    count = fields.shape[0]
    field_faces = [face[:count] for face in received]
    coarse_faces = []
    for number, face in enumerate(received):
        shape = own_faces(coarse)[number].shape
        coarse_faces.append(face[count, : shape[0], : shape[1], : shape[2]])
    return field_faces, coarse_faces


def gather_rows(block, per_side):
    count_dev = lax.axis_size("space")
    if count_dev > 16:
        return lax.all_gather(block[None], "space", axis=0, tiled=True)
    my_row = lax.axis_index("space")
    by_offset = jnp.stack([block] + [shifted(block, "space", k) for k in range(1, count_dev)])
    return jnp.take(by_offset, (my_row - jnp.arange(count_dev)) % count_dev, axis=0)


def pick(faces, number):
    return [face[number] for face in faces]


def with_faces(values, faces):
    lower_x, upper_x, lower_y, upper_y, lower_z, upper_z = faces
    return [
        jnp.concatenate([lower_x, values[:-1]], axis=0),
        jnp.concatenate([values[1:], upper_x], axis=0),
        jnp.concatenate([lower_y, values[:, :-1]], axis=1),
        jnp.concatenate([values[:, 1:], upper_y], axis=1),
        jnp.concatenate([lower_z, values[:, :, :-1]], axis=2),
        jnp.concatenate([values[:, :, 1:], upper_z], axis=2),
    ]


def rolled_faces(values, per_side):
    plane_step = per_side * per_side
    return [
        jnp.concatenate([jnp.roll(values[:, -1:], plane_step, axis=0), values[:, :-1]], axis=1),
        jnp.concatenate([values[:, 1:], jnp.roll(values[:, :1], -plane_step, axis=0)], axis=1),
        jnp.concatenate([jnp.roll(values[:, :, -1:], per_side, axis=0), values[:, :, :-1]], axis=2),
        jnp.concatenate([values[:, :, 1:], jnp.roll(values[:, :, :1], -per_side, axis=0)], axis=2),
        jnp.concatenate([jnp.roll(values[:, :, :, -1:], 1, axis=0), values[:, :, :, :-1]], axis=3),
        jnp.concatenate([values[:, :, :, 1:], jnp.roll(values[:, :, :, :1], -1, axis=0)], axis=3),
    ]


def coefficients(permeab, neighbors, scaling):
    face_coefs = [0.5 * (permeab + beside) for beside in neighbors]
    total_sum = face_coefs[0]
    for number in range(1, 6):
        total_sum = total_sum + face_coefs[number]
    return (face_coefs, scaling * total_sum)


def operate(values, neighbors, face_coefs, scaling):
    total_sum = face_coefs[0] * (values - neighbors[0])
    for number in range(1, 6):
        total_sum = total_sum + face_coefs[number] * (values - neighbors[number])
    return scaling * total_sum


def smooth(values, right_side, face_coefs, diagonal, scaling, neighbors):
    return values + OMEGA * (right_side - operate(values, neighbors, face_coefs, scaling)) / diagonal


def pair_mean(size, scale):
    rows = jnp.arange(size)[:, None] // 2
    cols = jnp.arange(size // 2)[None, :]
    return jnp.where(rows == cols, scale, 0.0).astype(jnp.float32)


def plane_mean(size_x, size_y):
    fine = jnp.arange(size_x * size_y)
    coarse_of = (fine // size_y // 2) * (size_y // 2) + (fine % size_y) // 2
    return jnp.where(
        jnp.arange(size_x * size_y // 4)[:, None] == coarse_of[None, :], 0.25, 0.0
    ).astype(jnp.float32)


def coarsen(values):
    size_x, size_y, size_z = values.shape
    along_z = jnp.dot(
        values.reshape(size_x * size_y, size_z),
        pair_mean(size_z, 0.5),
        precision=lax.Precision.HIGHEST,
    )
    both = jnp.dot(plane_mean(size_x, size_y), along_z, precision=lax.Precision.HIGHEST)
    return both.reshape(size_x // 2, size_y // 2, size_z // 2)


def refine(values):
    return jnp.repeat(jnp.repeat(jnp.repeat(values, 2, axis=0), 2, axis=1), 2, axis=2)


def coarsen_all(values):
    count_b, size_x, size_y, size_z = values.shape
    along_z = jnp.dot(
        values.reshape(count_b * size_x * size_y, size_z),
        pair_mean(size_z, 0.5),
        precision=lax.Precision.HIGHEST,
    ).reshape(count_b, size_x * size_y, size_z // 2)
    both = jnp.einsum(
        "pq,bqz->bpz", plane_mean(size_x, size_y), along_z, precision=lax.Precision.HIGHEST
    )
    return both.reshape(count_b, size_x // 2, size_y // 2, size_z // 2)


def refine_all(values):
    return jnp.repeat(jnp.repeat(jnp.repeat(values, 2, axis=1), 2, axis=2), 2, axis=3)


def refine_face(face):
    return jnp.repeat(jnp.repeat(face, 2, axis=0), 2, axis=1)


def refine_face_of(face):
    for axis in range(3):
        if face.shape[axis] != 1:
            face = jnp.repeat(face, 2, axis=axis)
    return face


def refined_faces(coarse_all, my_row, per_side):
    count_b = coarse_all.shape[0]

    def row(offset):
        return lax.dynamic_index_in_dim(coarse_all, (my_row + offset) % count_b, 0, keepdims=False)

    plane_step = per_side * per_side
    return [
        refine_face(row(-plane_step)[-1])[None],
        refine_face(row(plane_step)[0])[None],
        refine_face(row(-per_side)[:, -1])[:, None],
        refine_face(row(per_side)[:, 0])[:, None],
        refine_face(row(-1)[:, :, -1])[:, :, None],
        refine_face(row(1)[:, :, 0])[:, :, None],
    ]


def neighbour_rows(count_b, size_x, size_y, per_side):
    count_r = count_b * size_x * size_y
    index = jnp.arange(count_r)
    row = index // (size_x * size_y)
    at_x = index // size_y % size_x
    at_y = index % size_y
    plane_step = per_side * per_side
    picks = []
    for axis_no, (size, step) in enumerate(((size_x, plane_step), (size_y, per_side))):
        coord = at_x if axis_no == 0 else at_y
        for sign in (-1, 1):
            edge = size - 1 if sign > 0 else 0
            moved = jnp.where(coord == edge, size - 1 - edge, coord + sign)
            new_row = jnp.where(coord == edge, (row + sign * step) % count_b, row)
            if axis_no == 0:
                picks.append((new_row * size_x + moved) * size_y + at_y)
            else:
                picks.append((new_row * size_x + at_x) * size_y + moved)
    for sign in (-1, 1):
        picks.append((((row + sign) % count_b) * size_x + at_x) * size_y + at_y)
    target = jnp.concatenate(picks)
    return jnp.where(target[:, None] == index[None, :], 1.0, 0.0).astype(jnp.float32)


def lane_shift(size_z, sign):
    lanes_in = jnp.arange(size_z)[:, None]
    lanes_out = jnp.arange(size_z)[None, :]
    inner = jnp.where(lanes_in == lanes_out + sign, 1.0, 0.0)
    edge_in, edge_out = (size_z - 1, 0) if sign < 0 else (0, size_z - 1)
    wrap = jnp.where((lanes_in == edge_in) & (lanes_out == edge_out), 1.0, 0.0)
    return jnp.concatenate([inner, wrap]).astype(jnp.float32)


def flat_faces(values, picker, lower_z, upper_z):
    count_r, size_z = values.shape
    rows = jnp.dot(picker, values, precision=lax.Precision.HIGHEST)

    def along_z(shift, wrapped):
        return jnp.dot(values, shift[:size_z], precision=lax.Precision.HIGHEST) + jnp.dot(
            wrapped, shift[size_z:], precision=lax.Precision.HIGHEST
        )

    lower = along_z(lower_z, rows[4 * count_r : 5 * count_r])
    upper = along_z(upper_z, rows[5 * count_r :])
    return [rows[k * count_r : (k + 1) * count_r] for k in range(4)] + [lower, upper]


def row_mean(count_b, size_x, size_y):
    index = jnp.arange(count_b * size_x * size_y)
    row = index // (size_x * size_y)
    coarse_of = (row * (size_x // 2) + index // size_y % size_x // 2) * (size_y // 2) + index % size_y // 2
    return jnp.where(
        jnp.arange(count_b * size_x * size_y // 4)[:, None] == coarse_of[None, :], 0.25, 0.0
    ).astype(jnp.float32)


def global_cycle(all_rhs, all_perm, first_level, per_side):
    count_b, size_x, size_y, size_z = all_rhs.shape
    shapes = [(size_x >> n, size_y >> n, size_z >> n) for n in range(LEVELS - first_level + 1)]
    pickers = [neighbour_rows(count_b, sx, sy, per_side) for sx, sy, sz in shapes]
    shifts = [(lane_shift(sz, -1), lane_shift(sz, 1)) for sx, sy, sz in shapes]
    means = [(row_mean(count_b, sx, sy), pair_mean(sz, 0.5)) for sx, sy, sz in shapes[:-1]]

    def faces(values, number):
        return flat_faces(values, pickers[number], *shifts[number])

    def down(values, number):
        rows, lanes = means[number]
        return jnp.dot(
            rows,
            jnp.dot(values, lanes, precision=lax.Precision.HIGHEST),
            precision=lax.Precision.HIGHEST,
        )

    def up(values, number):
        rows, lanes = means[number]
        return jnp.dot(
            rows.T * 4.0,
            jnp.dot(values, lanes.T * 2.0, precision=lax.Precision.HIGHEST),
            precision=lax.Precision.HIGHEST,
        )

    perms = [all_perm.reshape(-1, size_z)]
    for number in range(LEVELS - first_level):
        perms.append(down(perms[-1], number))
    coefs = [
        coefficients(perms[number], faces(perms[number], number), 0.25 ** (first_level + number))
        for number in range(LEVELS - first_level + 1)
    ]
    right_side = all_rhs.reshape(-1, size_z)
    stored = []
    rights = []
    for number in range(LEVELS - first_level):
        face_coefs, diagonal = coefs[number]
        scaling = 0.25 ** (first_level + number)
        values = OMEGA * right_side / diagonal
        for sweep_no in range(SWEEPS - 1):
            values = smooth(values, right_side, face_coefs, diagonal, scaling, faces(values, number))
        leftover = right_side - operate(values, faces(values, number), face_coefs, scaling)
        stored.append(values)
        rights.append(right_side)
        right_side = down(leftover, number)
    last = LEVELS - first_level
    face_coefs, diagonal = coefs[last]
    scaling = 0.25**LEVELS
    correction = OMEGA * right_side / diagonal
    for sweep_no in range(CSWEEPS - 1):
        correction = smooth(
            correction, right_side, face_coefs, diagonal, scaling, faces(correction, last)
        )
    for number in reversed(range(LEVELS - first_level)):
        face_coefs, diagonal = coefs[number]
        scaling = 0.25 ** (first_level + number)
        values = stored[number] + up(correction, number)
        for sweep_no in range(SWEEPS):
            values = smooth(
                values, rights[number], face_coefs, diagonal, scaling, faces(values, number)
            )
        correction = values
    return correction.reshape(count_b, size_x, size_y, size_z)


def shards(perm_class, class_values, well_cells, well_rates, guess):
    count_dev = lax.axis_size("space")
    per_side = 2 + 2 * (count_dev // 64)
    my_row = lax.axis_index("space")
    block_no = (my_row + per_side * per_side + per_side + 1) % count_dev
    block_x = block_no // (per_side * per_side)
    block_y = block_no // per_side % per_side
    block_z = block_no % per_side
    classes = perm_class[0]
    width_x, width_y, width_z = classes.shape
    permeab = jnp.zeros(classes.shape, jnp.float32)
    for number in range(class_values.shape[0]):
        permeab = permeab + jnp.where(classes == number, class_values[number], 0.0)
    row_len = per_side * width_z
    plane = per_side * width_y * row_len
    glob_x = well_cells // plane
    glob_y = well_cells // row_len % (per_side * width_y)
    glob_z = well_cells % row_len
    onehot_x = jnp.where(
        (glob_x - block_x * width_x)[:, None] == jnp.arange(width_x)[None, :],
        well_rates[:, None],
        0.0,
    )
    onehot_y = jnp.where(
        (glob_y - block_y * width_y)[:, None] == jnp.arange(width_y)[None, :], 1.0, 0.0
    ).astype(jnp.float32)
    onehot_z = jnp.where(
        (glob_z - block_z * width_z)[:, None] == jnp.arange(width_z)[None, :], 1.0, 0.0
    ).astype(jnp.float32)
    source = jnp.einsum(
        "wi,wj,wk->ijk", onehot_x, onehot_y, onehot_z, precision=lax.Precision.HIGHEST
    )

    values = guess[0]
    coarse_perm = coarsen(permeab)
    first, coarse_first = exchange_with_coarse(jnp.stack([permeab, values]), coarse_perm, per_side)
    face_coefs, diagonal = coefficients(permeab, with_faces(permeab, pick(first, 0)), 1.0)
    values = smooth(values, source, face_coefs, diagonal, 1.0, with_faces(values, pick(first, 1)))
    for sweep_no in range(SWEEPS - 1):
        faces = pick(exchange(values[None], per_side), 0)
        values = smooth(values, source, face_coefs, diagonal, 1.0, with_faces(values, faces))
    stored_faces = pick(exchange(values[None], per_side), 0)
    leftover = source - operate(values, with_faces(values, stored_faces), face_coefs, 1.0)
    stored = values

    scaling = 0.25
    right_1 = coarsen(leftover)
    coefs_1, diagonal_1 = coefficients(coarse_perm, with_faces(coarse_perm, coarse_first), scaling)
    values_1 = OMEGA * right_1 / diagonal_1
    for sweep_no in range(SWEEPS - 1):
        faces = pick(exchange(values_1[None], per_side), 0)
        values_1 = smooth(values_1, right_1, coefs_1, diagonal_1, scaling, with_faces(values_1, faces))
    stored_faces_1 = pick(exchange(values_1[None], per_side), 0)
    leftover_1 = right_1 - operate(values_1, with_faces(values_1, stored_faces_1), coefs_1, scaling)
    stored_1 = values_1

    gathered = gather_rows(jnp.stack([coarsen(coarse_perm), coarsen(leftover_1)]), per_side)
    correction_all = global_cycle(gathered[:, 1], gathered[:, 0], 2, per_side)

    correction = lax.dynamic_index_in_dim(correction_all, my_row, 0, keepdims=False)
    values_1 = stored_1 + refine(correction)
    faces = [
        mine + theirs
        for mine, theirs in zip(stored_faces_1, refined_faces(correction_all, my_row, per_side))
    ]
    values_1 = smooth(values_1, right_1, coefs_1, diagonal_1, scaling, with_faces(values_1, faces))
    for sweep_no in range(SWEEPS - 1):
        faces = pick(exchange(values_1[None], per_side), 0)
        values_1 = smooth(values_1, right_1, coefs_1, diagonal_1, scaling, with_faces(values_1, faces))
    coarse_faces = pick(exchange(values_1[None], per_side), 0)

    values = stored + refine(values_1)
    faces = [mine + refine_face_of(theirs) for mine, theirs in zip(stored_faces, coarse_faces)]
    values = smooth(values, source, face_coefs, diagonal, 1.0, with_faces(values, faces))
    for sweep_no in range(SWEEPS - 1):
        faces = pick(exchange(values[None], per_side), 0)
        values = smooth(values, source, face_coefs, diagonal, 1.0, with_faces(values, faces))
    faces = pick(exchange(values[None], per_side), 0)
    residual = source - operate(values, with_faces(values, faces), face_coefs, 1.0)
    return (values[None], residual[None])


def solution(mesh):
    return jax.shard_map(
        shards,
        mesh=mesh,
        in_specs=(
            P("space", None, None, None),
            P(),
            P("real"),
            P("real"),
            P(("real", "space"), None, None, None),
        ),
        out_specs=(P(("real", "space"), None, None, None), P(("real", "space"), None, None, None)),
        check_vma=False,
    )
```

```python
import jax
import jax.numpy as jnp
from jax import lax
from jax.sharding import PartitionSpec as P

LEVELS = 3
SWEEPS = 2
CSWEEPS = 6


OMEGA = 0.8


def shifted(shard, axis, by):
    peers = lax.axis_size(axis)
    return lax.ppermute(shard, axis, [(i, (i + by) % peers) for i in range(peers)])


def exchange(fields, per_side):
    count_dev = lax.axis_size("space")
    plane_step = per_side * per_side
    if (2 * plane_step) % count_dev == 0:
        both_x = shifted(jnp.concatenate([fields[:, -1:], fields[:, :1]], axis=1), "space", plane_step)
        lower_x, upper_x = both_x[:, :1], both_x[:, 1:]
    else:
        lower_x = shifted(fields[:, -1:], "space", plane_step)
        upper_x = shifted(fields[:, :1], "space", -plane_step)
    lower_y = shifted(fields[:, :, -1:], "space", per_side)
    upper_y = shifted(fields[:, :, :1], "space", -per_side)
    lower_z = shifted(fields[:, :, :, -1:], "space", 1)
    upper_z = shifted(fields[:, :, :, :1], "space", -1)
    return [lower_x, upper_x, lower_y, upper_y, lower_z, upper_z]


def own_faces(values):
    return [values[-1:], values[:1], values[:, -1:], values[:, :1], values[:, :, -1:], values[:, :, :1]]


def exchange_mixed(fields, per_side):
    count_dev = lax.axis_size("space")
    plane_step = per_side * per_side
    outgoing = [own_faces(values) for values in fields]
    shifts = [plane_step, -plane_step, per_side, -per_side, 1, -1]
    flat = [jnp.concatenate([faces[d].reshape(-1) for faces in outgoing]) for d in range(6)]
    received = [None] * 6
    if (2 * plane_step) % count_dev == 0:
        both = shifted(jnp.concatenate([flat[0], flat[1]]), "space", plane_step)
        received[0], received[1] = both[: flat[0].shape[0]], both[flat[0].shape[0] :]
        rest = range(2, 6)
    else:
        rest = range(6)
    for d in rest:
        received[d] = shifted(flat[d], "space", shifts[d])
    result = [[None] * 6 for _ in fields]
    for d in range(6):
        offset = 0
        for number, faces in enumerate(outgoing):
            size = faces[d].size
            result[number][d] = received[d][offset : offset + size].reshape(faces[d].shape)
            offset += size
    return result


def exchange_with_coarse(fields, coarse, per_side):
    count_dev = lax.axis_size("space")
    plane_step = per_side * per_side
    size_x, size_y, size_z = fields.shape[1:]
    half_x, half_y, half_z = coarse.shape

    def padded(face):
        pads = [(0, full - part) if part != 1 else (0, 0) for full, part in zip((size_x, size_y, size_z), face.shape)]
        return jnp.pad(face, pads)[None]

    def message(number):
        pieces = [fields[:, -1:], fields[:, :1], fields[:, :, -1:], fields[:, :, :1], fields[:, :, :, -1:], fields[:, :, :, :1]]
        return jnp.concatenate([pieces[number], padded(own_faces(coarse)[number])], axis=0)

    shifts = [plane_step, -plane_step, per_side, -per_side, 1, -1]
    received = [None] * 6
    if (2 * plane_step) % count_dev == 0:
        both = shifted(jnp.concatenate([message(0), message(1)], axis=1), "space", plane_step)
        received[0], received[1] = both[:, :1], both[:, 1:]
        rest = range(2, 6)
    else:
        rest = range(6)
    for number in rest:
        received[number] = shifted(message(number), "space", shifts[number])
    count = fields.shape[0]
    field_faces = [face[:count] for face in received]
    coarse_faces = []
    for number, face in enumerate(received):
        shape = own_faces(coarse)[number].shape
        coarse_faces.append(face[count, : shape[0], : shape[1], : shape[2]])
    return field_faces, coarse_faces


def gather_rows(block, per_side):
    count_dev = lax.axis_size("space")
    if count_dev > 16:
        return lax.all_gather(block[None], "space", axis=0, tiled=True)
    my_row = lax.axis_index("space")
    by_offset = jnp.stack([block] + [shifted(block, "space", k) for k in range(1, count_dev)])
    return jnp.take(by_offset, (my_row - jnp.arange(count_dev)) % count_dev, axis=0)


def pick(faces, number):
    return [face[number] for face in faces]


def with_faces(values, faces):
    lower_x, upper_x, lower_y, upper_y, lower_z, upper_z = faces
    return [
        jnp.concatenate([lower_x, values[:-1]], axis=0),
        jnp.concatenate([values[1:], upper_x], axis=0),
        jnp.concatenate([lower_y, values[:, :-1]], axis=1),
        jnp.concatenate([values[:, 1:], upper_y], axis=1),
        jnp.concatenate([lower_z, values[:, :, :-1]], axis=2),
        jnp.concatenate([values[:, :, 1:], upper_z], axis=2),
    ]


def rolled_faces(values, per_side):
    plane_step = per_side * per_side
    return [
        jnp.concatenate([jnp.roll(values[:, -1:], plane_step, axis=0), values[:, :-1]], axis=1),
        jnp.concatenate([values[:, 1:], jnp.roll(values[:, :1], -plane_step, axis=0)], axis=1),
        jnp.concatenate([jnp.roll(values[:, :, -1:], per_side, axis=0), values[:, :, :-1]], axis=2),
        jnp.concatenate([values[:, :, 1:], jnp.roll(values[:, :, :1], -per_side, axis=0)], axis=2),
        jnp.concatenate([jnp.roll(values[:, :, :, -1:], 1, axis=0), values[:, :, :, :-1]], axis=3),
        jnp.concatenate([values[:, :, :, 1:], jnp.roll(values[:, :, :, :1], -1, axis=0)], axis=3),
    ]


def coefficients(permeab, neighbors, scaling):
    face_coefs = [0.5 * (permeab + beside) for beside in neighbors]
    total_sum = face_coefs[0]
    for number in range(1, 6):
        total_sum = total_sum + face_coefs[number]
    return (face_coefs, scaling * total_sum)


def operate(values, neighbors, face_coefs, scaling):
    total_sum = face_coefs[0] * (values - neighbors[0])
    for number in range(1, 6):
        total_sum = total_sum + face_coefs[number] * (values - neighbors[number])
    return scaling * total_sum


def smooth(values, right_side, face_coefs, diagonal, scaling, neighbors):
    return values + OMEGA * (right_side - operate(values, neighbors, face_coefs, scaling)) / diagonal


def pair_mean(size, scale):
    rows = jnp.arange(size)[:, None] // 2
    cols = jnp.arange(size // 2)[None, :]
    return jnp.where(rows == cols, scale, 0.0).astype(jnp.float32)


def plane_mean(size_x, size_y):
    fine = jnp.arange(size_x * size_y)
    coarse_of = (fine // size_y // 2) * (size_y // 2) + (fine % size_y) // 2
    return jnp.where(
        jnp.arange(size_x * size_y // 4)[:, None] == coarse_of[None, :], 0.25, 0.0
    ).astype(jnp.float32)


def coarsen(values):
    size_x, size_y, size_z = values.shape
    along_z = jnp.dot(
        values.reshape(size_x * size_y, size_z),
        pair_mean(size_z, 0.5),
        precision=lax.Precision.HIGHEST,
    )
    both = jnp.dot(plane_mean(size_x, size_y), along_z, precision=lax.Precision.HIGHEST)
    return both.reshape(size_x // 2, size_y // 2, size_z // 2)


def refine(values):
    return jnp.repeat(jnp.repeat(jnp.repeat(values, 2, axis=0), 2, axis=1), 2, axis=2)


def coarsen_all(values):
    count_b, size_x, size_y, size_z = values.shape
    along_z = jnp.dot(
        values.reshape(count_b * size_x * size_y, size_z),
        pair_mean(size_z, 0.5),
        precision=lax.Precision.HIGHEST,
    ).reshape(count_b, size_x * size_y, size_z // 2)
    both = jnp.einsum(
        "pq,bqz->bpz", plane_mean(size_x, size_y), along_z, precision=lax.Precision.HIGHEST
    )
    return both.reshape(count_b, size_x // 2, size_y // 2, size_z // 2)


def refine_all(values):
    return jnp.repeat(jnp.repeat(jnp.repeat(values, 2, axis=1), 2, axis=2), 2, axis=3)


def refine_face(face):
    return jnp.repeat(jnp.repeat(face, 2, axis=0), 2, axis=1)


def refine_face_of(face):
    for axis in range(3):
        if face.shape[axis] != 1:
            face = jnp.repeat(face, 2, axis=axis)
    return face


def refined_faces(coarse_all, my_row, per_side):
    count_b = coarse_all.shape[0]

    def row(offset):
        return lax.dynamic_index_in_dim(coarse_all, (my_row + offset) % count_b, 0, keepdims=False)

    plane_step = per_side * per_side
    return [
        refine_face(row(-plane_step)[-1])[None],
        refine_face(row(plane_step)[0])[None],
        refine_face(row(-per_side)[:, -1])[:, None],
        refine_face(row(per_side)[:, 0])[:, None],
        refine_face(row(-1)[:, :, -1])[:, :, None],
        refine_face(row(1)[:, :, 0])[:, :, None],
    ]


def neighbour_rows(count_b, size_x, size_y, per_side):
    count_r = count_b * size_x * size_y
    index = jnp.arange(count_r)
    row = index // (size_x * size_y)
    at_x = index // size_y % size_x
    at_y = index % size_y
    plane_step = per_side * per_side
    picks = []
    for axis_no, (size, step) in enumerate(((size_x, plane_step), (size_y, per_side))):
        coord = at_x if axis_no == 0 else at_y
        for sign in (-1, 1):
            edge = size - 1 if sign > 0 else 0
            moved = jnp.where(coord == edge, size - 1 - edge, coord + sign)
            new_row = jnp.where(coord == edge, (row + sign * step) % count_b, row)
            if axis_no == 0:
                picks.append((new_row * size_x + moved) * size_y + at_y)
            else:
                picks.append((new_row * size_x + at_x) * size_y + moved)
    for sign in (-1, 1):
        picks.append((((row + sign) % count_b) * size_x + at_x) * size_y + at_y)
    target = jnp.concatenate(picks)
    return jnp.where(target[:, None] == index[None, :], 1.0, 0.0).astype(jnp.float32)


def lane_shift(size_z, sign):
    lanes_in = jnp.arange(size_z)[:, None]
    lanes_out = jnp.arange(size_z)[None, :]
    inner = jnp.where(lanes_in == lanes_out + sign, 1.0, 0.0)
    edge_in, edge_out = (size_z - 1, 0) if sign < 0 else (0, size_z - 1)
    wrap = jnp.where((lanes_in == edge_in) & (lanes_out == edge_out), 1.0, 0.0)
    return jnp.concatenate([inner, wrap]).astype(jnp.float32)


def flat_faces(values, picker, lower_z, upper_z):
    count_r, size_z = values.shape
    rows = jnp.dot(picker, values, precision=lax.Precision.HIGHEST)

    def along_z(shift, wrapped):
        return jnp.dot(values, shift[:size_z], precision=lax.Precision.HIGHEST) + jnp.dot(
            wrapped, shift[size_z:], precision=lax.Precision.HIGHEST
        )

    lower = along_z(lower_z, rows[4 * count_r : 5 * count_r])
    upper = along_z(upper_z, rows[5 * count_r :])
    return [rows[k * count_r : (k + 1) * count_r] for k in range(4)] + [lower, upper]


def row_mean(count_b, size_x, size_y):
    index = jnp.arange(count_b * size_x * size_y)
    row = index // (size_x * size_y)
    coarse_of = (row * (size_x // 2) + index // size_y % size_x // 2) * (size_y // 2) + index % size_y // 2
    return jnp.where(
        jnp.arange(count_b * size_x * size_y // 4)[:, None] == coarse_of[None, :], 0.25, 0.0
    ).astype(jnp.float32)


def global_cycle(all_rhs, all_perm, first_level, per_side):
    count_b, size_x, size_y, size_z = all_rhs.shape
    shapes = [(size_x >> n, size_y >> n, size_z >> n) for n in range(LEVELS - first_level + 1)]
    pickers = [neighbour_rows(count_b, sx, sy, per_side) for sx, sy, sz in shapes]
    shifts = [(lane_shift(sz, -1), lane_shift(sz, 1)) for sx, sy, sz in shapes]
    means = [(row_mean(count_b, sx, sy), pair_mean(sz, 0.5)) for sx, sy, sz in shapes[:-1]]

    def faces(values, number):
        return flat_faces(values, pickers[number], *shifts[number])

    def down(values, number):
        rows, lanes = means[number]
        return jnp.dot(
            rows,
            jnp.dot(values, lanes, precision=lax.Precision.HIGHEST),
            precision=lax.Precision.HIGHEST,
        )

    def up(values, number):
        rows, lanes = means[number]
        return jnp.dot(
            rows.T * 4.0,
            jnp.dot(values, lanes.T * 2.0, precision=lax.Precision.HIGHEST),
            precision=lax.Precision.HIGHEST,
        )

    perms = [all_perm.reshape(-1, size_z)]
    for number in range(LEVELS - first_level):
        perms.append(down(perms[-1], number))
    coefs = [
        coefficients(perms[number], faces(perms[number], number), 0.25 ** (first_level + number))
        for number in range(LEVELS - first_level + 1)
    ]
    right_side = all_rhs.reshape(-1, size_z)
    stored = []
    rights = []
    for number in range(LEVELS - first_level):
        face_coefs, diagonal = coefs[number]
        scaling = 0.25 ** (first_level + number)
        values = OMEGA * right_side / diagonal
        for sweep_no in range(SWEEPS - 1):
            values = smooth(values, right_side, face_coefs, diagonal, scaling, faces(values, number))
        leftover = right_side - operate(values, faces(values, number), face_coefs, scaling)
        stored.append(values)
        rights.append(right_side)
        right_side = down(leftover, number)
    last = LEVELS - first_level
    face_coefs, diagonal = coefs[last]
    scaling = 0.25**LEVELS
    correction = OMEGA * right_side / diagonal
    for sweep_no in range(CSWEEPS - 1):
        correction = smooth(
            correction, right_side, face_coefs, diagonal, scaling, faces(correction, last)
        )
    for number in reversed(range(LEVELS - first_level)):
        face_coefs, diagonal = coefs[number]
        scaling = 0.25 ** (first_level + number)
        values = stored[number] + up(correction, number)
        for sweep_no in range(SWEEPS):
            values = smooth(
                values, rights[number], face_coefs, diagonal, scaling, faces(values, number)
            )
        correction = values
    return correction.reshape(count_b, size_x, size_y, size_z)


def shards(perm_class, class_values, well_cells, well_rates, guess):
    count_dev = lax.axis_size("space")
    per_side = 2 + 2 * (count_dev // 64)
    my_row = lax.axis_index("space")
    block_no = (my_row + per_side * per_side + per_side + 1) % count_dev
    block_x = block_no // (per_side * per_side)
    block_y = block_no // per_side % per_side
    block_z = block_no % per_side
    classes = perm_class[0]
    width_x, width_y, width_z = classes.shape
    permeab = jnp.zeros(classes.shape, jnp.float32)
    for number in range(class_values.shape[0]):
        permeab = permeab + jnp.where(classes == number, class_values[number], 0.0)
    row_len = per_side * width_z
    plane = per_side * width_y * row_len
    glob_x = well_cells // plane
    glob_y = well_cells // row_len % (per_side * width_y)
    glob_z = well_cells % row_len
    onehot_x = jnp.where(
        (glob_x - block_x * width_x)[:, None] == jnp.arange(width_x)[None, :],
        well_rates[:, None],
        0.0,
    )
    onehot_y = jnp.where(
        (glob_y - block_y * width_y)[:, None] == jnp.arange(width_y)[None, :], 1.0, 0.0
    ).astype(jnp.float32)
    onehot_z = jnp.where(
        (glob_z - block_z * width_z)[:, None] == jnp.arange(width_z)[None, :], 1.0, 0.0
    ).astype(jnp.float32)
    source = jnp.einsum(
        "wi,wj,wk->ijk", onehot_x, onehot_y, onehot_z, precision=lax.Precision.HIGHEST
    )

    values = guess[0]
    if count_dev * (width_x // 2) * (width_y // 2) <= 512:
        first = exchange(jnp.stack([permeab, values]), per_side)
        face_coefs, diagonal = coefficients(permeab, with_faces(permeab, pick(first, 0)), 1.0)
        values = smooth(values, source, face_coefs, diagonal, 1.0, with_faces(values, pick(first, 1)))
        for sweep_no in range(SWEEPS - 1):
            faces = pick(exchange(values[None], per_side), 0)
            values = smooth(values, source, face_coefs, diagonal, 1.0, with_faces(values, faces))
        stored_faces = pick(exchange(values[None], per_side), 0)
        leftover = source - operate(values, with_faces(values, stored_faces), face_coefs, 1.0)
        stored = values

        gathered = gather_rows(jnp.stack([coarsen(permeab), coarsen(leftover)]), per_side)
        correction_all = global_cycle(gathered[:, 1], gathered[:, 0], 1, per_side)

        correction = lax.dynamic_index_in_dim(correction_all, my_row, 0, keepdims=False)
        values = stored + refine(correction)
        faces = [
            mine + theirs
            for mine, theirs in zip(stored_faces, refined_faces(correction_all, my_row, per_side))
        ]
        values = smooth(values, source, face_coefs, diagonal, 1.0, with_faces(values, faces))
        for sweep_no in range(SWEEPS - 1):
            faces = pick(exchange(values[None], per_side), 0)
            values = smooth(values, source, face_coefs, diagonal, 1.0, with_faces(values, faces))
        faces = pick(exchange(values[None], per_side), 0)
        residual = source - operate(values, with_faces(values, faces), face_coefs, 1.0)
        return (values[None], residual[None])

    coarse_perm = coarsen(permeab)
    first, coarse_first = exchange_with_coarse(jnp.stack([permeab, values]), coarse_perm, per_side)
    face_coefs, diagonal = coefficients(permeab, with_faces(permeab, pick(first, 0)), 1.0)
    values = smooth(values, source, face_coefs, diagonal, 1.0, with_faces(values, pick(first, 1)))
    for sweep_no in range(SWEEPS - 1):
        faces = pick(exchange(values[None], per_side), 0)
        values = smooth(values, source, face_coefs, diagonal, 1.0, with_faces(values, faces))
    stored_faces = pick(exchange(values[None], per_side), 0)
    leftover = source - operate(values, with_faces(values, stored_faces), face_coefs, 1.0)
    stored = values

    scaling = 0.25
    right_1 = coarsen(leftover)
    coefs_1, diagonal_1 = coefficients(coarse_perm, with_faces(coarse_perm, coarse_first), scaling)
    values_1 = OMEGA * right_1 / diagonal_1
    for sweep_no in range(SWEEPS - 1):
        faces = pick(exchange(values_1[None], per_side), 0)
        values_1 = smooth(values_1, right_1, coefs_1, diagonal_1, scaling, with_faces(values_1, faces))
    stored_faces_1 = pick(exchange(values_1[None], per_side), 0)
    leftover_1 = right_1 - operate(values_1, with_faces(values_1, stored_faces_1), coefs_1, scaling)
    stored_1 = values_1

    gathered = gather_rows(jnp.stack([coarsen(coarse_perm), coarsen(leftover_1)]), per_side)
    correction_all = global_cycle(gathered[:, 1], gathered[:, 0], 2, per_side)

    correction = lax.dynamic_index_in_dim(correction_all, my_row, 0, keepdims=False)
    values_1 = stored_1 + refine(correction)
    faces = [
        mine + theirs
        for mine, theirs in zip(stored_faces_1, refined_faces(correction_all, my_row, per_side))
    ]
    values_1 = smooth(values_1, right_1, coefs_1, diagonal_1, scaling, with_faces(values_1, faces))
    for sweep_no in range(SWEEPS - 1):
        faces = pick(exchange(values_1[None], per_side), 0)
        values_1 = smooth(values_1, right_1, coefs_1, diagonal_1, scaling, with_faces(values_1, faces))
    coarse_faces = pick(exchange(values_1[None], per_side), 0)

    values = stored + refine(values_1)
    faces = [mine + refine_face_of(theirs) for mine, theirs in zip(stored_faces, coarse_faces)]
    values = smooth(values, source, face_coefs, diagonal, 1.0, with_faces(values, faces))
    for sweep_no in range(SWEEPS - 1):
        faces = pick(exchange(values[None], per_side), 0)
        values = smooth(values, source, face_coefs, diagonal, 1.0, with_faces(values, faces))
    faces = pick(exchange(values[None], per_side), 0)
    residual = source - operate(values, with_faces(values, faces), face_coefs, 1.0)
    return (values[None], residual[None])


def solution(mesh):
    return jax.shard_map(
        shards,
        mesh=mesh,
        in_specs=(
            P("space", None, None, None),
            P(),
            P("real"),
            P("real"),
            P(("real", "space"), None, None, None),
        ),
        out_specs=(P(("real", "space"), None, None, None), P(("real", "space"), None, None, None)),
        check_vma=False,
    )
```

```python
import jax
import jax.numpy as jnp
from jax import lax
from jax.sharding import PartitionSpec as P

LEVELS = 3
SWEEPS = 2
CSWEEPS = 6


OMEGA = 0.8


def shifted(shard, axis, by):
    peers = lax.axis_size(axis)
    return lax.ppermute(shard, axis, [(i, (i + by) % peers) for i in range(peers)])


def exchange(fields, per_side):
    count_dev = lax.axis_size("space")
    plane_step = per_side * per_side
    if (2 * plane_step) % count_dev == 0:
        both_x = shifted(jnp.concatenate([fields[:, -1:], fields[:, :1]], axis=1), "space", plane_step)
        lower_x, upper_x = both_x[:, :1], both_x[:, 1:]
    else:
        lower_x = shifted(fields[:, -1:], "space", plane_step)
        upper_x = shifted(fields[:, :1], "space", -plane_step)
    lower_y = shifted(fields[:, :, -1:], "space", per_side)
    upper_y = shifted(fields[:, :, :1], "space", -per_side)
    lower_z = shifted(fields[:, :, :, -1:], "space", 1)
    upper_z = shifted(fields[:, :, :, :1], "space", -1)
    return [lower_x, upper_x, lower_y, upper_y, lower_z, upper_z]


def own_faces(values):
    return [values[-1:], values[:1], values[:, -1:], values[:, :1], values[:, :, -1:], values[:, :, :1]]


def exchange_mixed(fields, per_side):
    count_dev = lax.axis_size("space")
    plane_step = per_side * per_side
    outgoing = [own_faces(values) for values in fields]
    shifts = [plane_step, -plane_step, per_side, -per_side, 1, -1]
    flat = [jnp.concatenate([faces[d].reshape(-1) for faces in outgoing]) for d in range(6)]
    received = [None] * 6
    if (2 * plane_step) % count_dev == 0:
        both = shifted(jnp.concatenate([flat[0], flat[1]]), "space", plane_step)
        received[0], received[1] = both[: flat[0].shape[0]], both[flat[0].shape[0] :]
        rest = range(2, 6)
    else:
        rest = range(6)
    for d in rest:
        received[d] = shifted(flat[d], "space", shifts[d])
    result = [[None] * 6 for _ in fields]
    for d in range(6):
        offset = 0
        for number, faces in enumerate(outgoing):
            size = faces[d].size
            result[number][d] = received[d][offset : offset + size].reshape(faces[d].shape)
            offset += size
    return result


def exchange_with_coarse(fields, coarse, per_side):
    count_dev = lax.axis_size("space")
    plane_step = per_side * per_side
    size_x, size_y, size_z = fields.shape[1:]
    half_x, half_y, half_z = coarse.shape

    def padded(face):
        pads = [(0, full - part) if part != 1 else (0, 0) for full, part in zip((size_x, size_y, size_z), face.shape)]
        return jnp.pad(face, pads)[None]

    def message(number):
        pieces = [fields[:, -1:], fields[:, :1], fields[:, :, -1:], fields[:, :, :1], fields[:, :, :, -1:], fields[:, :, :, :1]]
        return jnp.concatenate([pieces[number], padded(own_faces(coarse)[number])], axis=0)

    shifts = [plane_step, -plane_step, per_side, -per_side, 1, -1]
    received = [None] * 6
    if (2 * plane_step) % count_dev == 0:
        both = shifted(jnp.concatenate([message(0), message(1)], axis=1), "space", plane_step)
        received[0], received[1] = both[:, :1], both[:, 1:]
        rest = range(2, 6)
    else:
        rest = range(6)
    for number in rest:
        received[number] = shifted(message(number), "space", shifts[number])
    count = fields.shape[0]
    field_faces = [face[:count] for face in received]
    coarse_faces = []
    for number, face in enumerate(received):
        shape = own_faces(coarse)[number].shape
        coarse_faces.append(face[count, : shape[0], : shape[1], : shape[2]])
    return field_faces, coarse_faces


def gather_rows(block, per_side):
    count_dev = lax.axis_size("space")
    if count_dev > 16:
        return lax.all_gather(block[None], "space", axis=0, tiled=True)
    my_row = lax.axis_index("space")
    by_offset = jnp.stack([block] + [shifted(block, "space", k) for k in range(1, count_dev)])
    return jnp.take(by_offset, (my_row - jnp.arange(count_dev)) % count_dev, axis=0)


def pick(faces, number):
    return [face[number] for face in faces]


def with_faces(values, faces):
    lower_x, upper_x, lower_y, upper_y, lower_z, upper_z = faces
    return [
        jnp.concatenate([lower_x, values[:-1]], axis=0),
        jnp.concatenate([values[1:], upper_x], axis=0),
        jnp.concatenate([lower_y, values[:, :-1]], axis=1),
        jnp.concatenate([values[:, 1:], upper_y], axis=1),
        jnp.concatenate([lower_z, values[:, :, :-1]], axis=2),
        jnp.concatenate([values[:, :, 1:], upper_z], axis=2),
    ]


def rolled_faces(values, per_side):
    plane_step = per_side * per_side
    return [
        jnp.concatenate([jnp.roll(values[:, -1:], plane_step, axis=0), values[:, :-1]], axis=1),
        jnp.concatenate([values[:, 1:], jnp.roll(values[:, :1], -plane_step, axis=0)], axis=1),
        jnp.concatenate([jnp.roll(values[:, :, -1:], per_side, axis=0), values[:, :, :-1]], axis=2),
        jnp.concatenate([values[:, :, 1:], jnp.roll(values[:, :, :1], -per_side, axis=0)], axis=2),
        jnp.concatenate([jnp.roll(values[:, :, :, -1:], 1, axis=0), values[:, :, :, :-1]], axis=3),
        jnp.concatenate([values[:, :, :, 1:], jnp.roll(values[:, :, :, :1], -1, axis=0)], axis=3),
    ]


def coefficients(permeab, neighbors, scaling):
    face_coefs = [0.5 * (permeab + beside) for beside in neighbors]
    total_sum = face_coefs[0]
    for number in range(1, 6):
        total_sum = total_sum + face_coefs[number]
    return (face_coefs, scaling * total_sum)


def operate(values, neighbors, face_coefs, scaling):
    total_sum = face_coefs[0] * (values - neighbors[0])
    for number in range(1, 6):
        total_sum = total_sum + face_coefs[number] * (values - neighbors[number])
    return scaling * total_sum


def smooth(values, right_side, face_coefs, diagonal, scaling, neighbors):
    return values + OMEGA * (right_side - operate(values, neighbors, face_coefs, scaling)) / diagonal


def pair_mean(size, scale):
    rows = jnp.arange(size)[:, None] // 2
    cols = jnp.arange(size // 2)[None, :]
    return jnp.where(rows == cols, scale, 0.0).astype(jnp.float32)


def plane_mean(size_x, size_y):
    fine = jnp.arange(size_x * size_y)
    coarse_of = (fine // size_y // 2) * (size_y // 2) + (fine % size_y) // 2
    return jnp.where(
        jnp.arange(size_x * size_y // 4)[:, None] == coarse_of[None, :], 0.25, 0.0
    ).astype(jnp.float32)


def coarsen(values):
    size_x, size_y, size_z = values.shape
    along_z = jnp.dot(
        values.reshape(size_x * size_y, size_z),
        pair_mean(size_z, 0.5),
        precision=lax.Precision.HIGHEST,
    )
    both = jnp.dot(plane_mean(size_x, size_y), along_z, precision=lax.Precision.HIGHEST)
    return both.reshape(size_x // 2, size_y // 2, size_z // 2)


def refine(values):
    return jnp.repeat(jnp.repeat(jnp.repeat(values, 2, axis=0), 2, axis=1), 2, axis=2)


def coarsen_all(values):
    count_b, size_x, size_y, size_z = values.shape
    along_z = jnp.dot(
        values.reshape(count_b * size_x * size_y, size_z),
        pair_mean(size_z, 0.5),
        precision=lax.Precision.HIGHEST,
    ).reshape(count_b, size_x * size_y, size_z // 2)
    both = jnp.einsum(
        "pq,bqz->bpz", plane_mean(size_x, size_y), along_z, precision=lax.Precision.HIGHEST
    )
    return both.reshape(count_b, size_x // 2, size_y // 2, size_z // 2)


def refine_all(values):
    return jnp.repeat(jnp.repeat(jnp.repeat(values, 2, axis=1), 2, axis=2), 2, axis=3)


def refine_face(face):
    return jnp.repeat(jnp.repeat(face, 2, axis=0), 2, axis=1)


def refine_face_of(face):
    for axis in range(3):
        if face.shape[axis] != 1:
            face = jnp.repeat(face, 2, axis=axis)
    return face


def refined_faces(coarse_all, my_row, per_side):
    count_b = coarse_all.shape[0]

    def row(offset):
        return lax.dynamic_index_in_dim(coarse_all, (my_row + offset) % count_b, 0, keepdims=False)

    plane_step = per_side * per_side
    return [
        refine_face(row(-plane_step)[-1])[None],
        refine_face(row(plane_step)[0])[None],
        refine_face(row(-per_side)[:, -1])[:, None],
        refine_face(row(per_side)[:, 0])[:, None],
        refine_face(row(-1)[:, :, -1])[:, :, None],
        refine_face(row(1)[:, :, 0])[:, :, None],
    ]


def neighbour_rows(count_b, size_x, size_y, per_side):
    count_r = count_b * size_x * size_y
    index = jnp.arange(count_r)
    row = index // (size_x * size_y)
    at_x = index // size_y % size_x
    at_y = index % size_y
    plane_step = per_side * per_side
    picks = []
    for axis_no, (size, step) in enumerate(((size_x, plane_step), (size_y, per_side))):
        coord = at_x if axis_no == 0 else at_y
        for sign in (-1, 1):
            edge = size - 1 if sign > 0 else 0
            moved = jnp.where(coord == edge, size - 1 - edge, coord + sign)
            new_row = jnp.where(coord == edge, (row + sign * step) % count_b, row)
            if axis_no == 0:
                picks.append((new_row * size_x + moved) * size_y + at_y)
            else:
                picks.append((new_row * size_x + at_x) * size_y + moved)
    for sign in (-1, 1):
        picks.append((((row + sign) % count_b) * size_x + at_x) * size_y + at_y)
    target = jnp.concatenate(picks)
    return jnp.where(target[:, None] == index[None, :], 1.0, 0.0).astype(jnp.bfloat16)


def lane_shift(size_z, sign):
    lanes_in = jnp.arange(size_z)[:, None]
    lanes_out = jnp.arange(size_z)[None, :]
    inner = jnp.where(lanes_in == lanes_out + sign, 1.0, 0.0)
    edge_in, edge_out = (size_z - 1, 0) if sign < 0 else (0, size_z - 1)
    wrap = jnp.where((lanes_in == edge_in) & (lanes_out == edge_out), 1.0, 0.0)
    return jnp.concatenate([inner, wrap]).astype(jnp.bfloat16)


def split3(values):
    pieces = []
    rest = values
    for piece_no in range(3):
        piece = lax.reduce_precision(rest, exponent_bits=8, mantissa_bits=7)
        pieces.append(piece.astype(jnp.bfloat16))
        rest = rest - piece
    return pieces


def pick_rows(picker, values):
    size_z = values.shape[1]
    joined = jnp.concatenate(split3(values), axis=1)
    out = jnp.dot(picker, joined, preferred_element_type=jnp.float32)
    return (out[:, :size_z] + out[:, size_z : 2 * size_z]) + out[:, 2 * size_z :]


def pick_lanes(values, shift):
    count_r = values.shape[0]
    stacked = jnp.concatenate(split3(values), axis=0)
    out = jnp.dot(stacked, shift, preferred_element_type=jnp.float32)
    return (out[:count_r] + out[count_r : 2 * count_r]) + out[2 * count_r :]


def flat_faces(values, picker, lower_z, upper_z):
    count_r, size_z = values.shape
    rows = pick_rows(picker, values)

    def along_z(shift, wrapped):
        return pick_lanes(values, shift[:size_z]) + pick_lanes(wrapped, shift[size_z:])

    lower = along_z(lower_z, rows[4 * count_r : 5 * count_r])
    upper = along_z(upper_z, rows[5 * count_r :])
    return [rows[k * count_r : (k + 1) * count_r] for k in range(4)] + [lower, upper]


def row_mean(count_b, size_x, size_y):
    index = jnp.arange(count_b * size_x * size_y)
    row = index // (size_x * size_y)
    coarse_of = (row * (size_x // 2) + index // size_y % size_x // 2) * (size_y // 2) + index % size_y // 2
    return jnp.where(
        jnp.arange(count_b * size_x * size_y // 4)[:, None] == coarse_of[None, :], 0.25, 0.0
    ).astype(jnp.float32)


def global_cycle(all_rhs, all_perm, first_level, per_side):
    count_b, size_x, size_y, size_z = all_rhs.shape
    shapes = [(size_x >> n, size_y >> n, size_z >> n) for n in range(LEVELS - first_level + 1)]
    pickers = [neighbour_rows(count_b, sx, sy, per_side) for sx, sy, sz in shapes]
    shifts = [(lane_shift(sz, -1), lane_shift(sz, 1)) for sx, sy, sz in shapes]
    means = [(row_mean(count_b, sx, sy), pair_mean(sz, 0.5)) for sx, sy, sz in shapes[:-1]]

    def faces(values, number):
        return flat_faces(values, pickers[number], *shifts[number])

    def down(values, number):
        rows, lanes = means[number]
        return jnp.dot(
            rows,
            jnp.dot(values, lanes, precision=lax.Precision.HIGHEST),
            precision=lax.Precision.HIGHEST,
        )

    def up(values, number):
        rows, lanes = means[number]
        return jnp.dot(
            rows.T * 4.0,
            jnp.dot(values, lanes.T * 2.0, precision=lax.Precision.HIGHEST),
            precision=lax.Precision.HIGHEST,
        )

    perms = [all_perm.reshape(-1, size_z)]
    for number in range(LEVELS - first_level):
        perms.append(down(perms[-1], number))
    coefs = [
        coefficients(perms[number], faces(perms[number], number), 0.25 ** (first_level + number))
        for number in range(LEVELS - first_level + 1)
    ]
    right_side = all_rhs.reshape(-1, size_z)
    stored = []
    rights = []
    for number in range(LEVELS - first_level):
        face_coefs, diagonal = coefs[number]
        scaling = 0.25 ** (first_level + number)
        values = OMEGA * right_side / diagonal
        for sweep_no in range(SWEEPS - 1):
            values = smooth(values, right_side, face_coefs, diagonal, scaling, faces(values, number))
        leftover = right_side - operate(values, faces(values, number), face_coefs, scaling)
        stored.append(values)
        rights.append(right_side)
        right_side = down(leftover, number)
    last = LEVELS - first_level
    face_coefs, diagonal = coefs[last]
    scaling = 0.25**LEVELS
    correction = OMEGA * right_side / diagonal
    for sweep_no in range(CSWEEPS - 1):
        correction = smooth(
            correction, right_side, face_coefs, diagonal, scaling, faces(correction, last)
        )
    for number in reversed(range(LEVELS - first_level)):
        face_coefs, diagonal = coefs[number]
        scaling = 0.25 ** (first_level + number)
        values = stored[number] + up(correction, number)
        for sweep_no in range(SWEEPS):
            values = smooth(
                values, rights[number], face_coefs, diagonal, scaling, faces(values, number)
            )
        correction = values
    return correction.reshape(count_b, size_x, size_y, size_z)


def shards(perm_class, class_values, well_cells, well_rates, guess):
    count_dev = lax.axis_size("space")
    per_side = 2 + 2 * (count_dev // 64)
    my_row = lax.axis_index("space")
    block_no = (my_row + per_side * per_side + per_side + 1) % count_dev
    block_x = block_no // (per_side * per_side)
    block_y = block_no // per_side % per_side
    block_z = block_no % per_side
    classes = perm_class[0]
    width_x, width_y, width_z = classes.shape
    permeab = jnp.zeros(classes.shape, jnp.float32)
    for number in range(class_values.shape[0]):
        permeab = permeab + jnp.where(classes == number, class_values[number], 0.0)
    row_len = per_side * width_z
    plane = per_side * width_y * row_len
    glob_x = well_cells // plane
    glob_y = well_cells // row_len % (per_side * width_y)
    glob_z = well_cells % row_len
    onehot_x = jnp.where(
        (glob_x - block_x * width_x)[:, None] == jnp.arange(width_x)[None, :],
        well_rates[:, None],
        0.0,
    )
    onehot_y = jnp.where(
        (glob_y - block_y * width_y)[:, None] == jnp.arange(width_y)[None, :], 1.0, 0.0
    ).astype(jnp.float32)
    onehot_z = jnp.where(
        (glob_z - block_z * width_z)[:, None] == jnp.arange(width_z)[None, :], 1.0, 0.0
    ).astype(jnp.float32)
    source = jnp.einsum(
        "wi,wj,wk->ijk", onehot_x, onehot_y, onehot_z, precision=lax.Precision.HIGHEST
    )

    values = guess[0]
    if count_dev * (width_x // 2) * (width_y // 2) <= 512:
        first = exchange(jnp.stack([permeab, values]), per_side)
        face_coefs, diagonal = coefficients(permeab, with_faces(permeab, pick(first, 0)), 1.0)
        values = smooth(values, source, face_coefs, diagonal, 1.0, with_faces(values, pick(first, 1)))
        for sweep_no in range(SWEEPS - 1):
            faces = pick(exchange(values[None], per_side), 0)
            values = smooth(values, source, face_coefs, diagonal, 1.0, with_faces(values, faces))
        stored_faces = pick(exchange(values[None], per_side), 0)
        leftover = source - operate(values, with_faces(values, stored_faces), face_coefs, 1.0)
        stored = values

        gathered = gather_rows(jnp.stack([coarsen(permeab), coarsen(leftover)]), per_side)
        correction_all = global_cycle(gathered[:, 1], gathered[:, 0], 1, per_side)

        correction = lax.dynamic_index_in_dim(correction_all, my_row, 0, keepdims=False)
        values = stored + refine(correction)
        faces = [
            mine + theirs
            for mine, theirs in zip(stored_faces, refined_faces(correction_all, my_row, per_side))
        ]
        values = smooth(values, source, face_coefs, diagonal, 1.0, with_faces(values, faces))
        for sweep_no in range(SWEEPS - 1):
            faces = pick(exchange(values[None], per_side), 0)
            values = smooth(values, source, face_coefs, diagonal, 1.0, with_faces(values, faces))
        faces = pick(exchange(values[None], per_side), 0)
        residual = source - operate(values, with_faces(values, faces), face_coefs, 1.0)
        return (values[None], residual[None])

    coarse_perm = coarsen(permeab)
    first, coarse_first = exchange_with_coarse(jnp.stack([permeab, values]), coarse_perm, per_side)
    face_coefs, diagonal = coefficients(permeab, with_faces(permeab, pick(first, 0)), 1.0)
    values = smooth(values, source, face_coefs, diagonal, 1.0, with_faces(values, pick(first, 1)))
    for sweep_no in range(SWEEPS - 1):
        faces = pick(exchange(values[None], per_side), 0)
        values = smooth(values, source, face_coefs, diagonal, 1.0, with_faces(values, faces))
    stored_faces = pick(exchange(values[None], per_side), 0)
    leftover = source - operate(values, with_faces(values, stored_faces), face_coefs, 1.0)
    stored = values

    scaling = 0.25
    right_1 = coarsen(leftover)
    coefs_1, diagonal_1 = coefficients(coarse_perm, with_faces(coarse_perm, coarse_first), scaling)
    values_1 = OMEGA * right_1 / diagonal_1
    for sweep_no in range(SWEEPS - 1):
        faces = pick(exchange(values_1[None], per_side), 0)
        values_1 = smooth(values_1, right_1, coefs_1, diagonal_1, scaling, with_faces(values_1, faces))
    stored_faces_1 = pick(exchange(values_1[None], per_side), 0)
    leftover_1 = right_1 - operate(values_1, with_faces(values_1, stored_faces_1), coefs_1, scaling)
    stored_1 = values_1

    gathered = gather_rows(jnp.stack([coarsen(coarse_perm), coarsen(leftover_1)]), per_side)
    correction_all = global_cycle(gathered[:, 1], gathered[:, 0], 2, per_side)

    correction = lax.dynamic_index_in_dim(correction_all, my_row, 0, keepdims=False)
    values_1 = stored_1 + refine(correction)
    faces = [
        mine + theirs
        for mine, theirs in zip(stored_faces_1, refined_faces(correction_all, my_row, per_side))
    ]
    values_1 = smooth(values_1, right_1, coefs_1, diagonal_1, scaling, with_faces(values_1, faces))
    for sweep_no in range(SWEEPS - 1):
        faces = pick(exchange(values_1[None], per_side), 0)
        values_1 = smooth(values_1, right_1, coefs_1, diagonal_1, scaling, with_faces(values_1, faces))
    coarse_faces = pick(exchange(values_1[None], per_side), 0)

    values = stored + refine(values_1)
    faces = [mine + refine_face_of(theirs) for mine, theirs in zip(stored_faces, coarse_faces)]
    values = smooth(values, source, face_coefs, diagonal, 1.0, with_faces(values, faces))
    for sweep_no in range(SWEEPS - 1):
        faces = pick(exchange(values[None], per_side), 0)
        values = smooth(values, source, face_coefs, diagonal, 1.0, with_faces(values, faces))
    faces = pick(exchange(values[None], per_side), 0)
    residual = source - operate(values, with_faces(values, faces), face_coefs, 1.0)
    return (values[None], residual[None])


def solution(mesh):
    return jax.shard_map(
        shards,
        mesh=mesh,
        in_specs=(
            P("space", None, None, None),
            P(),
            P("real"),
            P("real"),
            P(("real", "space"), None, None, None),
        ),
        out_specs=(P(("real", "space"), None, None, None), P(("real", "space"), None, None, None)),
        check_vma=False,
    )
```

```python
import jax
import jax.numpy as jnp
from jax import lax
from jax.sharding import PartitionSpec as P

LEVELS = 3
SWEEPS = 2
CSWEEPS = 6


OMEGA = 0.8


def shifted(shard, axis, by):
    peers = lax.axis_size(axis)
    return lax.ppermute(shard, axis, [(i, (i + by) % peers) for i in range(peers)])


def exchange(fields, per_side):
    count_dev = lax.axis_size("space")
    plane_step = per_side * per_side

    def stack(number):
        return jnp.stack([own_faces(values)[number] for values in fields])

    if (2 * plane_step) % count_dev == 0:
        both_x = shifted(jnp.concatenate([stack(0), stack(1)], axis=1), "space", plane_step)
        lower_x, upper_x = both_x[:, :1], both_x[:, 1:]
    else:
        lower_x = shifted(stack(0), "space", plane_step)
        upper_x = shifted(stack(1), "space", -plane_step)
    lower_y = shifted(stack(2), "space", per_side)
    upper_y = shifted(stack(3), "space", -per_side)
    lower_z = shifted(stack(4), "space", 1)
    upper_z = shifted(stack(5), "space", -1)
    return [lower_x, upper_x, lower_y, upper_y, lower_z, upper_z]


def own_faces(values):
    return [values[-1:], values[:1], values[:, -1:], values[:, :1], values[:, :, -1:], values[:, :, :1]]


def exchange_mixed(fields, per_side):
    count_dev = lax.axis_size("space")
    plane_step = per_side * per_side
    outgoing = [own_faces(values) for values in fields]
    shifts = [plane_step, -plane_step, per_side, -per_side, 1, -1]
    flat = [jnp.concatenate([faces[d].reshape(-1) for faces in outgoing]) for d in range(6)]
    received = [None] * 6
    if (2 * plane_step) % count_dev == 0:
        both = shifted(jnp.concatenate([flat[0], flat[1]]), "space", plane_step)
        received[0], received[1] = both[: flat[0].shape[0]], both[flat[0].shape[0] :]
        rest = range(2, 6)
    else:
        rest = range(6)
    for d in rest:
        received[d] = shifted(flat[d], "space", shifts[d])
    result = [[None] * 6 for _ in fields]
    for d in range(6):
        offset = 0
        for number, faces in enumerate(outgoing):
            size = faces[d].size
            result[number][d] = received[d][offset : offset + size].reshape(faces[d].shape)
            offset += size
    return result


def exchange_with_coarse(fields, coarse, per_side):
    count_dev = lax.axis_size("space")
    plane_step = per_side * per_side
    size_x, size_y, size_z = fields.shape[1:]
    half_x, half_y, half_z = coarse.shape

    def padded(face):
        pads = [(0, full - part) if part != 1 else (0, 0) for full, part in zip((size_x, size_y, size_z), face.shape)]
        return jnp.pad(face, pads)[None]

    def message(number):
        pieces = [fields[:, -1:], fields[:, :1], fields[:, :, -1:], fields[:, :, :1], fields[:, :, :, -1:], fields[:, :, :, :1]]
        return jnp.concatenate([pieces[number], padded(own_faces(coarse)[number])], axis=0)

    shifts = [plane_step, -plane_step, per_side, -per_side, 1, -1]
    received = [None] * 6
    if (2 * plane_step) % count_dev == 0:
        both = shifted(jnp.concatenate([message(0), message(1)], axis=1), "space", plane_step)
        received[0], received[1] = both[:, :1], both[:, 1:]
        rest = range(2, 6)
    else:
        rest = range(6)
    for number in rest:
        received[number] = shifted(message(number), "space", shifts[number])
    count = fields.shape[0]
    field_faces = [face[:count] for face in received]
    coarse_faces = []
    for number, face in enumerate(received):
        shape = own_faces(coarse)[number].shape
        coarse_faces.append(face[count, : shape[0], : shape[1], : shape[2]])
    return field_faces, coarse_faces


def gather_rows(block, per_side):
    count_dev = lax.axis_size("space")
    if count_dev > 16:
        return lax.all_gather(block[None], "space", axis=0, tiled=True)
    my_row = lax.axis_index("space")
    by_offset = jnp.stack([block] + [shifted(block, "space", k) for k in range(1, count_dev)])
    return jnp.take(by_offset, (my_row - jnp.arange(count_dev)) % count_dev, axis=0)


def pick(faces, number):
    return [face[number] for face in faces]


def with_faces(values, faces):
    lower_x, upper_x, lower_y, upper_y, lower_z, upper_z = faces
    return [
        jnp.concatenate([lower_x, values[:-1]], axis=0),
        jnp.concatenate([values[1:], upper_x], axis=0),
        jnp.concatenate([lower_y, values[:, :-1]], axis=1),
        jnp.concatenate([values[:, 1:], upper_y], axis=1),
        jnp.concatenate([lower_z, values[:, :, :-1]], axis=2),
        jnp.concatenate([values[:, :, 1:], upper_z], axis=2),
    ]


def rolled_faces(values, per_side):
    plane_step = per_side * per_side
    return [
        jnp.concatenate([jnp.roll(values[:, -1:], plane_step, axis=0), values[:, :-1]], axis=1),
        jnp.concatenate([values[:, 1:], jnp.roll(values[:, :1], -plane_step, axis=0)], axis=1),
        jnp.concatenate([jnp.roll(values[:, :, -1:], per_side, axis=0), values[:, :, :-1]], axis=2),
        jnp.concatenate([values[:, :, 1:], jnp.roll(values[:, :, :1], -per_side, axis=0)], axis=2),
        jnp.concatenate([jnp.roll(values[:, :, :, -1:], 1, axis=0), values[:, :, :, :-1]], axis=3),
        jnp.concatenate([values[:, :, :, 1:], jnp.roll(values[:, :, :, :1], -1, axis=0)], axis=3),
    ]


def coefficients(permeab, neighbors, scaling):
    face_coefs = [0.5 * (permeab + beside) for beside in neighbors]
    total_sum = face_coefs[0]
    for number in range(1, 6):
        total_sum = total_sum + face_coefs[number]
    return (face_coefs, scaling * total_sum)


def operate(values, neighbors, face_coefs, scaling):
    total_sum = face_coefs[0] * (values - neighbors[0])
    for number in range(1, 6):
        total_sum = total_sum + face_coefs[number] * (values - neighbors[number])
    return scaling * total_sum


def smooth(values, right_side, face_coefs, diagonal, scaling, neighbors):
    return values + OMEGA * (right_side - operate(values, neighbors, face_coefs, scaling)) / diagonal


def pair_mean(size, scale):
    rows = jnp.arange(size)[:, None] // 2
    cols = jnp.arange(size // 2)[None, :]
    return jnp.where(rows == cols, scale, 0.0).astype(jnp.float32)


def plane_mean(size_x, size_y):
    fine = jnp.arange(size_x * size_y)
    coarse_of = (fine // size_y // 2) * (size_y // 2) + (fine % size_y) // 2
    return jnp.where(
        jnp.arange(size_x * size_y // 4)[:, None] == coarse_of[None, :], 0.25, 0.0
    ).astype(jnp.float32)


def coarsen(values):
    size_x, size_y, size_z = values.shape
    along_z = jnp.dot(
        values.reshape(size_x * size_y, size_z),
        pair_mean(size_z, 0.5),
        precision=lax.Precision.HIGHEST,
    )
    both = jnp.dot(plane_mean(size_x, size_y), along_z, precision=lax.Precision.HIGHEST)
    return both.reshape(size_x // 2, size_y // 2, size_z // 2)


def refine(values):
    return jnp.repeat(jnp.repeat(jnp.repeat(values, 2, axis=0), 2, axis=1), 2, axis=2)


def coarsen_all(values):
    count_b, size_x, size_y, size_z = values.shape
    along_z = jnp.dot(
        values.reshape(count_b * size_x * size_y, size_z),
        pair_mean(size_z, 0.5),
        precision=lax.Precision.HIGHEST,
    ).reshape(count_b, size_x * size_y, size_z // 2)
    both = jnp.einsum(
        "pq,bqz->bpz", plane_mean(size_x, size_y), along_z, precision=lax.Precision.HIGHEST
    )
    return both.reshape(count_b, size_x // 2, size_y // 2, size_z // 2)


def refine_all(values):
    return jnp.repeat(jnp.repeat(jnp.repeat(values, 2, axis=1), 2, axis=2), 2, axis=3)


def refine_face(face):
    return jnp.repeat(jnp.repeat(face, 2, axis=0), 2, axis=1)


def refine_face_of(face):
    for axis in range(3):
        if face.shape[axis] != 1:
            face = jnp.repeat(face, 2, axis=axis)
    return face


def refined_faces(coarse_all, my_row, per_side):
    count_b = coarse_all.shape[0]

    def row(offset):
        return lax.dynamic_index_in_dim(coarse_all, (my_row + offset) % count_b, 0, keepdims=False)

    plane_step = per_side * per_side
    return [
        refine_face(row(-plane_step)[-1])[None],
        refine_face(row(plane_step)[0])[None],
        refine_face(row(-per_side)[:, -1])[:, None],
        refine_face(row(per_side)[:, 0])[:, None],
        refine_face(row(-1)[:, :, -1])[:, :, None],
        refine_face(row(1)[:, :, 0])[:, :, None],
    ]


def neighbour_rows(count_b, size_x, size_y, per_side):
    count_r = count_b * size_x * size_y
    index = jnp.arange(count_r)
    row = index // (size_x * size_y)
    at_x = index // size_y % size_x
    at_y = index % size_y
    plane_step = per_side * per_side
    picks = []
    for axis_no, (size, step) in enumerate(((size_x, plane_step), (size_y, per_side))):
        coord = at_x if axis_no == 0 else at_y
        for sign in (-1, 1):
            edge = size - 1 if sign > 0 else 0
            moved = jnp.where(coord == edge, size - 1 - edge, coord + sign)
            new_row = jnp.where(coord == edge, (row + sign * step) % count_b, row)
            if axis_no == 0:
                picks.append((new_row * size_x + moved) * size_y + at_y)
            else:
                picks.append((new_row * size_x + at_x) * size_y + moved)
    for sign in (-1, 1):
        picks.append((((row + sign) % count_b) * size_x + at_x) * size_y + at_y)
    target = jnp.concatenate(picks)
    return jnp.where(target[:, None] == index[None, :], 1.0, 0.0).astype(jnp.bfloat16)


def lane_shift(size_z, sign):
    lanes_in = jnp.arange(size_z)[:, None]
    lanes_out = jnp.arange(size_z)[None, :]
    inner = jnp.where(lanes_in == lanes_out + sign, 1.0, 0.0)
    edge_in, edge_out = (size_z - 1, 0) if sign < 0 else (0, size_z - 1)
    wrap = jnp.where((lanes_in == edge_in) & (lanes_out == edge_out), 1.0, 0.0)
    return jnp.concatenate([inner, wrap]).astype(jnp.bfloat16)


def split3(values):
    pieces = []
    rest = values
    for piece_no in range(3):
        piece = lax.reduce_precision(rest, exponent_bits=8, mantissa_bits=7)
        pieces.append(piece.astype(jnp.bfloat16))
        rest = rest - piece
    return pieces


def pick_rows(picker, values):
    size_z = values.shape[1]
    joined = jnp.concatenate(split3(values), axis=1)
    out = jnp.dot(picker, joined, preferred_element_type=jnp.float32)
    return (out[:, :size_z] + out[:, size_z : 2 * size_z]) + out[:, 2 * size_z :]


def pick_lanes(values, shift):
    count_r = values.shape[0]
    stacked = jnp.concatenate(split3(values), axis=0)
    out = jnp.dot(stacked, shift, preferred_element_type=jnp.float32)
    return (out[:count_r] + out[count_r : 2 * count_r]) + out[2 * count_r :]


def flat_faces(values, picker, lower_z, upper_z):
    count_r, size_z = values.shape
    rows = pick_rows(picker, values)
    shifts = jnp.concatenate(
        [lower_z[:size_z], upper_z[:size_z], lower_z[size_z:], upper_z[size_z:]], axis=1
    )
    out = pick_lanes(jnp.concatenate([values, rows[4 * count_r :]], axis=0), shifts)
    lower = out[:count_r, :size_z] + out[count_r : 2 * count_r, 2 * size_z : 3 * size_z]
    upper = out[:count_r, size_z : 2 * size_z] + out[2 * count_r :, 3 * size_z :]
    return [rows[k * count_r : (k + 1) * count_r] for k in range(4)] + [lower, upper]


def row_mean(count_b, size_x, size_y):
    index = jnp.arange(count_b * size_x * size_y)
    row = index // (size_x * size_y)
    coarse_of = (row * (size_x // 2) + index // size_y % size_x // 2) * (size_y // 2) + index % size_y // 2
    return jnp.where(
        jnp.arange(count_b * size_x * size_y // 4)[:, None] == coarse_of[None, :], 0.25, 0.0
    ).astype(jnp.float32)


def global_cycle(all_rhs, all_perm, first_level, per_side):
    count_b, size_x, size_y, size_z = all_rhs.shape
    shapes = [(size_x >> n, size_y >> n, size_z >> n) for n in range(LEVELS - first_level + 1)]
    pickers = [neighbour_rows(count_b, sx, sy, per_side) for sx, sy, sz in shapes]
    shifts = [(lane_shift(sz, -1), lane_shift(sz, 1)) for sx, sy, sz in shapes]
    means = [(row_mean(count_b, sx, sy), pair_mean(sz, 0.5)) for sx, sy, sz in shapes[:-1]]

    def faces(values, number):
        return flat_faces(values, pickers[number], *shifts[number])

    def down(values, number):
        rows, lanes = means[number]
        return jnp.dot(
            rows,
            jnp.dot(values, lanes, precision=lax.Precision.HIGHEST),
            precision=lax.Precision.HIGHEST,
        )

    def up(values, number):
        rows, lanes = means[number]
        return jnp.dot(
            rows.T * 4.0,
            jnp.dot(values, lanes.T * 2.0, precision=lax.Precision.HIGHEST),
            precision=lax.Precision.HIGHEST,
        )

    perms = [all_perm.reshape(-1, size_z)]
    for number in range(LEVELS - first_level):
        perms.append(down(perms[-1], number))
    coefs = [
        coefficients(perms[number], faces(perms[number], number), 0.25 ** (first_level + number))
        for number in range(LEVELS - first_level + 1)
    ]
    right_side = all_rhs.reshape(-1, size_z)
    stored = []
    rights = []
    for number in range(LEVELS - first_level):
        face_coefs, diagonal = coefs[number]
        scaling = 0.25 ** (first_level + number)
        values = OMEGA * right_side / diagonal
        for sweep_no in range(SWEEPS - 1):
            values = smooth(values, right_side, face_coefs, diagonal, scaling, faces(values, number))
        leftover = right_side - operate(values, faces(values, number), face_coefs, scaling)
        stored.append(values)
        rights.append(right_side)
        right_side = down(leftover, number)
    last = LEVELS - first_level
    face_coefs, diagonal = coefs[last]
    scaling = 0.25**LEVELS
    correction = OMEGA * right_side / diagonal
    for sweep_no in range(CSWEEPS - 1):
        correction = smooth(
            correction, right_side, face_coefs, diagonal, scaling, faces(correction, last)
        )
    for number in reversed(range(LEVELS - first_level)):
        face_coefs, diagonal = coefs[number]
        scaling = 0.25 ** (first_level + number)
        values = stored[number] + up(correction, number)
        for sweep_no in range(SWEEPS):
            values = smooth(
                values, rights[number], face_coefs, diagonal, scaling, faces(values, number)
            )
        correction = values
    return correction.reshape(count_b, size_x, size_y, size_z)


def shards(perm_class, class_values, well_cells, well_rates, guess):
    count_dev = lax.axis_size("space")
    per_side = 2 + 2 * (count_dev // 64)
    my_row = lax.axis_index("space")
    block_no = (my_row + per_side * per_side + per_side + 1) % count_dev
    block_x = block_no // (per_side * per_side)
    block_y = block_no // per_side % per_side
    block_z = block_no % per_side
    classes = perm_class[0]
    width_x, width_y, width_z = classes.shape
    permeab = jnp.zeros(classes.shape, jnp.float32)
    for number in range(class_values.shape[0]):
        permeab = permeab + jnp.where(classes == number, class_values[number], 0.0)
    row_len = per_side * width_z
    plane = per_side * width_y * row_len
    glob_x = well_cells // plane
    glob_y = well_cells // row_len % (per_side * width_y)
    glob_z = well_cells % row_len
    onehot_x = jnp.where(
        (glob_x - block_x * width_x)[:, None] == jnp.arange(width_x)[None, :],
        well_rates[:, None],
        0.0,
    )
    onehot_y = jnp.where(
        (glob_y - block_y * width_y)[:, None] == jnp.arange(width_y)[None, :], 1.0, 0.0
    ).astype(jnp.float32)
    onehot_z = jnp.where(
        (glob_z - block_z * width_z)[:, None] == jnp.arange(width_z)[None, :], 1.0, 0.0
    ).astype(jnp.float32)
    source = jnp.einsum(
        "wi,wj,wk->ijk", onehot_x, onehot_y, onehot_z, precision=lax.Precision.HIGHEST
    )

    values = guess[0]
    if count_dev * (width_x // 2) * (width_y // 2) <= 512:
        first = exchange([permeab, values], per_side)
        face_coefs, diagonal = coefficients(permeab, with_faces(permeab, pick(first, 0)), 1.0)
        values = smooth(values, source, face_coefs, diagonal, 1.0, with_faces(values, pick(first, 1)))
        for sweep_no in range(SWEEPS - 1):
            faces = pick(exchange([values], per_side), 0)
            values = smooth(values, source, face_coefs, diagonal, 1.0, with_faces(values, faces))
        stored_faces = pick(exchange([values], per_side), 0)
        leftover = source - operate(values, with_faces(values, stored_faces), face_coefs, 1.0)
        stored = values

        gathered = gather_rows(jnp.stack([coarsen(permeab), coarsen(leftover)]), per_side)
        correction_all = global_cycle(gathered[:, 1], gathered[:, 0], 1, per_side)

        correction = lax.dynamic_index_in_dim(correction_all, my_row, 0, keepdims=False)
        values = stored + refine(correction)
        faces = [
            mine + theirs
            for mine, theirs in zip(stored_faces, refined_faces(correction_all, my_row, per_side))
        ]
        values = smooth(values, source, face_coefs, diagonal, 1.0, with_faces(values, faces))
        for sweep_no in range(SWEEPS - 1):
            faces = pick(exchange([values], per_side), 0)
            values = smooth(values, source, face_coefs, diagonal, 1.0, with_faces(values, faces))
        faces = pick(exchange([values], per_side), 0)
        residual = source - operate(values, with_faces(values, faces), face_coefs, 1.0)
        return (values[None], residual[None])

    coarse_perm = coarsen(permeab)
    first, coarse_first = exchange_with_coarse(jnp.stack([permeab, values]), coarse_perm, per_side)
    face_coefs, diagonal = coefficients(permeab, with_faces(permeab, pick(first, 0)), 1.0)
    values = smooth(values, source, face_coefs, diagonal, 1.0, with_faces(values, pick(first, 1)))
    for sweep_no in range(SWEEPS - 1):
        faces = pick(exchange([values], per_side), 0)
        values = smooth(values, source, face_coefs, diagonal, 1.0, with_faces(values, faces))
    stored_faces = pick(exchange([values], per_side), 0)
    leftover = source - operate(values, with_faces(values, stored_faces), face_coefs, 1.0)
    stored = values

    scaling = 0.25
    right_1 = coarsen(leftover)
    coefs_1, diagonal_1 = coefficients(coarse_perm, with_faces(coarse_perm, coarse_first), scaling)
    values_1 = OMEGA * right_1 / diagonal_1
    for sweep_no in range(SWEEPS - 1):
        faces = pick(exchange([values_1], per_side), 0)
        values_1 = smooth(values_1, right_1, coefs_1, diagonal_1, scaling, with_faces(values_1, faces))
    stored_faces_1 = pick(exchange([values_1], per_side), 0)
    leftover_1 = right_1 - operate(values_1, with_faces(values_1, stored_faces_1), coefs_1, scaling)
    stored_1 = values_1

    gathered = gather_rows(jnp.stack([coarsen(coarse_perm), coarsen(leftover_1)]), per_side)
    correction_all = global_cycle(gathered[:, 1], gathered[:, 0], 2, per_side)

    correction = lax.dynamic_index_in_dim(correction_all, my_row, 0, keepdims=False)
    values_1 = stored_1 + refine(correction)
    faces = [
        mine + theirs
        for mine, theirs in zip(stored_faces_1, refined_faces(correction_all, my_row, per_side))
    ]
    values_1 = smooth(values_1, right_1, coefs_1, diagonal_1, scaling, with_faces(values_1, faces))
    for sweep_no in range(SWEEPS - 1):
        faces = pick(exchange([values_1], per_side), 0)
        values_1 = smooth(values_1, right_1, coefs_1, diagonal_1, scaling, with_faces(values_1, faces))
    coarse_faces = pick(exchange([values_1], per_side), 0)

    values = stored + refine(values_1)
    faces = [mine + refine_face_of(theirs) for mine, theirs in zip(stored_faces, coarse_faces)]
    values = smooth(values, source, face_coefs, diagonal, 1.0, with_faces(values, faces))
    for sweep_no in range(SWEEPS - 1):
        faces = pick(exchange([values], per_side), 0)
        values = smooth(values, source, face_coefs, diagonal, 1.0, with_faces(values, faces))
    faces = pick(exchange([values], per_side), 0)
    residual = source - operate(values, with_faces(values, faces), face_coefs, 1.0)
    return (values[None], residual[None])


def solution(mesh):
    return jax.shard_map(
        shards,
        mesh=mesh,
        in_specs=(
            P("space", None, None, None),
            P(),
            P("real"),
            P("real"),
            P(("real", "space"), None, None, None),
        ),
        out_specs=(P(("real", "space"), None, None, None), P(("real", "space"), None, None, None)),
        check_vma=False,
    )
```

```python
import jax
import jax.numpy as jnp
from jax import lax
from jax.sharding import PartitionSpec as P

LEVELS = 3
SWEEPS = 2
CSWEEPS = 6


OMEGA = 0.8


def shifted(shard, axis, by):
    peers = lax.axis_size(axis)
    return lax.ppermute(shard, axis, [(i, (i + by) % peers) for i in range(peers)])


def exchange(fields, per_side):
    count_dev = lax.axis_size("space")
    plane_step = per_side * per_side

    def stack(number):
        return jnp.stack([own_faces(values)[number] for values in fields])

    if (2 * plane_step) % count_dev == 0:
        both_x = shifted(jnp.concatenate([stack(0), stack(1)], axis=1), "space", plane_step)
        lower_x, upper_x = both_x[:, :1], both_x[:, 1:]
    else:
        lower_x = shifted(stack(0), "space", plane_step)
        upper_x = shifted(stack(1), "space", -plane_step)
    lower_y = shifted(stack(2), "space", per_side)
    upper_y = shifted(stack(3), "space", -per_side)
    lower_z = shifted(stack(4), "space", 1)
    upper_z = shifted(stack(5), "space", -1)
    return [lower_x, upper_x, lower_y, upper_y, lower_z, upper_z]


def own_faces(values):
    return [values[-1:], values[:1], values[:, -1:], values[:, :1], values[:, :, -1:], values[:, :, :1]]


def exchange_mixed(fields, per_side):
    count_dev = lax.axis_size("space")
    plane_step = per_side * per_side
    outgoing = [own_faces(values) for values in fields]
    shifts = [plane_step, -plane_step, per_side, -per_side, 1, -1]
    flat = [jnp.concatenate([faces[d].reshape(-1) for faces in outgoing]) for d in range(6)]
    received = [None] * 6
    if (2 * plane_step) % count_dev == 0:
        both = shifted(jnp.concatenate([flat[0], flat[1]]), "space", plane_step)
        received[0], received[1] = both[: flat[0].shape[0]], both[flat[0].shape[0] :]
        rest = range(2, 6)
    else:
        rest = range(6)
    for d in rest:
        received[d] = shifted(flat[d], "space", shifts[d])
    result = [[None] * 6 for _ in fields]
    for d in range(6):
        offset = 0
        for number, faces in enumerate(outgoing):
            size = faces[d].size
            result[number][d] = received[d][offset : offset + size].reshape(faces[d].shape)
            offset += size
    return result


def exchange_with_coarse(fields, coarse, per_side):
    count_dev = lax.axis_size("space")
    plane_step = per_side * per_side
    size_x, size_y, size_z = fields.shape[1:]
    half_x, half_y, half_z = coarse.shape

    def padded(face):
        pads = [(0, full - part) if part != 1 else (0, 0) for full, part in zip((size_x, size_y, size_z), face.shape)]
        return jnp.pad(face, pads)[None]

    def message(number):
        pieces = [fields[:, -1:], fields[:, :1], fields[:, :, -1:], fields[:, :, :1], fields[:, :, :, -1:], fields[:, :, :, :1]]
        return jnp.concatenate([pieces[number], padded(own_faces(coarse)[number])], axis=0)

    shifts = [plane_step, -plane_step, per_side, -per_side, 1, -1]
    received = [None] * 6
    if (2 * plane_step) % count_dev == 0:
        both = shifted(jnp.concatenate([message(0), message(1)], axis=1), "space", plane_step)
        received[0], received[1] = both[:, :1], both[:, 1:]
        rest = range(2, 6)
    else:
        rest = range(6)
    for number in rest:
        received[number] = shifted(message(number), "space", shifts[number])
    count = fields.shape[0]
    field_faces = [face[:count] for face in received]
    coarse_faces = []
    for number, face in enumerate(received):
        shape = own_faces(coarse)[number].shape
        coarse_faces.append(face[count, : shape[0], : shape[1], : shape[2]])
    return field_faces, coarse_faces


def gather_rows(block, per_side):
    count_dev = lax.axis_size("space")
    if count_dev > 16:
        return lax.all_gather(block[None], "space", axis=0, tiled=True)
    copies = jnp.broadcast_to(block[None], (count_dev,) + block.shape)
    return lax.all_to_all(copies, "space", 0, 0, tiled=True)


def pick(faces, number):
    return [face[number] for face in faces]


def with_faces(values, faces):
    lower_x, upper_x, lower_y, upper_y, lower_z, upper_z = faces
    return [
        jnp.concatenate([lower_x, values[:-1]], axis=0),
        jnp.concatenate([values[1:], upper_x], axis=0),
        jnp.concatenate([lower_y, values[:, :-1]], axis=1),
        jnp.concatenate([values[:, 1:], upper_y], axis=1),
        jnp.concatenate([lower_z, values[:, :, :-1]], axis=2),
        jnp.concatenate([values[:, :, 1:], upper_z], axis=2),
    ]


def rolled_faces(values, per_side):
    plane_step = per_side * per_side
    return [
        jnp.concatenate([jnp.roll(values[:, -1:], plane_step, axis=0), values[:, :-1]], axis=1),
        jnp.concatenate([values[:, 1:], jnp.roll(values[:, :1], -plane_step, axis=0)], axis=1),
        jnp.concatenate([jnp.roll(values[:, :, -1:], per_side, axis=0), values[:, :, :-1]], axis=2),
        jnp.concatenate([values[:, :, 1:], jnp.roll(values[:, :, :1], -per_side, axis=0)], axis=2),
        jnp.concatenate([jnp.roll(values[:, :, :, -1:], 1, axis=0), values[:, :, :, :-1]], axis=3),
        jnp.concatenate([values[:, :, :, 1:], jnp.roll(values[:, :, :, :1], -1, axis=0)], axis=3),
    ]


def coefficients(permeab, neighbors, scaling):
    face_coefs = [0.5 * (permeab + beside) for beside in neighbors]
    total_sum = face_coefs[0]
    for number in range(1, 6):
        total_sum = total_sum + face_coefs[number]
    return (face_coefs, scaling * total_sum)


def operate(values, neighbors, face_coefs, scaling):
    total_sum = face_coefs[0] * (values - neighbors[0])
    for number in range(1, 6):
        total_sum = total_sum + face_coefs[number] * (values - neighbors[number])
    return scaling * total_sum


def smooth(values, right_side, face_coefs, diagonal, scaling, neighbors):
    return values + OMEGA * (right_side - operate(values, neighbors, face_coefs, scaling)) / diagonal


def pair_mean(size, scale):
    rows = jnp.arange(size)[:, None] // 2
    cols = jnp.arange(size // 2)[None, :]
    return jnp.where(rows == cols, scale, 0.0).astype(jnp.float32)


def plane_mean(size_x, size_y):
    fine = jnp.arange(size_x * size_y)
    coarse_of = (fine // size_y // 2) * (size_y // 2) + (fine % size_y) // 2
    return jnp.where(
        jnp.arange(size_x * size_y // 4)[:, None] == coarse_of[None, :], 0.25, 0.0
    ).astype(jnp.float32)


def coarsen(values):
    size_x, size_y, size_z = values.shape
    along_z = jnp.dot(
        values.reshape(size_x * size_y, size_z),
        pair_mean(size_z, 0.5),
        precision=lax.Precision.HIGHEST,
    )
    both = jnp.dot(plane_mean(size_x, size_y), along_z, precision=lax.Precision.HIGHEST)
    return both.reshape(size_x // 2, size_y // 2, size_z // 2)


def refine(values):
    return jnp.repeat(jnp.repeat(jnp.repeat(values, 2, axis=0), 2, axis=1), 2, axis=2)


def coarsen_all(values):
    count_b, size_x, size_y, size_z = values.shape
    along_z = jnp.dot(
        values.reshape(count_b * size_x * size_y, size_z),
        pair_mean(size_z, 0.5),
        precision=lax.Precision.HIGHEST,
    ).reshape(count_b, size_x * size_y, size_z // 2)
    both = jnp.einsum(
        "pq,bqz->bpz", plane_mean(size_x, size_y), along_z, precision=lax.Precision.HIGHEST
    )
    return both.reshape(count_b, size_x // 2, size_y // 2, size_z // 2)


def refine_all(values):
    return jnp.repeat(jnp.repeat(jnp.repeat(values, 2, axis=1), 2, axis=2), 2, axis=3)


def refine_face(face):
    return jnp.repeat(jnp.repeat(face, 2, axis=0), 2, axis=1)


def refine_face_of(face):
    for axis in range(3):
        if face.shape[axis] != 1:
            face = jnp.repeat(face, 2, axis=axis)
    return face


def refined_faces(coarse_all, my_row, per_side):
    count_b = coarse_all.shape[0]

    def row(offset):
        return lax.dynamic_index_in_dim(coarse_all, (my_row + offset) % count_b, 0, keepdims=False)

    plane_step = per_side * per_side
    return [
        refine_face(row(-plane_step)[-1])[None],
        refine_face(row(plane_step)[0])[None],
        refine_face(row(-per_side)[:, -1])[:, None],
        refine_face(row(per_side)[:, 0])[:, None],
        refine_face(row(-1)[:, :, -1])[:, :, None],
        refine_face(row(1)[:, :, 0])[:, :, None],
    ]


def neighbour_rows(count_b, size_x, size_y, per_side):
    count_r = count_b * size_x * size_y
    index = jnp.arange(count_r)
    row = index // (size_x * size_y)
    at_x = index // size_y % size_x
    at_y = index % size_y
    plane_step = per_side * per_side
    picks = []
    for axis_no, (size, step) in enumerate(((size_x, plane_step), (size_y, per_side))):
        coord = at_x if axis_no == 0 else at_y
        for sign in (-1, 1):
            edge = size - 1 if sign > 0 else 0
            moved = jnp.where(coord == edge, size - 1 - edge, coord + sign)
            new_row = jnp.where(coord == edge, (row + sign * step) % count_b, row)
            if axis_no == 0:
                picks.append((new_row * size_x + moved) * size_y + at_y)
            else:
                picks.append((new_row * size_x + at_x) * size_y + moved)
    for sign in (-1, 1):
        picks.append((((row + sign) % count_b) * size_x + at_x) * size_y + at_y)
    target = jnp.concatenate(picks)
    return jnp.where(target[:, None] == index[None, :], 1.0, 0.0).astype(jnp.bfloat16)


def lane_shift(size_z, sign):
    lanes_in = jnp.arange(size_z)[:, None]
    lanes_out = jnp.arange(size_z)[None, :]
    inner = jnp.where(lanes_in == lanes_out + sign, 1.0, 0.0)
    edge_in, edge_out = (size_z - 1, 0) if sign < 0 else (0, size_z - 1)
    wrap = jnp.where((lanes_in == edge_in) & (lanes_out == edge_out), 1.0, 0.0)
    return jnp.concatenate([inner, wrap]).astype(jnp.bfloat16)


def split3(values):
    pieces = []
    rest = values
    for piece_no in range(3):
        piece = lax.reduce_precision(rest, exponent_bits=8, mantissa_bits=7)
        pieces.append(piece.astype(jnp.bfloat16))
        rest = rest - piece
    return pieces


def pick_rows(picker, values):
    size_z = values.shape[1]
    joined = jnp.concatenate(split3(values), axis=1)
    out = jnp.dot(picker, joined, preferred_element_type=jnp.float32)
    return (out[:, :size_z] + out[:, size_z : 2 * size_z]) + out[:, 2 * size_z :]


def pick_lanes(values, shift):
    count_r = values.shape[0]
    stacked = jnp.concatenate(split3(values), axis=0)
    out = jnp.dot(stacked, shift, preferred_element_type=jnp.float32)
    return (out[:count_r] + out[count_r : 2 * count_r]) + out[2 * count_r :]


def flat_faces(values, picker, lower_z, upper_z):
    count_r, size_z = values.shape
    rows = pick_rows(picker, values)
    shifts = jnp.concatenate(
        [lower_z[:size_z], upper_z[:size_z], lower_z[size_z:], upper_z[size_z:]], axis=1
    )
    out = pick_lanes(jnp.concatenate([values, rows[4 * count_r :]], axis=0), shifts)
    lower = out[:count_r, :size_z] + out[count_r : 2 * count_r, 2 * size_z : 3 * size_z]
    upper = out[:count_r, size_z : 2 * size_z] + out[2 * count_r :, 3 * size_z :]
    return [rows[k * count_r : (k + 1) * count_r] for k in range(4)] + [lower, upper]


def row_mean(count_b, size_x, size_y):
    index = jnp.arange(count_b * size_x * size_y)
    row = index // (size_x * size_y)
    coarse_of = (row * (size_x // 2) + index // size_y % size_x // 2) * (size_y // 2) + index % size_y // 2
    return jnp.where(
        jnp.arange(count_b * size_x * size_y // 4)[:, None] == coarse_of[None, :], 0.25, 0.0
    ).astype(jnp.float32)


def global_cycle(all_rhs, all_perm, first_level, per_side):
    count_b, size_x, size_y, size_z = all_rhs.shape
    shapes = [(size_x >> n, size_y >> n, size_z >> n) for n in range(LEVELS - first_level + 1)]
    pickers = [neighbour_rows(count_b, sx, sy, per_side) for sx, sy, sz in shapes]
    shifts = [(lane_shift(sz, -1), lane_shift(sz, 1)) for sx, sy, sz in shapes]
    means = [(row_mean(count_b, sx, sy), pair_mean(sz, 0.5)) for sx, sy, sz in shapes[:-1]]

    def faces(values, number):
        return flat_faces(values, pickers[number], *shifts[number])

    def down(values, number):
        rows, lanes = means[number]
        return jnp.dot(
            rows,
            jnp.dot(values, lanes, precision=lax.Precision.HIGHEST),
            precision=lax.Precision.HIGHEST,
        )

    def up(values, number):
        rows, lanes = means[number]
        return jnp.dot(
            rows.T * 4.0,
            jnp.dot(values, lanes.T * 2.0, precision=lax.Precision.HIGHEST),
            precision=lax.Precision.HIGHEST,
        )

    perms = [all_perm.reshape(-1, size_z)]
    for number in range(LEVELS - first_level):
        perms.append(down(perms[-1], number))
    coefs = [
        coefficients(perms[number], faces(perms[number], number), 0.25 ** (first_level + number))
        for number in range(LEVELS - first_level + 1)
    ]
    right_side = all_rhs.reshape(-1, size_z)
    stored = []
    rights = []
    for number in range(LEVELS - first_level):
        face_coefs, diagonal = coefs[number]
        scaling = 0.25 ** (first_level + number)
        values = OMEGA * right_side / diagonal
        for sweep_no in range(SWEEPS - 1):
            values = smooth(values, right_side, face_coefs, diagonal, scaling, faces(values, number))
        leftover = right_side - operate(values, faces(values, number), face_coefs, scaling)
        stored.append(values)
        rights.append(right_side)
        right_side = down(leftover, number)
    last = LEVELS - first_level
    face_coefs, diagonal = coefs[last]
    scaling = 0.25**LEVELS
    correction = OMEGA * right_side / diagonal
    for sweep_no in range(CSWEEPS - 1):
        correction = smooth(
            correction, right_side, face_coefs, diagonal, scaling, faces(correction, last)
        )
    for number in reversed(range(LEVELS - first_level)):
        face_coefs, diagonal = coefs[number]
        scaling = 0.25 ** (first_level + number)
        values = stored[number] + up(correction, number)
        for sweep_no in range(SWEEPS):
            values = smooth(
                values, rights[number], face_coefs, diagonal, scaling, faces(values, number)
            )
        correction = values
    return correction.reshape(count_b, size_x, size_y, size_z)


def shards(perm_class, class_values, well_cells, well_rates, guess):
    count_dev = lax.axis_size("space")
    per_side = 2 + 2 * (count_dev // 64)
    my_row = lax.axis_index("space")
    block_no = (my_row + per_side * per_side + per_side + 1) % count_dev
    block_x = block_no // (per_side * per_side)
    block_y = block_no // per_side % per_side
    block_z = block_no % per_side
    classes = perm_class[0]
    width_x, width_y, width_z = classes.shape
    permeab = jnp.zeros(classes.shape, jnp.float32)
    for number in range(class_values.shape[0]):
        permeab = permeab + jnp.where(classes == number, class_values[number], 0.0)
    row_len = per_side * width_z
    plane = per_side * width_y * row_len
    glob_x = well_cells // plane
    glob_y = well_cells // row_len % (per_side * width_y)
    glob_z = well_cells % row_len
    onehot_x = jnp.where(
        (glob_x - block_x * width_x)[:, None] == jnp.arange(width_x)[None, :],
        well_rates[:, None],
        0.0,
    )
    onehot_y = jnp.where(
        (glob_y - block_y * width_y)[:, None] == jnp.arange(width_y)[None, :], 1.0, 0.0
    ).astype(jnp.float32)
    onehot_z = jnp.where(
        (glob_z - block_z * width_z)[:, None] == jnp.arange(width_z)[None, :], 1.0, 0.0
    ).astype(jnp.float32)
    source = jnp.einsum(
        "wi,wj,wk->ijk", onehot_x, onehot_y, onehot_z, precision=lax.Precision.HIGHEST
    )

    values = guess[0]
    if count_dev * (width_x // 2) * (width_y // 2) <= 512:
        first = exchange([permeab, values], per_side)
        face_coefs, diagonal = coefficients(permeab, with_faces(permeab, pick(first, 0)), 1.0)
        values = smooth(values, source, face_coefs, diagonal, 1.0, with_faces(values, pick(first, 1)))
        for sweep_no in range(SWEEPS - 1):
            faces = pick(exchange([values], per_side), 0)
            values = smooth(values, source, face_coefs, diagonal, 1.0, with_faces(values, faces))
        stored_faces = pick(exchange([values], per_side), 0)
        leftover = source - operate(values, with_faces(values, stored_faces), face_coefs, 1.0)
        stored = values

        gathered = gather_rows(jnp.stack([coarsen(permeab), coarsen(leftover)]), per_side)
        correction_all = global_cycle(gathered[:, 1], gathered[:, 0], 1, per_side)

        correction = lax.dynamic_index_in_dim(correction_all, my_row, 0, keepdims=False)
        values = stored + refine(correction)
        faces = [
            mine + theirs
            for mine, theirs in zip(stored_faces, refined_faces(correction_all, my_row, per_side))
        ]
        values = smooth(values, source, face_coefs, diagonal, 1.0, with_faces(values, faces))
        for sweep_no in range(SWEEPS - 1):
            faces = pick(exchange([values], per_side), 0)
            values = smooth(values, source, face_coefs, diagonal, 1.0, with_faces(values, faces))
        faces = pick(exchange([values], per_side), 0)
        residual = source - operate(values, with_faces(values, faces), face_coefs, 1.0)
        return (values[None], residual[None])

    coarse_perm = coarsen(permeab)
    first, coarse_first = exchange_with_coarse(jnp.stack([permeab, values]), coarse_perm, per_side)
    face_coefs, diagonal = coefficients(permeab, with_faces(permeab, pick(first, 0)), 1.0)
    values = smooth(values, source, face_coefs, diagonal, 1.0, with_faces(values, pick(first, 1)))
    for sweep_no in range(SWEEPS - 1):
        faces = pick(exchange([values], per_side), 0)
        values = smooth(values, source, face_coefs, diagonal, 1.0, with_faces(values, faces))
    stored_faces = pick(exchange([values], per_side), 0)
    leftover = source - operate(values, with_faces(values, stored_faces), face_coefs, 1.0)
    stored = values

    scaling = 0.25
    right_1 = coarsen(leftover)
    coefs_1, diagonal_1 = coefficients(coarse_perm, with_faces(coarse_perm, coarse_first), scaling)
    values_1 = OMEGA * right_1 / diagonal_1
    for sweep_no in range(SWEEPS - 1):
        faces = pick(exchange([values_1], per_side), 0)
        values_1 = smooth(values_1, right_1, coefs_1, diagonal_1, scaling, with_faces(values_1, faces))
    stored_faces_1 = pick(exchange([values_1], per_side), 0)
    leftover_1 = right_1 - operate(values_1, with_faces(values_1, stored_faces_1), coefs_1, scaling)
    stored_1 = values_1

    gathered = gather_rows(jnp.stack([coarsen(coarse_perm), coarsen(leftover_1)]), per_side)
    correction_all = global_cycle(gathered[:, 1], gathered[:, 0], 2, per_side)

    correction = lax.dynamic_index_in_dim(correction_all, my_row, 0, keepdims=False)
    values_1 = stored_1 + refine(correction)
    faces = [
        mine + theirs
        for mine, theirs in zip(stored_faces_1, refined_faces(correction_all, my_row, per_side))
    ]
    values_1 = smooth(values_1, right_1, coefs_1, diagonal_1, scaling, with_faces(values_1, faces))
    for sweep_no in range(SWEEPS - 1):
        faces = pick(exchange([values_1], per_side), 0)
        values_1 = smooth(values_1, right_1, coefs_1, diagonal_1, scaling, with_faces(values_1, faces))
    coarse_faces = pick(exchange([values_1], per_side), 0)

    values = stored + refine(values_1)
    faces = [mine + refine_face_of(theirs) for mine, theirs in zip(stored_faces, coarse_faces)]
    values = smooth(values, source, face_coefs, diagonal, 1.0, with_faces(values, faces))
    for sweep_no in range(SWEEPS - 1):
        faces = pick(exchange([values], per_side), 0)
        values = smooth(values, source, face_coefs, diagonal, 1.0, with_faces(values, faces))
    faces = pick(exchange([values], per_side), 0)
    residual = source - operate(values, with_faces(values, faces), face_coefs, 1.0)
    return (values[None], residual[None])


def solution(mesh):
    return jax.shard_map(
        shards,
        mesh=mesh,
        in_specs=(
            P("space", None, None, None),
            P(),
            P("real"),
            P("real"),
            P(("real", "space"), None, None, None),
        ),
        out_specs=(P(("real", "space"), None, None, None), P(("real", "space"), None, None, None)),
        check_vma=False,
    )
```

```python
import jax
import jax.numpy as jnp
from jax import lax
from jax.sharding import PartitionSpec as P

LEVELS = 3
SWEEPS = 2
CSWEEPS = 6


OMEGA = 0.8


def shifted(shard, axis, by):
    peers = lax.axis_size(axis)
    return lax.ppermute(shard, axis, [(i, (i + by) % peers) for i in range(peers)])


def exchange(fields, per_side):
    count_dev = lax.axis_size("space")
    plane_step = per_side * per_side

    def stack(number):
        return jnp.stack([own_faces(values)[number] for values in fields])

    if (2 * plane_step) % count_dev == 0:
        both_x = shifted(jnp.concatenate([stack(0), stack(1)], axis=1), "space", plane_step)
        lower_x, upper_x = both_x[:, :1], both_x[:, 1:]
    else:
        lower_x = shifted(stack(0), "space", plane_step)
        upper_x = shifted(stack(1), "space", -plane_step)
    lower_y = shifted(stack(2), "space", per_side)
    upper_y = shifted(stack(3), "space", -per_side)
    lower_z = shifted(stack(4), "space", 1)
    upper_z = shifted(stack(5), "space", -1)
    return [lower_x, upper_x, lower_y, upper_y, lower_z, upper_z]


def own_faces(values):
    return [values[-1:], values[:1], values[:, -1:], values[:, :1], values[:, :, -1:], values[:, :, :1]]


def exchange_mixed(fields, per_side):
    count_dev = lax.axis_size("space")
    plane_step = per_side * per_side
    outgoing = [own_faces(values) for values in fields]
    shifts = [plane_step, -plane_step, per_side, -per_side, 1, -1]
    flat = [jnp.concatenate([faces[d].reshape(-1) for faces in outgoing]) for d in range(6)]
    received = [None] * 6
    if (2 * plane_step) % count_dev == 0:
        both = shifted(jnp.concatenate([flat[0], flat[1]]), "space", plane_step)
        received[0], received[1] = both[: flat[0].shape[0]], both[flat[0].shape[0] :]
        rest = range(2, 6)
    else:
        rest = range(6)
    for d in rest:
        received[d] = shifted(flat[d], "space", shifts[d])
    result = [[None] * 6 for _ in fields]
    for d in range(6):
        offset = 0
        for number, faces in enumerate(outgoing):
            size = faces[d].size
            result[number][d] = received[d][offset : offset + size].reshape(faces[d].shape)
            offset += size
    return result


def exchange_with_coarse(fields, coarse, per_side):
    count_dev = lax.axis_size("space")
    plane_step = per_side * per_side
    size_x, size_y, size_z = fields.shape[1:]
    half_x, half_y, half_z = coarse.shape

    def padded(face):
        pads = [(0, full - part) if part != 1 else (0, 0) for full, part in zip((size_x, size_y, size_z), face.shape)]
        return jnp.pad(face, pads)[None]

    def message(number):
        pieces = [fields[:, -1:], fields[:, :1], fields[:, :, -1:], fields[:, :, :1], fields[:, :, :, -1:], fields[:, :, :, :1]]
        return jnp.concatenate([pieces[number], padded(own_faces(coarse)[number])], axis=0)

    shifts = [plane_step, -plane_step, per_side, -per_side, 1, -1]
    received = [None] * 6
    if (2 * plane_step) % count_dev == 0:
        both = shifted(jnp.concatenate([message(0), message(1)], axis=1), "space", plane_step)
        received[0], received[1] = both[:, :1], both[:, 1:]
        rest = range(2, 6)
    else:
        rest = range(6)
    for number in rest:
        received[number] = shifted(message(number), "space", shifts[number])
    count = fields.shape[0]
    field_faces = [face[:count] for face in received]
    coarse_faces = []
    for number, face in enumerate(received):
        shape = own_faces(coarse)[number].shape
        coarse_faces.append(face[count, : shape[0], : shape[1], : shape[2]])
    return field_faces, coarse_faces


def gather_rows(block, per_side):
    count_dev = lax.axis_size("space")
    if count_dev > 16:
        return lax.all_gather(block[None], "space", axis=0, tiled=True)
    my_row = lax.axis_index("space")
    by_offset = jnp.stack([block] + [shifted(block, "space", k) for k in range(1, count_dev)])
    return jnp.take(by_offset, (my_row - jnp.arange(count_dev)) % count_dev, axis=0)


def pick(faces, number):
    return [face[number] for face in faces]


def with_faces(values, faces):
    lower_x, upper_x, lower_y, upper_y, lower_z, upper_z = faces
    return [
        jnp.concatenate([lower_x, values[:-1]], axis=0),
        jnp.concatenate([values[1:], upper_x], axis=0),
        jnp.concatenate([lower_y, values[:, :-1]], axis=1),
        jnp.concatenate([values[:, 1:], upper_y], axis=1),
        jnp.concatenate([lower_z, values[:, :, :-1]], axis=2),
        jnp.concatenate([values[:, :, 1:], upper_z], axis=2),
    ]


def rolled_faces(values, per_side):
    plane_step = per_side * per_side
    return [
        jnp.concatenate([jnp.roll(values[:, -1:], plane_step, axis=0), values[:, :-1]], axis=1),
        jnp.concatenate([values[:, 1:], jnp.roll(values[:, :1], -plane_step, axis=0)], axis=1),
        jnp.concatenate([jnp.roll(values[:, :, -1:], per_side, axis=0), values[:, :, :-1]], axis=2),
        jnp.concatenate([values[:, :, 1:], jnp.roll(values[:, :, :1], -per_side, axis=0)], axis=2),
        jnp.concatenate([jnp.roll(values[:, :, :, -1:], 1, axis=0), values[:, :, :, :-1]], axis=3),
        jnp.concatenate([values[:, :, :, 1:], jnp.roll(values[:, :, :, :1], -1, axis=0)], axis=3),
    ]


def coefficients(permeab, neighbors, scaling):
    face_coefs = [0.5 * (permeab + beside) for beside in neighbors]
    total_sum = face_coefs[0]
    for number in range(1, 6):
        total_sum = total_sum + face_coefs[number]
    return (face_coefs, scaling * total_sum)


def operate(values, neighbors, face_coefs, scaling):
    total_sum = face_coefs[0] * (values - neighbors[0])
    for number in range(1, 6):
        total_sum = total_sum + face_coefs[number] * (values - neighbors[number])
    return scaling * total_sum


def smooth(values, right_side, face_coefs, diagonal, scaling, neighbors):
    return values + OMEGA * (right_side - operate(values, neighbors, face_coefs, scaling)) / diagonal


def pair_mean(size, scale):
    rows = jnp.arange(size)[:, None] // 2
    cols = jnp.arange(size // 2)[None, :]
    return jnp.where(rows == cols, scale, 0.0).astype(jnp.float32)


def plane_mean(size_x, size_y):
    fine = jnp.arange(size_x * size_y)
    coarse_of = (fine // size_y // 2) * (size_y // 2) + (fine % size_y) // 2
    return jnp.where(
        jnp.arange(size_x * size_y // 4)[:, None] == coarse_of[None, :], 0.25, 0.0
    ).astype(jnp.float32)


def coarsen(values):
    size_x, size_y, size_z = values.shape
    along_z = jnp.dot(
        values.reshape(size_x * size_y, size_z),
        pair_mean(size_z, 0.5),
        precision=lax.Precision.HIGHEST,
    )
    both = jnp.dot(plane_mean(size_x, size_y), along_z, precision=lax.Precision.HIGHEST)
    return both.reshape(size_x // 2, size_y // 2, size_z // 2)


def refine(values):
    return jnp.repeat(jnp.repeat(jnp.repeat(values, 2, axis=0), 2, axis=1), 2, axis=2)


def coarsen_all(values):
    count_b, size_x, size_y, size_z = values.shape
    along_z = jnp.dot(
        values.reshape(count_b * size_x * size_y, size_z),
        pair_mean(size_z, 0.5),
        precision=lax.Precision.HIGHEST,
    ).reshape(count_b, size_x * size_y, size_z // 2)
    both = jnp.einsum(
        "pq,bqz->bpz", plane_mean(size_x, size_y), along_z, precision=lax.Precision.HIGHEST
    )
    return both.reshape(count_b, size_x // 2, size_y // 2, size_z // 2)


def refine_all(values):
    return jnp.repeat(jnp.repeat(jnp.repeat(values, 2, axis=1), 2, axis=2), 2, axis=3)


def refine_face(face):
    return jnp.repeat(jnp.repeat(face, 2, axis=0), 2, axis=1)


def refine_face_of(face):
    for axis in range(3):
        if face.shape[axis] != 1:
            face = jnp.repeat(face, 2, axis=axis)
    return face


def refined_faces(coarse_all, my_row, per_side):
    count_b = coarse_all.shape[0]

    def row(offset):
        return lax.dynamic_index_in_dim(coarse_all, (my_row + offset) % count_b, 0, keepdims=False)

    plane_step = per_side * per_side
    return [
        refine_face(row(-plane_step)[-1])[None],
        refine_face(row(plane_step)[0])[None],
        refine_face(row(-per_side)[:, -1])[:, None],
        refine_face(row(per_side)[:, 0])[:, None],
        refine_face(row(-1)[:, :, -1])[:, :, None],
        refine_face(row(1)[:, :, 0])[:, :, None],
    ]


def neighbour_rows(count_b, size_x, size_y, per_side):
    count_r = count_b * size_x * size_y
    index = jnp.arange(count_r)
    row = index // (size_x * size_y)
    at_x = index // size_y % size_x
    at_y = index % size_y
    plane_step = per_side * per_side
    picks = []
    for axis_no, (size, step) in enumerate(((size_x, plane_step), (size_y, per_side))):
        coord = at_x if axis_no == 0 else at_y
        for sign in (-1, 1):
            edge = size - 1 if sign > 0 else 0
            moved = jnp.where(coord == edge, size - 1 - edge, coord + sign)
            new_row = jnp.where(coord == edge, (row + sign * step) % count_b, row)
            if axis_no == 0:
                picks.append((new_row * size_x + moved) * size_y + at_y)
            else:
                picks.append((new_row * size_x + at_x) * size_y + moved)
    for sign in (-1, 1):
        picks.append((((row + sign) % count_b) * size_x + at_x) * size_y + at_y)
    target = jnp.concatenate(picks)
    return jnp.where(target[:, None] == index[None, :], 1.0, 0.0).astype(jnp.bfloat16)


def lane_shift(size_z, sign):
    lanes_in = jnp.arange(size_z)[:, None]
    lanes_out = jnp.arange(size_z)[None, :]
    inner = jnp.where(lanes_in == lanes_out + sign, 1.0, 0.0)
    edge_in, edge_out = (size_z - 1, 0) if sign < 0 else (0, size_z - 1)
    wrap = jnp.where((lanes_in == edge_in) & (lanes_out == edge_out), 1.0, 0.0)
    return jnp.concatenate([inner, wrap]).astype(jnp.bfloat16)


def split3(values):
    pieces = []
    rest = values
    for piece_no in range(3):
        piece = lax.reduce_precision(rest, exponent_bits=8, mantissa_bits=7)
        pieces.append(piece.astype(jnp.bfloat16))
        rest = rest - piece
    return pieces


def lane_tile(size):
    return -(-size // 128) * 128


def pick_rows(picker, values):
    size_z = values.shape[1]
    width = lane_tile(size_z)
    joined = jnp.concatenate(
        [jnp.pad(piece, ((0, 0), (0, width - size_z))) for piece in split3(values)], axis=1
    )
    out = jnp.dot(picker, joined, preferred_element_type=jnp.float32)
    return (out[:, :size_z] + out[:, width : width + size_z]) + out[:, 2 * width : 2 * width + size_z]


def pick_lanes(values, shift):
    count_r = values.shape[0]
    stacked = jnp.concatenate(split3(values), axis=0)
    out = jnp.dot(stacked, shift, preferred_element_type=jnp.float32)
    return (out[:count_r] + out[count_r : 2 * count_r]) + out[2 * count_r :]


def flat_faces(values, picker, lower_z, upper_z):
    count_r, size_z = values.shape
    rows = pick_rows(picker, values)
    shifts = jnp.concatenate(
        [lower_z[:size_z], upper_z[:size_z], lower_z[size_z:], upper_z[size_z:]], axis=1
    )
    out = pick_lanes(jnp.concatenate([values, rows[4 * count_r :]], axis=0), shifts)
    lower = out[:count_r, :size_z] + out[count_r : 2 * count_r, 2 * size_z : 3 * size_z]
    upper = out[:count_r, size_z : 2 * size_z] + out[2 * count_r :, 3 * size_z :]
    return [rows[k * count_r : (k + 1) * count_r] for k in range(4)] + [lower, upper]


def row_mean(count_b, size_x, size_y):
    index = jnp.arange(count_b * size_x * size_y)
    row = index // (size_x * size_y)
    coarse_of = (row * (size_x // 2) + index // size_y % size_x // 2) * (size_y // 2) + index % size_y // 2
    return jnp.where(
        jnp.arange(count_b * size_x * size_y // 4)[:, None] == coarse_of[None, :], 0.25, 0.0
    ).astype(jnp.float32)


def global_cycle(all_rhs, all_perm, first_level, per_side):
    count_b, size_x, size_y, size_z = all_rhs.shape
    shapes = [(size_x >> n, size_y >> n, size_z >> n) for n in range(LEVELS - first_level + 1)]
    pickers = [neighbour_rows(count_b, sx, sy, per_side) for sx, sy, sz in shapes]
    shifts = [(lane_shift(sz, -1), lane_shift(sz, 1)) for sx, sy, sz in shapes]
    means = [(row_mean(count_b, sx, sy), pair_mean(sz, 0.5)) for sx, sy, sz in shapes[:-1]]

    def faces(values, number):
        return flat_faces(values, pickers[number], *shifts[number])

    def down(values, number):
        rows, lanes = means[number]
        return jnp.dot(
            rows,
            jnp.dot(values, lanes, precision=lax.Precision.HIGHEST),
            precision=lax.Precision.HIGHEST,
        )

    def up(values, number):
        rows, lanes = means[number]
        return jnp.dot(
            rows.T * 4.0,
            jnp.dot(values, lanes.T * 2.0, precision=lax.Precision.HIGHEST),
            precision=lax.Precision.HIGHEST,
        )

    perms = [all_perm.reshape(-1, size_z)]
    for number in range(LEVELS - first_level):
        perms.append(down(perms[-1], number))
    coefs = [
        coefficients(perms[number], faces(perms[number], number), 0.25 ** (first_level + number))
        for number in range(LEVELS - first_level + 1)
    ]
    right_side = all_rhs.reshape(-1, size_z)
    stored = []
    rights = []
    for number in range(LEVELS - first_level):
        face_coefs, diagonal = coefs[number]
        scaling = 0.25 ** (first_level + number)
        values = OMEGA * right_side / diagonal
        for sweep_no in range(SWEEPS - 1):
            values = smooth(values, right_side, face_coefs, diagonal, scaling, faces(values, number))
        leftover = right_side - operate(values, faces(values, number), face_coefs, scaling)
        stored.append(values)
        rights.append(right_side)
        right_side = down(leftover, number)
    last = LEVELS - first_level
    face_coefs, diagonal = coefs[last]
    scaling = 0.25**LEVELS
    correction = OMEGA * right_side / diagonal
    for sweep_no in range(CSWEEPS - 1):
        correction = smooth(
            correction, right_side, face_coefs, diagonal, scaling, faces(correction, last)
        )
    for number in reversed(range(LEVELS - first_level)):
        face_coefs, diagonal = coefs[number]
        scaling = 0.25 ** (first_level + number)
        values = stored[number] + up(correction, number)
        for sweep_no in range(SWEEPS):
            values = smooth(
                values, rights[number], face_coefs, diagonal, scaling, faces(values, number)
            )
        correction = values
    return correction.reshape(count_b, size_x, size_y, size_z)


def shards(perm_class, class_values, well_cells, well_rates, guess):
    count_dev = lax.axis_size("space")
    per_side = 2 + 2 * (count_dev // 64)
    my_row = lax.axis_index("space")
    block_no = (my_row + per_side * per_side + per_side + 1) % count_dev
    block_x = block_no // (per_side * per_side)
    block_y = block_no // per_side % per_side
    block_z = block_no % per_side
    classes = perm_class[0]
    width_x, width_y, width_z = classes.shape
    permeab = jnp.zeros(classes.shape, jnp.float32)
    for number in range(class_values.shape[0]):
        permeab = permeab + jnp.where(classes == number, class_values[number], 0.0)
    row_len = per_side * width_z
    plane = per_side * width_y * row_len
    glob_x = well_cells // plane
    glob_y = well_cells // row_len % (per_side * width_y)
    glob_z = well_cells % row_len
    onehot_x = jnp.where(
        (glob_x - block_x * width_x)[:, None] == jnp.arange(width_x)[None, :],
        well_rates[:, None],
        0.0,
    )
    onehot_y = jnp.where(
        (glob_y - block_y * width_y)[:, None] == jnp.arange(width_y)[None, :], 1.0, 0.0
    ).astype(jnp.float32)
    onehot_z = jnp.where(
        (glob_z - block_z * width_z)[:, None] == jnp.arange(width_z)[None, :], 1.0, 0.0
    ).astype(jnp.float32)
    source = jnp.einsum(
        "wi,wj,wk->ijk", onehot_x, onehot_y, onehot_z, precision=lax.Precision.HIGHEST
    )

    values = guess[0]
    if count_dev * (width_x // 2) * (width_y // 2) <= 512:
        first = exchange([permeab, values], per_side)
        face_coefs, diagonal = coefficients(permeab, with_faces(permeab, pick(first, 0)), 1.0)
        values = smooth(values, source, face_coefs, diagonal, 1.0, with_faces(values, pick(first, 1)))
        for sweep_no in range(SWEEPS - 1):
            faces = pick(exchange([values], per_side), 0)
            values = smooth(values, source, face_coefs, diagonal, 1.0, with_faces(values, faces))
        stored_faces = pick(exchange([values], per_side), 0)
        leftover = source - operate(values, with_faces(values, stored_faces), face_coefs, 1.0)
        stored = values

        gathered = gather_rows(jnp.stack([coarsen(permeab), coarsen(leftover)]), per_side)
        correction_all = global_cycle(gathered[:, 1], gathered[:, 0], 1, per_side)

        correction = lax.dynamic_index_in_dim(correction_all, my_row, 0, keepdims=False)
        values = stored + refine(correction)
        faces = [
            mine + theirs
            for mine, theirs in zip(stored_faces, refined_faces(correction_all, my_row, per_side))
        ]
        values = smooth(values, source, face_coefs, diagonal, 1.0, with_faces(values, faces))
        for sweep_no in range(SWEEPS - 1):
            faces = pick(exchange([values], per_side), 0)
            values = smooth(values, source, face_coefs, diagonal, 1.0, with_faces(values, faces))
        faces = pick(exchange([values], per_side), 0)
        residual = source - operate(values, with_faces(values, faces), face_coefs, 1.0)
        return (values[None], residual[None])

    coarse_perm = coarsen(permeab)
    first, coarse_first = exchange_with_coarse(jnp.stack([permeab, values]), coarse_perm, per_side)
    face_coefs, diagonal = coefficients(permeab, with_faces(permeab, pick(first, 0)), 1.0)
    values = smooth(values, source, face_coefs, diagonal, 1.0, with_faces(values, pick(first, 1)))
    for sweep_no in range(SWEEPS - 1):
        faces = pick(exchange([values], per_side), 0)
        values = smooth(values, source, face_coefs, diagonal, 1.0, with_faces(values, faces))
    stored_faces = pick(exchange([values], per_side), 0)
    leftover = source - operate(values, with_faces(values, stored_faces), face_coefs, 1.0)
    stored = values

    scaling = 0.25
    right_1 = coarsen(leftover)
    coefs_1, diagonal_1 = coefficients(coarse_perm, with_faces(coarse_perm, coarse_first), scaling)
    values_1 = OMEGA * right_1 / diagonal_1
    for sweep_no in range(SWEEPS - 1):
        faces = pick(exchange([values_1], per_side), 0)
        values_1 = smooth(values_1, right_1, coefs_1, diagonal_1, scaling, with_faces(values_1, faces))
    stored_faces_1 = pick(exchange([values_1], per_side), 0)
    leftover_1 = right_1 - operate(values_1, with_faces(values_1, stored_faces_1), coefs_1, scaling)
    stored_1 = values_1

    gathered = gather_rows(jnp.stack([coarsen(coarse_perm), coarsen(leftover_1)]), per_side)
    correction_all = global_cycle(gathered[:, 1], gathered[:, 0], 2, per_side)

    correction = lax.dynamic_index_in_dim(correction_all, my_row, 0, keepdims=False)
    values_1 = stored_1 + refine(correction)
    faces = [
        mine + theirs
        for mine, theirs in zip(stored_faces_1, refined_faces(correction_all, my_row, per_side))
    ]
    values_1 = smooth(values_1, right_1, coefs_1, diagonal_1, scaling, with_faces(values_1, faces))
    for sweep_no in range(SWEEPS - 1):
        faces = pick(exchange([values_1], per_side), 0)
        values_1 = smooth(values_1, right_1, coefs_1, diagonal_1, scaling, with_faces(values_1, faces))
    coarse_faces = pick(exchange([values_1], per_side), 0)

    values = stored + refine(values_1)
    faces = [mine + refine_face_of(theirs) for mine, theirs in zip(stored_faces, coarse_faces)]
    values = smooth(values, source, face_coefs, diagonal, 1.0, with_faces(values, faces))
    for sweep_no in range(SWEEPS - 1):
        faces = pick(exchange([values], per_side), 0)
        values = smooth(values, source, face_coefs, diagonal, 1.0, with_faces(values, faces))
    faces = pick(exchange([values], per_side), 0)
    residual = source - operate(values, with_faces(values, faces), face_coefs, 1.0)
    return (values[None], residual[None])


def solution(mesh):
    return jax.shard_map(
        shards,
        mesh=mesh,
        in_specs=(
            P("space", None, None, None),
            P(),
            P("real"),
            P("real"),
            P(("real", "space"), None, None, None),
        ),
        out_specs=(P(("real", "space"), None, None, None), P(("real", "space"), None, None, None)),
        check_vma=False,
    )
```

```python
import jax
import jax.numpy as jnp
from jax import lax
from jax.sharding import PartitionSpec as P

LEVELS = 3
SWEEPS = 2
CSWEEPS = 6


OMEGA = 0.8


def shifted(shard, axis, by):
    peers = lax.axis_size(axis)
    return lax.ppermute(shard, axis, [(i, (i + by) % peers) for i in range(peers)])


def exchange(fields, per_side):
    count_dev = lax.axis_size("space")
    plane_step = per_side * per_side

    def stack(number):
        return jnp.stack([own_faces(values)[number] for values in fields])

    if (2 * plane_step) % count_dev == 0:
        both_x = shifted(jnp.concatenate([stack(0), stack(1)], axis=1), "space", plane_step)
        lower_x, upper_x = both_x[:, :1], both_x[:, 1:]
    else:
        lower_x = shifted(stack(0), "space", plane_step)
        upper_x = shifted(stack(1), "space", -plane_step)
    lower_y = shifted(stack(2), "space", per_side)
    upper_y = shifted(stack(3), "space", -per_side)
    lower_z = shifted(stack(4), "space", 1)
    upper_z = shifted(stack(5), "space", -1)
    return [lower_x, upper_x, lower_y, upper_y, lower_z, upper_z]


def own_faces(values):
    return [values[-1:], values[:1], values[:, -1:], values[:, :1], values[:, :, -1:], values[:, :, :1]]


def exchange_mixed(fields, per_side):
    count_dev = lax.axis_size("space")
    plane_step = per_side * per_side
    outgoing = [own_faces(values) for values in fields]
    shifts = [plane_step, -plane_step, per_side, -per_side, 1, -1]
    flat = [jnp.concatenate([faces[d].reshape(-1) for faces in outgoing]) for d in range(6)]
    received = [None] * 6
    if (2 * plane_step) % count_dev == 0:
        both = shifted(jnp.concatenate([flat[0], flat[1]]), "space", plane_step)
        received[0], received[1] = both[: flat[0].shape[0]], both[flat[0].shape[0] :]
        rest = range(2, 6)
    else:
        rest = range(6)
    for d in rest:
        received[d] = shifted(flat[d], "space", shifts[d])
    result = [[None] * 6 for _ in fields]
    for d in range(6):
        offset = 0
        for number, faces in enumerate(outgoing):
            size = faces[d].size
            result[number][d] = received[d][offset : offset + size].reshape(faces[d].shape)
            offset += size
    return result


def exchange_with_coarse(fields, coarse, per_side):
    count_dev = lax.axis_size("space")
    plane_step = per_side * per_side
    size_x, size_y, size_z = fields.shape[1:]
    half_x, half_y, half_z = coarse.shape

    def padded(face):
        pads = [(0, full - part) if part != 1 else (0, 0) for full, part in zip((size_x, size_y, size_z), face.shape)]
        return jnp.pad(face, pads)[None]

    def message(number):
        pieces = [fields[:, -1:], fields[:, :1], fields[:, :, -1:], fields[:, :, :1], fields[:, :, :, -1:], fields[:, :, :, :1]]
        return jnp.concatenate([pieces[number], padded(own_faces(coarse)[number])], axis=0)

    shifts = [plane_step, -plane_step, per_side, -per_side, 1, -1]
    received = [None] * 6
    if (2 * plane_step) % count_dev == 0:
        both = shifted(jnp.concatenate([message(0), message(1)], axis=1), "space", plane_step)
        received[0], received[1] = both[:, :1], both[:, 1:]
        rest = range(2, 6)
    else:
        rest = range(6)
    for number in rest:
        received[number] = shifted(message(number), "space", shifts[number])
    count = fields.shape[0]
    field_faces = [face[:count] for face in received]
    coarse_faces = []
    for number, face in enumerate(received):
        shape = own_faces(coarse)[number].shape
        coarse_faces.append(face[count, : shape[0], : shape[1], : shape[2]])
    return field_faces, coarse_faces


def gather_rows(block, per_side):
    count_dev = lax.axis_size("space")
    if count_dev > 16:
        return lax.all_gather(block[None], "space", axis=0, tiled=True)
    my_row = lax.axis_index("space")
    by_offset = jnp.stack([block] + [shifted(block, "space", k) for k in range(1, count_dev)])
    return jnp.take(by_offset, (my_row - jnp.arange(count_dev)) % count_dev, axis=0)


def pick(faces, number):
    return [face[number] for face in faces]


def with_faces(values, faces):
    lower_x, upper_x, lower_y, upper_y, lower_z, upper_z = faces
    return [
        jnp.concatenate([lower_x, values[:-1]], axis=0),
        jnp.concatenate([values[1:], upper_x], axis=0),
        jnp.concatenate([lower_y, values[:, :-1]], axis=1),
        jnp.concatenate([values[:, 1:], upper_y], axis=1),
        jnp.concatenate([lower_z, values[:, :, :-1]], axis=2),
        jnp.concatenate([values[:, :, 1:], upper_z], axis=2),
    ]


def rolled_faces(values, per_side):
    plane_step = per_side * per_side
    return [
        jnp.concatenate([jnp.roll(values[:, -1:], plane_step, axis=0), values[:, :-1]], axis=1),
        jnp.concatenate([values[:, 1:], jnp.roll(values[:, :1], -plane_step, axis=0)], axis=1),
        jnp.concatenate([jnp.roll(values[:, :, -1:], per_side, axis=0), values[:, :, :-1]], axis=2),
        jnp.concatenate([values[:, :, 1:], jnp.roll(values[:, :, :1], -per_side, axis=0)], axis=2),
        jnp.concatenate([jnp.roll(values[:, :, :, -1:], 1, axis=0), values[:, :, :, :-1]], axis=3),
        jnp.concatenate([values[:, :, :, 1:], jnp.roll(values[:, :, :, :1], -1, axis=0)], axis=3),
    ]


def coefficients(permeab, neighbors, scaling):
    face_coefs = [0.5 * (permeab + beside) for beside in neighbors]
    total_sum = face_coefs[0]
    for number in range(1, 6):
        total_sum = total_sum + face_coefs[number]
    return (face_coefs, scaling * total_sum)


def operate(values, neighbors, face_coefs, scaling):
    total_sum = face_coefs[0] * (values - neighbors[0])
    for number in range(1, 6):
        total_sum = total_sum + face_coefs[number] * (values - neighbors[number])
    return scaling * total_sum


def smooth(values, right_side, face_coefs, diagonal, scaling, neighbors):
    return values + OMEGA * (right_side - operate(values, neighbors, face_coefs, scaling)) / diagonal


def pair_mean(size, scale):
    rows = jnp.arange(size)[:, None] // 2
    cols = jnp.arange(size // 2)[None, :]
    return jnp.where(rows == cols, scale, 0.0).astype(jnp.float32)


def plane_mean(size_x, size_y):
    fine = jnp.arange(size_x * size_y)
    coarse_of = (fine // size_y // 2) * (size_y // 2) + (fine % size_y) // 2
    return jnp.where(
        jnp.arange(size_x * size_y // 4)[:, None] == coarse_of[None, :], 0.25, 0.0
    ).astype(jnp.float32)


def coarsen(values):
    size_x, size_y, size_z = values.shape
    along_z = jnp.dot(
        values.reshape(size_x * size_y, size_z),
        pair_mean(size_z, 0.5),
        precision=lax.Precision.HIGHEST,
    )
    both = jnp.dot(plane_mean(size_x, size_y), along_z, precision=lax.Precision.HIGHEST)
    return both.reshape(size_x // 2, size_y // 2, size_z // 2)


def refine(values):
    return jnp.repeat(jnp.repeat(jnp.repeat(values, 2, axis=0), 2, axis=1), 2, axis=2)


def coarsen_all(values):
    count_b, size_x, size_y, size_z = values.shape
    along_z = jnp.dot(
        values.reshape(count_b * size_x * size_y, size_z),
        pair_mean(size_z, 0.5),
        precision=lax.Precision.HIGHEST,
    ).reshape(count_b, size_x * size_y, size_z // 2)
    both = jnp.einsum(
        "pq,bqz->bpz", plane_mean(size_x, size_y), along_z, precision=lax.Precision.HIGHEST
    )
    return both.reshape(count_b, size_x // 2, size_y // 2, size_z // 2)


def refine_all(values):
    return jnp.repeat(jnp.repeat(jnp.repeat(values, 2, axis=1), 2, axis=2), 2, axis=3)


def refine_face(face):
    return jnp.repeat(jnp.repeat(face, 2, axis=0), 2, axis=1)


def refine_face_of(face):
    for axis in range(3):
        if face.shape[axis] != 1:
            face = jnp.repeat(face, 2, axis=axis)
    return face


def refined_faces(coarse_all, my_row, per_side):
    count_b = coarse_all.shape[0]

    def row(offset):
        return lax.dynamic_index_in_dim(coarse_all, (my_row + offset) % count_b, 0, keepdims=False)

    plane_step = per_side * per_side
    return [
        refine_face(row(-plane_step)[-1])[None],
        refine_face(row(plane_step)[0])[None],
        refine_face(row(-per_side)[:, -1])[:, None],
        refine_face(row(per_side)[:, 0])[:, None],
        refine_face(row(-1)[:, :, -1])[:, :, None],
        refine_face(row(1)[:, :, 0])[:, :, None],
    ]


def neighbour_rows(count_b, size_x, size_y, per_side):
    count_r = count_b * size_x * size_y
    index = jnp.arange(count_r)
    row = index // (size_x * size_y)
    at_x = index // size_y % size_x
    at_y = index % size_y
    plane_step = per_side * per_side
    picks = []
    for axis_no, (size, step) in enumerate(((size_x, plane_step), (size_y, per_side))):
        coord = at_x if axis_no == 0 else at_y
        for sign in (-1, 1):
            edge = size - 1 if sign > 0 else 0
            moved = jnp.where(coord == edge, size - 1 - edge, coord + sign)
            new_row = jnp.where(coord == edge, (row + sign * step) % count_b, row)
            if axis_no == 0:
                picks.append((new_row * size_x + moved) * size_y + at_y)
            else:
                picks.append((new_row * size_x + at_x) * size_y + moved)
    for sign in (-1, 1):
        picks.append((((row + sign) % count_b) * size_x + at_x) * size_y + at_y)
    target = jnp.concatenate(picks)
    return jnp.where(target[:, None] == index[None, :], 1.0, 0.0).astype(jnp.bfloat16)


def lane_shift(size_z, sign):
    lanes_in = jnp.arange(size_z)[:, None]
    lanes_out = jnp.arange(size_z)[None, :]
    inner = jnp.where(lanes_in == lanes_out + sign, 1.0, 0.0)
    edge_in, edge_out = (size_z - 1, 0) if sign < 0 else (0, size_z - 1)
    wrap = jnp.where((lanes_in == edge_in) & (lanes_out == edge_out), 1.0, 0.0)
    return jnp.concatenate([inner, wrap]).astype(jnp.bfloat16)


def split3(values):
    pieces = []
    rest = values
    for piece_no in range(3):
        piece = lax.reduce_precision(rest, exponent_bits=8, mantissa_bits=7)
        pieces.append(piece.astype(jnp.bfloat16))
        rest = rest - piece
    return pieces


def pick_rows(picker, values):
    size_z = values.shape[1]
    joined = jnp.concatenate(split3(values), axis=1)
    out = jnp.dot(picker, joined, preferred_element_type=jnp.float32)
    return (out[:, :size_z] + out[:, size_z : 2 * size_z]) + out[:, 2 * size_z :]


def pick_lanes(values, shift):
    count_r = values.shape[0]
    stacked = jnp.concatenate(split3(values), axis=0)
    out = jnp.dot(stacked, shift, preferred_element_type=jnp.float32)
    return (out[:count_r] + out[count_r : 2 * count_r]) + out[2 * count_r :]


def flat_faces(values, picker, lower_z, upper_z):
    count_r, size_z = values.shape
    rows = pick_rows(picker, values)
    shifts = jnp.concatenate(
        [lower_z[:size_z], upper_z[:size_z], lower_z[size_z:], upper_z[size_z:]], axis=1
    )
    out = pick_lanes(jnp.concatenate([values, rows[4 * count_r :]], axis=0), shifts)
    lower = out[:count_r, :size_z] + out[count_r : 2 * count_r, 2 * size_z : 3 * size_z]
    upper = out[:count_r, size_z : 2 * size_z] + out[2 * count_r :, 3 * size_z :]
    return [rows[k * count_r : (k + 1) * count_r] for k in range(4)] + [lower, upper]


def row_mean(count_b, size_x, size_y):
    index = jnp.arange(count_b * size_x * size_y)
    row = index // (size_x * size_y)
    coarse_of = (row * (size_x // 2) + index // size_y % size_x // 2) * (size_y // 2) + index % size_y // 2
    return jnp.where(
        jnp.arange(count_b * size_x * size_y // 4)[:, None] == coarse_of[None, :], 0.25, 0.0
    ).astype(jnp.float32)


def global_cycle(all_rhs, all_perm, first_level, per_side):
    count_b, size_x, size_y, size_z = all_rhs.shape
    shapes = [(size_x >> n, size_y >> n, size_z >> n) for n in range(LEVELS - first_level + 1)]
    pickers = [neighbour_rows(count_b, sx, sy, per_side) for sx, sy, sz in shapes]
    shifts = [(lane_shift(sz, -1), lane_shift(sz, 1)) for sx, sy, sz in shapes]
    means = [(row_mean(count_b, sx, sy), pair_mean(sz, 0.5)) for sx, sy, sz in shapes[:-1]]

    def faces(values, number):
        return flat_faces(values, pickers[number], *shifts[number])

    def down(values, number):
        rows, lanes = means[number]
        return jnp.dot(
            rows,
            jnp.dot(values, lanes, precision=lax.Precision.HIGHEST),
            precision=lax.Precision.HIGHEST,
        )

    def up(values, number):
        rows, lanes = means[number]
        return jnp.dot(
            rows.T * 4.0,
            jnp.dot(values, lanes.T * 2.0, precision=lax.Precision.HIGHEST),
            precision=lax.Precision.HIGHEST,
        )

    perms = [all_perm.reshape(-1, size_z)]
    for number in range(LEVELS - first_level):
        perms.append(down(perms[-1], number))
    coefs = [
        coefficients(perms[number], faces(perms[number], number), 0.25 ** (first_level + number))
        for number in range(LEVELS - first_level + 1)
    ]
    right_side = all_rhs.reshape(-1, size_z)
    stored = []
    rights = []
    for number in range(LEVELS - first_level):
        face_coefs, diagonal = coefs[number]
        scaling = 0.25 ** (first_level + number)
        values = OMEGA * right_side / diagonal
        for sweep_no in range(SWEEPS - 1):
            values = smooth(values, right_side, face_coefs, diagonal, scaling, faces(values, number))
        leftover = right_side - operate(values, faces(values, number), face_coefs, scaling)
        stored.append(values)
        rights.append(right_side)
        right_side = down(leftover, number)
    last = LEVELS - first_level
    face_coefs, diagonal = coefs[last]
    scaling = 0.25**LEVELS
    correction = OMEGA * right_side / diagonal
    for sweep_no in range(CSWEEPS - 1):
        correction = smooth(
            correction, right_side, face_coefs, diagonal, scaling, faces(correction, last)
        )
    for number in reversed(range(LEVELS - first_level)):
        face_coefs, diagonal = coefs[number]
        scaling = 0.25 ** (first_level + number)
        values = stored[number] + up(correction, number)
        for sweep_no in range(SWEEPS):
            values = smooth(
                values, rights[number], face_coefs, diagonal, scaling, faces(values, number)
            )
        correction = values
    return correction.reshape(count_b, size_x, size_y, size_z)


def shards(perm_class, class_values, well_cells, well_rates, guess):
    count_dev = lax.axis_size("space")
    per_side = 2 + 2 * (count_dev // 64)
    my_row = lax.axis_index("space")
    block_no = (my_row + per_side * per_side + per_side + 1) % count_dev
    block_x = block_no // (per_side * per_side)
    block_y = block_no // per_side % per_side
    block_z = block_no % per_side
    classes = perm_class[0]
    width_x, width_y, width_z = classes.shape
    count_c = class_values.shape[0]
    if count_c == 8:
        low = jnp.where(classes < 2, jnp.where(classes < 1, class_values[0], class_values[1]),
                        jnp.where(classes < 3, class_values[2], class_values[3]))
        high = jnp.where(classes < 6, jnp.where(classes < 5, class_values[4], class_values[5]),
                         jnp.where(classes < 7, class_values[6], class_values[7]))
        permeab = jnp.where(classes < 4, low, high).astype(jnp.float32)
    else:
        permeab = jnp.zeros(classes.shape, jnp.float32)
        for number in range(count_c):
            permeab = permeab + jnp.where(classes == number, class_values[number], 0.0)
    row_len = per_side * width_z
    plane = per_side * width_y * row_len
    glob_x = well_cells // plane
    glob_y = well_cells // row_len % (per_side * width_y)
    glob_z = well_cells % row_len
    onehot_x = jnp.where(
        (glob_x - block_x * width_x)[:, None] == jnp.arange(width_x)[None, :],
        well_rates[:, None],
        0.0,
    )
    onehot_y = jnp.where(
        (glob_y - block_y * width_y)[:, None] == jnp.arange(width_y)[None, :], 1.0, 0.0
    ).astype(jnp.float32)
    onehot_z = jnp.where(
        (glob_z - block_z * width_z)[:, None] == jnp.arange(width_z)[None, :], 1.0, 0.0
    ).astype(jnp.float32)
    source = jnp.einsum(
        "wi,wj,wk->ijk", onehot_x, onehot_y, onehot_z, precision=lax.Precision.HIGHEST
    )

    values = guess[0]
    if count_dev * (width_x // 2) * (width_y // 2) <= 512:
        first = exchange([permeab, values], per_side)
        face_coefs, diagonal = coefficients(permeab, with_faces(permeab, pick(first, 0)), 1.0)
        values = smooth(values, source, face_coefs, diagonal, 1.0, with_faces(values, pick(first, 1)))
        for sweep_no in range(SWEEPS - 1):
            faces = pick(exchange([values], per_side), 0)
            values = smooth(values, source, face_coefs, diagonal, 1.0, with_faces(values, faces))
        stored_faces = pick(exchange([values], per_side), 0)
        leftover = source - operate(values, with_faces(values, stored_faces), face_coefs, 1.0)
        stored = values

        gathered = gather_rows(jnp.stack([coarsen(permeab), coarsen(leftover)]), per_side)
        correction_all = global_cycle(gathered[:, 1], gathered[:, 0], 1, per_side)

        correction = lax.dynamic_index_in_dim(correction_all, my_row, 0, keepdims=False)
        values = stored + refine(correction)
        faces = [
            mine + theirs
            for mine, theirs in zip(stored_faces, refined_faces(correction_all, my_row, per_side))
        ]
        values = smooth(values, source, face_coefs, diagonal, 1.0, with_faces(values, faces))
        for sweep_no in range(SWEEPS - 1):
            faces = pick(exchange([values], per_side), 0)
            values = smooth(values, source, face_coefs, diagonal, 1.0, with_faces(values, faces))
        faces = pick(exchange([values], per_side), 0)
        residual = source - operate(values, with_faces(values, faces), face_coefs, 1.0)
        return (values[None], residual[None])

    coarse_perm = coarsen(permeab)
    first, coarse_first = exchange_with_coarse(jnp.stack([permeab, values]), coarse_perm, per_side)
    face_coefs, diagonal = coefficients(permeab, with_faces(permeab, pick(first, 0)), 1.0)
    values = smooth(values, source, face_coefs, diagonal, 1.0, with_faces(values, pick(first, 1)))
    for sweep_no in range(SWEEPS - 1):
        faces = pick(exchange([values], per_side), 0)
        values = smooth(values, source, face_coefs, diagonal, 1.0, with_faces(values, faces))
    stored_faces = pick(exchange([values], per_side), 0)
    leftover = source - operate(values, with_faces(values, stored_faces), face_coefs, 1.0)
    stored = values

    scaling = 0.25
    right_1 = coarsen(leftover)
    coefs_1, diagonal_1 = coefficients(coarse_perm, with_faces(coarse_perm, coarse_first), scaling)
    values_1 = OMEGA * right_1 / diagonal_1
    for sweep_no in range(SWEEPS - 1):
        faces = pick(exchange([values_1], per_side), 0)
        values_1 = smooth(values_1, right_1, coefs_1, diagonal_1, scaling, with_faces(values_1, faces))
    stored_faces_1 = pick(exchange([values_1], per_side), 0)
    leftover_1 = right_1 - operate(values_1, with_faces(values_1, stored_faces_1), coefs_1, scaling)
    stored_1 = values_1

    gathered = gather_rows(jnp.stack([coarsen(coarse_perm), coarsen(leftover_1)]), per_side)
    correction_all = global_cycle(gathered[:, 1], gathered[:, 0], 2, per_side)

    correction = lax.dynamic_index_in_dim(correction_all, my_row, 0, keepdims=False)
    values_1 = stored_1 + refine(correction)
    faces = [
        mine + theirs
        for mine, theirs in zip(stored_faces_1, refined_faces(correction_all, my_row, per_side))
    ]
    values_1 = smooth(values_1, right_1, coefs_1, diagonal_1, scaling, with_faces(values_1, faces))
    for sweep_no in range(SWEEPS - 1):
        faces = pick(exchange([values_1], per_side), 0)
        values_1 = smooth(values_1, right_1, coefs_1, diagonal_1, scaling, with_faces(values_1, faces))
    coarse_faces = pick(exchange([values_1], per_side), 0)

    values = stored + refine(values_1)
    faces = [mine + refine_face_of(theirs) for mine, theirs in zip(stored_faces, coarse_faces)]
    values = smooth(values, source, face_coefs, diagonal, 1.0, with_faces(values, faces))
    for sweep_no in range(SWEEPS - 1):
        faces = pick(exchange([values], per_side), 0)
        values = smooth(values, source, face_coefs, diagonal, 1.0, with_faces(values, faces))
    faces = pick(exchange([values], per_side), 0)
    residual = source - operate(values, with_faces(values, faces), face_coefs, 1.0)
    return (values[None], residual[None])


def solution(mesh):
    return jax.shard_map(
        shards,
        mesh=mesh,
        in_specs=(
            P("space", None, None, None),
            P(),
            P("real"),
            P("real"),
            P(("real", "space"), None, None, None),
        ),
        out_specs=(P(("real", "space"), None, None, None), P(("real", "space"), None, None, None)),
        check_vma=False,
    )
```
